256 devices in a mesh: gx: 4 (over x), gy: 4 (over y), ta: 16 (over z, core).
Axes of the slice: x: 4, y: 4, z: 8, core: 2. Of those that a mesh axis runs over, the one named last changes fastest.
Arguments:
- tokens: bfloat16 [4, 4, 32, 128, 512], P('gx', 'gy', 'ta'), may hold values from -6 to 6
- validity: int32 [4, 4, 32, 128], P('gx', 'gy', 'ta'), may hold values 0 or 1
- tile_counts: int32 [4, 4], replicated, may hold values from 16 to 128, as said below
- neighbours: int32 [4, 4, 9], P('gx', 'gy'), may hold values from 0 to 1, as said below
- mask_token: bfloat16 [512], replicated, may hold values from -4 to 4
- norm_gains: float32 [3, 512], replicated, may hold values from 0.25 to 1.75
- agent_qkv: bfloat16 [512, 1536], replicated, may hold values from -3 to 3
- agent_out: bfloat16 [512, 512], replicated, may hold values from -0.25 to 0.25
- time_qkv: bfloat16 [512, 1536], replicated, may hold values from -3 to 3
- time_out: bfloat16 [512, 512], replicated, may hold values from -0.25 to 0.25
- widen_weight: bfloat16 [512, 2048], replicated, may hold values from -0.25 to 0.25
- narrow_weight: bfloat16 [2048, 512], replicated, may hold values from -0.125 to 0.125
Outputs:
- layer_out: bfloat16 [4, 4, 32, 128, 512], P('gx', 'gy', 'ta')
The draws below stay inside these ranges and needn't reach their ends.
Inputs may be any that keep to these rules, and one draw needn't show every extreme that they name: Tile i, j has its live agents in slots 0 to tile_counts[i, j] - 1; some tile is full. `neighbours`: entry 3 (di + 1) + (dj + 1) is 1 when the tile attends to the tile at offset di, dj; the centre entry is always 1. `validity`: 1 marks an observed agent step.
All inputs are finite; a program needn't handle non-finite values. No bound on the sum of `validity` on one device may be relied on, other than what follows from the above.
Results may differ from the reference program's by a relative error of at most 0.015.
Values may be sent and summed in bfloat16 or wider, within the bound.
No kernel may reach another device: no remote copies, remote signals or barrier semaphores. Data moves between devices by JAX's collectives and lax.ppermute only.
A program may use at most 128 MiB of HBM per device.

```python
from functools import partial
import jax
import jax.numpy as jnp
from jax import lax

D = 512
HEADS = 8
HEAD_DIM = 64
FF = 2048
A_DEV = 128
NTX = 4
NTY = 4
T_SIZE = 32


def draw_tile_counts(key, part):
    drawn_counts = jax.random.randint(jax.random.fold_in(key, 11), (NTX * NTY,), A_DEV // 8, A_DEV + 1)
    chosen_tile = jax.random.randint(jax.random.fold_in(key, 12), (), 0, NTX * NTY)
    flat_counts = jnp.where(jnp.arange(NTX * NTY) == chosen_tile, A_DEV, drawn_counts)
    return flat_counts.reshape(NTX, NTY).astype(jnp.int32)


def draw_neighbours(key, part):
    drawn_bits = jax.random.randint(jax.random.fold_in(key, 13), (NTX, NTY, 9), 0, 4)
    flags = (drawn_bits > 0).astype(jnp.int32)
    return flags.at[:, :, 4].set(1).astype(jnp.int32)


def projection_draw(key):
    spread_scale = D ** (-0.5)
    drawn = jax.random.truncated_normal(jax.random.fold_in(key, 1), -3.0, 3.0, (D, 3 * D), jnp.float32) * spread_scale
    return jnp.clip(drawn, -3.0, 3.0)


def draw_agent_qkv(key, part):
    return projection_draw(jax.random.fold_in(key, 21)).astype(jnp.bfloat16)


def draw_time_qkv(key, part):
    return projection_draw(jax.random.fold_in(key, 22)).astype(jnp.bfloat16)


def plant(values, stream_key, low, high):
    shape = values.shape
    index_at = [jax.random.randint(jax.random.fold_in(stream_key, axis), (), 0, shape[axis]) for axis in range(len(shape))]
    values = values.at[tuple(index_at)].set(low)
    longest = shape.index(max(shape))
    index_at[longest] = (index_at[longest] + 1) % shape[longest]
    return values.at[tuple(index_at)].set(high)


def block_scale(rng, dims, cuts, smallest, high):
    factor_of = 1.0
    for position, blocks in cuts:
        steps = jax.random.uniform(jax.random.fold_in(jax.random.fold_in(rng, 6), position), (blocks,), jnp.float32, smallest / len(cuts), high / len(cuts))
        factor_of = factor_of * jnp.repeat(jnp.exp(steps), dims[position] // blocks).reshape((-1,) + (1,) * (len(dims) - 1 - position))
    return factor_of


def noise(key, dims, scale, reach, cuts=(), kind=jnp.bfloat16):
    entries = scale * jax.random.normal(key, dims, jnp.float32)
    if cuts:
        entries = entries * block_scale(key, dims, cuts, -0.22, 0.18)
    return jnp.clip(entries, -reach, reach).astype(kind)


def setup_inputs(seed: int = 0) -> dict:
    arg_keys = jax.random.split(jax.random.key(seed), 13)
    tokens = noise(arg_keys[0], (NTX, NTY, T_SIZE, A_DEV, D), 1.0, 6.0, ((0, 4), (1, 4), (2, 16)))
    validity = plant((jax.random.randint(arg_keys[1], (NTX, NTY, T_SIZE, A_DEV), 0, 4) < 3).astype(jnp.int32), jax.random.fold_in(arg_keys[1], 1), 0, 1)
    tile_counts = draw_tile_counts(jax.random.fold_in(arg_keys[12], 71), 0)
    neighbours = draw_neighbours(jax.random.fold_in(arg_keys[12], 71), 0)
    mask_token = noise(arg_keys[4], (D,), 1.0, 4.0)
    norm_gains = jnp.clip(1.0 + 0.15 * jax.random.normal(arg_keys[5], (3, D), jnp.float32), 0.25, 1.75)
    agent_qkv = draw_agent_qkv(jax.random.fold_in(arg_keys[12], 71), 0)
    agent_out = noise(arg_keys[7], (D, D), D ** -0.5, 0.25)
    time_qkv = draw_time_qkv(jax.random.fold_in(arg_keys[12], 71), 0)
    time_out = noise(arg_keys[9], (D, D), D ** -0.5, 0.25)
    widen_weight = noise(arg_keys[10], (D, FF), D ** -0.5, 0.25)
    narrow_weight = noise(arg_keys[11], (FF, D), FF ** -0.5, 0.125)
    return {"tokens": tokens, "validity": validity, "tile_counts": tile_counts, "neighbours": neighbours, "mask_token": mask_token, "norm_gains": norm_gains, "agent_qkv": agent_qkv, "agent_out": agent_out, "time_qkv": time_qkv, "time_out": time_out, "widen_weight": widen_weight, "narrow_weight": narrow_weight}


EPSILON = 1e-05
NEGATIVE = -1e+30

def layer_norm(values, gain_row):
    values = values.astype(jnp.float32)
    center = values - lax.optimization_barrier(jnp.mean(values, axis=-1, keepdims=True))
    spread = lax.optimization_barrier(jnp.mean(center * center, axis=-1, keepdims=True))
    return (center * lax.rsqrt(spread + EPSILON) * gain_row).astype(jnp.bfloat16)

def project(values, weight):
    return jnp.dot(values, weight, preferred_element_type=jnp.float32)

def agent_attention(queries, padded_kv, padded_live, neighbour_flags, tile_index):
    tile_index = tile_index.astype(jnp.int32)
    tile_row = (tile_index // NTY).astype(jnp.int32)
    column = (tile_index % NTY).astype(jnp.int32)
    zero = jnp.zeros((), jnp.int32)
    near_block = lax.dynamic_slice(padded_kv, (tile_row, column, zero, zero, zero), (3, 3, T_SIZE, A_DEV, 2 * D))
    near_live = lax.dynamic_slice(padded_live, (tile_row, column, zero), (3, 3, A_DEV))
    chosen = neighbour_flags[tile_index].reshape(3, 3) == 1
    key_live = (near_live & chosen[:, :, None]).reshape(9 * A_DEV)
    own_queries = queries[tile_index].astype(jnp.float32).reshape(T_SIZE, A_DEV, HEADS, HEAD_DIM)
    key_rows = near_block[..., :D].astype(jnp.float32).reshape(3, 3, T_SIZE, A_DEV, HEADS, HEAD_DIM)
    value_rows = near_block[..., D:].astype(jnp.float32).reshape(3, 3, T_SIZE, A_DEV, HEADS, HEAD_DIM)
    value_rows = value_rows.transpose(2, 0, 1, 3, 4, 5).reshape(T_SIZE, 9 * A_DEV, HEADS, HEAD_DIM)
    scores = jnp.einsum('tqhd,xytkhd->thqxyk', own_queries, key_rows).reshape(T_SIZE, HEADS, A_DEV, 9 * A_DEV)
    scores = scores * HEAD_DIM ** (-0.5)
    scores = jnp.where(key_live, scores, NEGATIVE)
    row_max = lax.optimization_barrier(jnp.max(scores, axis=-1, keepdims=True))
    weights = jnp.exp(scores - row_max)
    weights = (weights / lax.optimization_barrier(jnp.sum(weights, axis=-1, keepdims=True))).astype(jnp.bfloat16)
    weights = lax.optimization_barrier(weights).astype(jnp.float32)
    attended = jnp.einsum('thqn,tnhd->tqhd', weights, value_rows)
    return attended.reshape(T_SIZE, A_DEV, D).astype(jnp.bfloat16)

def time_attention(exchanged):
    own_queries = exchanged[..., :D].astype(jnp.float32).reshape(T_SIZE, A_DEV, HEADS, HEAD_DIM)
    key_rows = exchanged[..., D:2 * D].astype(jnp.float32).reshape(T_SIZE, A_DEV, HEADS, HEAD_DIM)
    value_rows = exchanged[..., 2 * D:].astype(jnp.float32).reshape(T_SIZE, A_DEV, HEADS, HEAD_DIM)
    scores = jnp.einsum('qahd,kahd->ahqk', own_queries, key_rows) * HEAD_DIM ** (-0.5)
    row_max = lax.optimization_barrier(jnp.max(scores, axis=-1, keepdims=True))
    weights = jnp.exp(scores - row_max)
    weights = weights / lax.optimization_barrier(jnp.sum(weights, axis=-1, keepdims=True))
    attended = jnp.einsum('ahqk,kahd->qahd', weights, value_rows, precision=lax.Precision.HIGHEST)
    return attended.reshape(T_SIZE, A_DEV, D).astype(jnp.bfloat16)

def reference(tokens, validity, tile_counts, neighbours, mask_token, norm_gains, agent_qkv, agent_out, time_qkv, time_out, widen_weight, narrow_weight):
    masked_input = jnp.where(validity[..., None] == 1, tokens, mask_token)
    normed = layer_norm(masked_input, norm_gains[0])
    packed = project(normed, agent_qkv).astype(jnp.bfloat16)
    queries = packed[..., :D].reshape(NTX * NTY, T_SIZE, A_DEV, D)
    padded_kv = jnp.pad(packed[..., D:], ((1, 1), (1, 1), (0, 0), (0, 0), (0, 0)))
    slot_ids = jnp.arange(A_DEV, dtype=jnp.int32)
    slot_live = slot_ids[None, None, :] < tile_counts[:, :, None]
    padded_live = jnp.pad(slot_live, ((1, 1), (1, 1), (0, 0)))
    neighbour_flags = neighbours.reshape(NTX * NTY, 9)
    tile_list = jnp.arange(NTX * NTY, dtype=jnp.int32)
    attended = lax.map(partial(agent_attention, queries, padded_kv, padded_live, neighbour_flags), tile_list)
    attended = attended.reshape(NTX, NTY, T_SIZE, A_DEV, D)
    after_agents = (masked_input.astype(jnp.float32) + project(attended, agent_out)).astype(jnp.bfloat16)
    normed = layer_norm(after_agents, norm_gains[1])
    packed = project(normed, time_qkv).astype(jnp.bfloat16).reshape(NTX * NTY, T_SIZE, A_DEV, 3 * D)
    attended = lax.map(time_attention, packed).reshape(NTX, NTY, T_SIZE, A_DEV, D)
    after_time = (after_agents.astype(jnp.float32) + project(attended, time_out)).astype(jnp.bfloat16)
    normed = layer_norm(after_time, norm_gains[2])
    hidden = jnp.maximum(project(normed, widen_weight), 0.0).astype(jnp.bfloat16)
    return (after_time.astype(jnp.float32) + project(hidden, narrow_weight)).astype(jnp.bfloat16)
```

```python
import math

import jax
import jax.numpy as jnp
from jax import lax
from jax.sharding import PartitionSpec as P

HEADS = 8


EPSILON = 1e-05
NEGATIVE = -1e30


def shift(piece, axis, step):
    count = lax.axis_size(axis)
    if step > 0:
        pairs = [(i, i + 1) for i in range(count - 1)]
    else:
        pairs = [(i + 1, i) for i in range(count - 1)]
    return lax.ppermute(piece, axis, pairs)


def halo(piece):
    west = shift(piece, "gx", 1)
    east = shift(piece, "gx", -1)
    south = shift(piece, "gy", 1)
    north = shift(piece, "gy", -1)
    north_east = shift(north, "gx", -1)
    south_west = shift(south, "gx", 1)
    south_east = shift(east, "gy", 1)
    north_west = shift(west, "gy", -1)
    return [south_west, west, north_west, south, piece, north, south_east, east, north_east]


def layer_norm(values, gain_row):
    values = values.astype(jnp.float32)
    center = values - jnp.mean(values, axis=-1, keepdims=True)
    spread = jnp.mean(center * center, axis=-1, keepdims=True)
    return (center * lax.rsqrt(spread + EPSILON) * gain_row).astype(jnp.bfloat16)


def project(values, weight):
    return jnp.dot(values, weight, preferred_element_type=jnp.float32)


def per_device(
    tokens,
    validity,
    tile_counts,
    neighbours,
    mask_token,
    norm_gains,
    agent_qkv,
    agent_out,
    time_qkv,
    time_out,
    widen_weight,
    narrow_weight,
):
    model_width = tokens.shape[-1]
    head_count = HEADS
    head_dim = model_width // head_count
    moments = tokens.shape[2]
    slot_count = tokens.shape[3]
    score_scale = 1.0 / math.sqrt(head_dim)
    rows = tokens.reshape(moments, slot_count, model_width)
    live_rows = validity.reshape(moments, slot_count)
    masked_input = jnp.where(live_rows[..., None] == 1, rows, mask_token)

    normed = layer_norm(masked_input, norm_gains[0])
    agent_w = agent_qkv.reshape(model_width, 3, head_count, head_dim)
    kv = jnp.einsum(
        "tsc,cjhe->jthse", normed, agent_w[:, 1:], preferred_element_type=jnp.float32
    ).astype(jnp.bfloat16)
    near = halo(kv)
    queries = jnp.einsum(
        "tsc,che->thse", normed, agent_w[:, 0], preferred_element_type=jnp.float32
    ).astype(jnp.bfloat16)
    near_all = jnp.concatenate(near, axis=3)
    keys = near_all[0]
    values = near_all[1]
    column_index = lax.axis_index("gx")
    row_index = lax.axis_index("gy")
    padded_counts = jnp.pad(tile_counts, 1)
    near_counts = lax.dynamic_slice(padded_counts, (column_index, row_index), (3, 3))
    chosen = neighbours[0, 0].reshape(3, 3) == 1
    slot_ids = jnp.arange(slot_count, dtype=jnp.int32)
    key_live = ((slot_ids[None, None, :] < near_counts[:, :, None]) & chosen[:, :, None]).reshape(
        9 * slot_count
    )
    scores = jnp.einsum("thqe,thke->thqk", queries, keys, preferred_element_type=jnp.float32)
    scores = scores * score_scale
    scores = jnp.where(key_live, scores, NEGATIVE)
    row_max = jnp.max(scores, axis=-1, keepdims=True)
    weights = jnp.exp(scores - row_max)
    weights = (weights / jnp.sum(weights, axis=-1, keepdims=True)).astype(jnp.bfloat16)
    mixed = jnp.einsum(
        "thqk,thke->thqe", weights, values, preferred_element_type=jnp.float32
    ).astype(jnp.bfloat16)
    agent_proj = jnp.einsum(
        "thqe,hef->tqf",
        mixed,
        agent_out.reshape(head_count, head_dim, model_width),
        preferred_element_type=jnp.float32,
    )
    after_agents = (masked_input.astype(jnp.float32) + agent_proj).astype(jnp.bfloat16)

    normed = layer_norm(after_agents, norm_gains[1])
    packed = project(normed, time_qkv).astype(jnp.bfloat16)
    spread = lax.all_to_all(packed, "ta", 1, 0, tiled=True)
    steps = spread.shape[0]
    group = spread.shape[1]
    spread = spread.reshape(steps, group, 3, head_count, head_dim)
    time_scores = (
        jnp.einsum(
            "qshe,kshe->shqk",
            spread[:, :, 0],
            spread[:, :, 1],
            preferred_element_type=jnp.float32,
        )
        * score_scale
    )
    time_max = jnp.max(time_scores, axis=-1, keepdims=True)
    time_weights = jnp.exp(time_scores - time_max)
    time_weights = time_weights / jnp.sum(time_weights, axis=-1, keepdims=True)
    time_mix = jnp.einsum(
        "shqk,kshe->qshe",
        time_weights,
        spread[:, :, 2].astype(jnp.float32),
        precision=lax.Precision.HIGHEST,
    ).astype(jnp.bfloat16)
    time_mix = lax.all_to_all(
        time_mix.reshape(steps, group, model_width), "ta", 0, 1, tiled=True
    )
    after_time = (after_agents.astype(jnp.float32) + project(time_mix, time_out)).astype(
        jnp.bfloat16
    )
    normed = layer_norm(after_time, norm_gains[2])
    hidden = jnp.maximum(project(normed, widen_weight), 0.0).astype(jnp.bfloat16)
    out = (after_time.astype(jnp.float32) + project(hidden, narrow_weight)).astype(jnp.bfloat16)
    return out.reshape(tokens.shape)


def solution(mesh):
    in_specs = (
        P("gx", "gy", "ta", None, None),
        P("gx", "gy", "ta", None),
        P(),
        P("gx", "gy", None),
        P(),
        P(),
        P(),
        P(),
        P(),
        P(),
        P(),
        P(),
    )
    out_specs = P("gx", "gy", "ta", None, None)
    return jax.shard_map(
        per_device, mesh=mesh, in_specs=in_specs, out_specs=out_specs, check_vma=False
    )
```

```python
import math

import jax
import jax.numpy as jnp
from jax import lax
from jax.sharding import PartitionSpec as P

HEADS = 8


EPSILON = 1e-05
NEGATIVE = -1e30


def shift(piece, axis, step):
    count = lax.axis_size(axis)
    if step > 0:
        pairs = [(i, i + 1) for i in range(count - 1)]
    else:
        pairs = [(i + 1, i) for i in range(count - 1)]
    return lax.ppermute(piece, axis, pairs)


def halo(piece):
    west = shift(piece, "gx", 1)
    east = shift(piece, "gx", -1)
    south = shift(piece, "gy", 1)
    north = shift(piece, "gy", -1)
    north_east = shift(north, "gx", -1)
    south_west = shift(south, "gx", 1)
    south_east = shift(east, "gy", 1)
    north_west = shift(west, "gy", -1)
    return [south_west, west, north_west, south, piece, north, south_east, east, north_east]


def layer_norm(values, gain_row):
    values = values.astype(jnp.float32)
    center = values - jnp.mean(values, axis=-1, keepdims=True)
    spread = jnp.mean(center * center, axis=-1, keepdims=True)
    return (center * lax.rsqrt(spread + EPSILON) * gain_row).astype(jnp.bfloat16)


def project(values, weight):
    return jnp.dot(values, weight, preferred_element_type=jnp.float32)


def per_device(
    tokens,
    validity,
    tile_counts,
    neighbours,
    mask_token,
    norm_gains,
    agent_qkv,
    agent_out,
    time_qkv,
    time_out,
    widen_weight,
    narrow_weight,
):
    model_width = tokens.shape[-1]
    head_count = HEADS
    head_dim = model_width // head_count
    moments = tokens.shape[2]
    slot_count = tokens.shape[3]
    score_scale = 1.0 / math.sqrt(head_dim)
    rows = tokens.reshape(moments, slot_count, model_width)
    live_rows = validity.reshape(moments, slot_count)
    masked_input = jnp.where(live_rows[..., None] == 1, rows, mask_token)

    normed = layer_norm(masked_input, norm_gains[0])
    near = jnp.stack(halo(normed))
    agent_w = agent_qkv.reshape(model_width, 3, head_count, head_dim)
    queries = jnp.einsum(
        "tsc,che->thse", normed, agent_w[:, 0], preferred_element_type=jnp.float32
    ).astype(jnp.bfloat16)
    kv = jnp.einsum(
        "ntsc,cjhe->jthnse", near, agent_w[:, 1:], preferred_element_type=jnp.float32
    ).astype(jnp.bfloat16)
    kv = kv.reshape(2, moments, head_count, 9 * slot_count, head_dim)
    keys = kv[0]
    values = kv[1]
    column_index = lax.axis_index("gx")
    row_index = lax.axis_index("gy")
    padded_counts = jnp.pad(tile_counts, 1)
    near_counts = lax.dynamic_slice(padded_counts, (column_index, row_index), (3, 3))
    chosen = neighbours[0, 0].reshape(3, 3) == 1
    slot_ids = jnp.arange(slot_count, dtype=jnp.int32)
    key_live = ((slot_ids[None, None, :] < near_counts[:, :, None]) & chosen[:, :, None]).reshape(
        9 * slot_count
    )
    scores = jnp.einsum("thqe,thke->thqk", queries, keys, preferred_element_type=jnp.float32)
    scores = scores * score_scale
    scores = jnp.where(key_live, scores, NEGATIVE)
    row_max = jnp.max(scores, axis=-1, keepdims=True)
    weights = jnp.exp(scores - row_max)
    weights = (weights / jnp.sum(weights, axis=-1, keepdims=True)).astype(jnp.bfloat16)
    mixed = jnp.einsum(
        "thqk,thke->thqe", weights, values, preferred_element_type=jnp.float32
    ).astype(jnp.bfloat16)
    agent_proj = jnp.einsum(
        "thqe,hef->tqf",
        mixed,
        agent_out.reshape(head_count, head_dim, model_width),
        preferred_element_type=jnp.float32,
    )
    after_agents = (masked_input.astype(jnp.float32) + agent_proj).astype(jnp.bfloat16)

    after_agents = lax.all_to_all(after_agents, "ta", 1, 0, tiled=True)
    steps = after_agents.shape[0]
    group = after_agents.shape[1]
    normed = layer_norm(after_agents, norm_gains[1])
    packed = project(normed, time_qkv).astype(jnp.bfloat16)
    packed = packed.reshape(steps, group, 3, head_count, head_dim)
    time_scores = (
        jnp.einsum(
            "qshe,kshe->shqk",
            packed[:, :, 0],
            packed[:, :, 1],
            preferred_element_type=jnp.float32,
        )
        * score_scale
    )
    time_max = jnp.max(time_scores, axis=-1, keepdims=True)
    time_weights = jnp.exp(time_scores - time_max)
    time_weights = time_weights / jnp.sum(time_weights, axis=-1, keepdims=True)
    time_mix = jnp.einsum(
        "shqk,kshe->qshe",
        time_weights,
        packed[:, :, 2].astype(jnp.float32),
        precision=lax.Precision.HIGHEST,
    ).astype(jnp.bfloat16)
    time_mix = time_mix.reshape(steps, group, model_width)
    after_time = (after_agents.astype(jnp.float32) + project(time_mix, time_out)).astype(
        jnp.bfloat16
    )
    normed = layer_norm(after_time, norm_gains[2])
    hidden = jnp.maximum(project(normed, widen_weight), 0.0).astype(jnp.bfloat16)
    out = (after_time.astype(jnp.float32) + project(hidden, narrow_weight)).astype(jnp.bfloat16)
    out = lax.all_to_all(out, "ta", 0, 1, tiled=True)
    return out.reshape(tokens.shape)


def solution(mesh):
    in_specs = (
        P("gx", "gy", "ta", None, None),
        P("gx", "gy", "ta", None),
        P(),
        P("gx", "gy", None),
        P(),
        P(),
        P(),
        P(),
        P(),
        P(),
        P(),
        P(),
    )
    out_specs = P("gx", "gy", "ta", None, None)
    return jax.shard_map(
        per_device, mesh=mesh, in_specs=in_specs, out_specs=out_specs, check_vma=False
    )
```

```python
import functools
import math

import jax
import jax.numpy as jnp
from jax import lax
from jax.experimental import pallas as pl
from jax.sharding import PartitionSpec as P

HEADS = 8


EPSILON = 1e-05
NEGATIVE = -1e30


def shift(piece, axis, step):
    count = lax.axis_size(axis)
    if step > 0:
        pairs = [(i, i + 1) for i in range(count - 1)]
    else:
        pairs = [(i + 1, i) for i in range(count - 1)]
    return lax.ppermute(piece, axis, pairs)


def halo(piece):
    west = shift(piece, "gx", 1)
    east = shift(piece, "gx", -1)
    south = shift(piece, "gy", 1)
    north = shift(piece, "gy", -1)
    north_east = shift(north, "gx", -1)
    south_west = shift(south, "gx", 1)
    south_east = shift(east, "gy", 1)
    north_west = shift(west, "gy", -1)
    return [south_west, west, north_west, south, piece, north, south_east, east, north_east]


def layer_norm(values, gain_row):
    values = values.astype(jnp.float32)
    center = values - jnp.mean(values, axis=-1, keepdims=True)
    spread = jnp.mean(center * center, axis=-1, keepdims=True)
    return (center * lax.rsqrt(spread + EPSILON) * gain_row).astype(jnp.bfloat16)


def project(values, weight):
    return jnp.dot(values, weight, preferred_element_type=jnp.float32)


def agent_kernel(live_ref, q_ref, k_ref, v_ref, o_ref, *, scale, head_dim):
    live = live_ref[...] != 0
    queries = q_ref[0]
    slots = k_ref.shape[1] * k_ref.shape[2]
    keys = k_ref[0].reshape(slots, k_ref.shape[3])
    values = v_ref[0].reshape(slots, v_ref.shape[3])
    lane = lax.broadcasted_iota(jnp.int32, (1, queries.shape[1]), 1)
    mixed = jnp.zeros(o_ref.shape[1:], jnp.float32)
    for half in range(queries.shape[1] // head_dim):
        chosen = (lane // head_dim) == half
        own = jnp.where(chosen, queries, jnp.zeros_like(queries))
        scores = lax.dot_general(
            own, keys, (((1,), (1,)), ((), ())), preferred_element_type=jnp.float32
        )
        scores = jnp.where(live, scores * scale, NEGATIVE)
        row_max = jnp.max(scores, axis=-1, keepdims=True)
        weights = jnp.exp(scores - row_max)
        weights = (weights / jnp.sum(weights, axis=-1, keepdims=True)).astype(jnp.bfloat16)
        part = jnp.dot(weights, values, preferred_element_type=jnp.float32)
        mixed = jnp.where(chosen, part, mixed)
    o_ref[0] = mixed.astype(o_ref.dtype)


def agent_attention(live, queries, kv, head_dim, interpret=False):
    moments, slot_count, model_width = queries.shape
    lanes = 2 * head_dim
    pairs = model_width // lanes
    near = kv.shape[1]
    body = functools.partial(agent_kernel, scale=1.0 / math.sqrt(head_dim), head_dim=head_dim)
    return pl.pallas_call(
        body,
        grid=(moments, pairs),
        in_specs=[
            pl.BlockSpec(live.shape, lambda t, p: (0, 0)),
            pl.BlockSpec((1, slot_count, lanes), lambda t, p: (t, 0, p)),
            pl.BlockSpec((1, near, slot_count, lanes), lambda t, p: (t, 0, 0, p)),
            pl.BlockSpec((1, near, slot_count, lanes), lambda t, p: (t, 0, 0, p + pairs)),
        ],
        out_specs=pl.BlockSpec((1, slot_count, lanes), lambda t, p: (t, 0, p)),
        out_shape=jax.ShapeDtypeStruct(queries.shape, jnp.bfloat16),
        interpret=interpret,
    )(live, queries, kv, kv)


def per_device(
    tokens,
    validity,
    tile_counts,
    neighbours,
    mask_token,
    norm_gains,
    agent_qkv,
    agent_out,
    time_qkv,
    time_out,
    widen_weight,
    narrow_weight,
):
    model_width = tokens.shape[-1]
    head_count = HEADS
    head_dim = model_width // head_count
    moments = tokens.shape[2]
    slot_count = tokens.shape[3]
    score_scale = 1.0 / math.sqrt(head_dim)
    rows = tokens.reshape(moments, slot_count, model_width)
    live_rows = validity.reshape(moments, slot_count)
    masked_input = jnp.where(live_rows[..., None] == 1, rows, mask_token)

    normed = layer_norm(masked_input, norm_gains[0])
    near = jnp.stack(halo(normed), axis=1)
    queries = project(normed, agent_qkv[:, :model_width]).astype(jnp.bfloat16)
    kv = project(near, agent_qkv[:, model_width:]).astype(jnp.bfloat16)
    column_index = lax.axis_index("gx")
    row_index = lax.axis_index("gy")
    padded_counts = jnp.pad(tile_counts, 1)
    near_counts = lax.dynamic_slice(padded_counts, (column_index, row_index), (3, 3))
    chosen = neighbours[0, 0].reshape(3, 3) == 1
    slot_ids = jnp.arange(slot_count, dtype=jnp.int32)
    key_live = ((slot_ids[None, None, :] < near_counts[:, :, None]) & chosen[:, :, None]).reshape(
        1, 9 * slot_count
    )
    mixed = agent_attention(key_live.astype(jnp.int32), queries, kv, head_dim)
    agent_proj = project(mixed, agent_out)
    after_agents = (masked_input.astype(jnp.float32) + agent_proj).astype(jnp.bfloat16)

    after_agents = lax.all_to_all(after_agents, "ta", 1, 0, tiled=True)
    steps = after_agents.shape[0]
    group = after_agents.shape[1]
    normed = layer_norm(after_agents, norm_gains[1])
    packed = project(normed, time_qkv).astype(jnp.bfloat16)
    packed = packed.reshape(steps, group, 3, head_count, head_dim)
    time_scores = (
        jnp.einsum(
            "qshe,kshe->shqk",
            packed[:, :, 0],
            packed[:, :, 1],
            preferred_element_type=jnp.float32,
        )
        * score_scale
    )
    time_max = jnp.max(time_scores, axis=-1, keepdims=True)
    time_weights = jnp.exp(time_scores - time_max)
    time_weights = time_weights / jnp.sum(time_weights, axis=-1, keepdims=True)
    time_mix = jnp.einsum(
        "shqk,kshe->qshe",
        time_weights,
        packed[:, :, 2].astype(jnp.float32),
        precision=lax.Precision.HIGHEST,
    ).astype(jnp.bfloat16)
    time_mix = time_mix.reshape(steps, group, model_width)
    after_time = (after_agents.astype(jnp.float32) + project(time_mix, time_out)).astype(
        jnp.bfloat16
    )
    normed = layer_norm(after_time, norm_gains[2])
    hidden = jnp.maximum(project(normed, widen_weight), 0.0).astype(jnp.bfloat16)
    out = (after_time.astype(jnp.float32) + project(hidden, narrow_weight)).astype(jnp.bfloat16)
    out = lax.all_to_all(out, "ta", 0, 1, tiled=True)
    return out.reshape(tokens.shape)


def solution(mesh):
    in_specs = (
        P("gx", "gy", "ta", None, None),
        P("gx", "gy", "ta", None),
        P(),
        P("gx", "gy", None),
        P(),
        P(),
        P(),
        P(),
        P(),
        P(),
        P(),
        P(),
    )
    out_specs = P("gx", "gy", "ta", None, None)
    return jax.shard_map(
        per_device, mesh=mesh, in_specs=in_specs, out_specs=out_specs, check_vma=False
    )
```

```python
import functools
import math

import jax
import jax.numpy as jnp
from jax import lax
from jax.experimental import pallas as pl
from jax.sharding import PartitionSpec as P

HEADS = 8


EPSILON = 1e-05
NEGATIVE = -1e30


def shift(piece, axis, step):
    count = lax.axis_size(axis)
    if step > 0:
        pairs = [(i, i + 1) for i in range(count - 1)]
    else:
        pairs = [(i + 1, i) for i in range(count - 1)]
    return lax.ppermute(piece, axis, pairs)


def halo(piece):
    west = shift(piece, "gx", 1)
    east = shift(piece, "gx", -1)
    middle = jnp.stack([west, piece, east], axis=1)
    south = shift(middle, "gy", 1)
    north = shift(middle, "gy", -1)
    return [south, middle, north]


def layer_norm(values, gain_row):
    values = values.astype(jnp.float32)
    center = values - jnp.mean(values, axis=-1, keepdims=True)
    spread = jnp.mean(center * center, axis=-1, keepdims=True)
    return (center * lax.rsqrt(spread + EPSILON) * gain_row).astype(jnp.bfloat16)


def project(values, weight):
    return jnp.dot(values, weight, preferred_element_type=jnp.float32)


def agent_kernel(live_ref, q_ref, *refs, scale, head_dim):
    o_ref = refs[-1]
    groups = (len(refs) - 1) // 2
    live = live_ref[...] != 0
    queries = q_ref[0]
    keys = []
    values = []
    for k_ref, v_ref in zip(refs[:groups], refs[groups:-1]):
        slots = k_ref.shape[1] * k_ref.shape[2]
        keys.append(k_ref[0].reshape(slots, k_ref.shape[3]))
        values.append(v_ref[0].reshape(slots, v_ref.shape[3]))
    lane = lax.broadcasted_iota(jnp.int32, (1, queries.shape[1]), 1)
    mixed = jnp.zeros(o_ref.shape[1:], jnp.float32)
    for half in range(queries.shape[1] // head_dim):
        chosen = (lane // head_dim) == half
        own = jnp.where(chosen, queries, jnp.zeros_like(queries))
        scores = jnp.concatenate(
            [
                lax.dot_general(
                    own, key, (((1,), (1,)), ((), ())), preferred_element_type=jnp.float32
                )
                for key in keys
            ],
            axis=1,
        )
        scores = jnp.where(live, scores * scale, NEGATIVE)
        row_max = jnp.max(scores, axis=-1, keepdims=True)
        weights = jnp.exp(scores - row_max)
        weights = (weights / jnp.sum(weights, axis=-1, keepdims=True)).astype(jnp.bfloat16)
        part = None
        start = 0
        for value in values:
            piece = jnp.dot(
                weights[:, start : start + value.shape[0]], value, preferred_element_type=jnp.float32
            )
            part = piece if part is None else part + piece
            start += value.shape[0]
        mixed = jnp.where(chosen, part, mixed)
    o_ref[0] = mixed.astype(o_ref.dtype)


def agent_attention(live, queries, kv_groups, head_dim, interpret=False):
    moments, slot_count, model_width = queries.shape
    lanes = 2 * head_dim
    pairs = model_width // lanes
    body = functools.partial(agent_kernel, scale=1.0 / math.sqrt(head_dim), head_dim=head_dim)
    key_specs = [
        pl.BlockSpec((1, kv.shape[1], slot_count, lanes), lambda t, p: (t, 0, 0, p))
        for kv in kv_groups
    ]
    value_specs = [
        pl.BlockSpec((1, kv.shape[1], slot_count, lanes), lambda t, p: (t, 0, 0, p + pairs))
        for kv in kv_groups
    ]
    return pl.pallas_call(
        body,
        grid=(moments, pairs),
        in_specs=[
            pl.BlockSpec(live.shape, lambda t, p: (0, 0)),
            pl.BlockSpec((1, slot_count, lanes), lambda t, p: (t, 0, p)),
        ]
        + key_specs
        + value_specs,
        out_specs=pl.BlockSpec((1, slot_count, lanes), lambda t, p: (t, 0, p)),
        out_shape=jax.ShapeDtypeStruct(queries.shape, jnp.bfloat16),
        interpret=interpret,
    )(live, queries, *kv_groups, *kv_groups)


def per_device(
    tokens,
    validity,
    tile_counts,
    neighbours,
    mask_token,
    norm_gains,
    agent_qkv,
    agent_out,
    time_qkv,
    time_out,
    widen_weight,
    narrow_weight,
):
    model_width = tokens.shape[-1]
    head_count = HEADS
    head_dim = model_width // head_count
    moments = tokens.shape[2]
    slot_count = tokens.shape[3]
    score_scale = 1.0 / math.sqrt(head_dim)
    rows = tokens.reshape(moments, slot_count, model_width)
    live_rows = validity.reshape(moments, slot_count)
    masked_input = jnp.where(live_rows[..., None] == 1, rows, mask_token)

    normed = layer_norm(masked_input, norm_gains[0])
    queries = project(normed, agent_qkv[:, :model_width]).astype(jnp.bfloat16)
    kv_groups = [
        project(group, agent_qkv[:, model_width:]).astype(jnp.bfloat16) for group in halo(normed)
    ]
    column_index = lax.axis_index("gx")
    row_index = lax.axis_index("gy")
    padded_counts = jnp.pad(tile_counts, 1)
    near_counts = lax.dynamic_slice(padded_counts, (column_index, row_index), (3, 3))
    chosen = neighbours[0, 0].reshape(3, 3) == 1
    slot_ids = jnp.arange(slot_count, dtype=jnp.int32)
    key_live = (slot_ids[None, None, :] < near_counts[:, :, None]) & chosen[:, :, None]
    key_live = key_live.transpose(1, 0, 2).reshape(1, 9 * slot_count)
    mixed = agent_attention(key_live.astype(jnp.int32), queries, kv_groups, head_dim)
    agent_proj = project(mixed, agent_out)
    after_agents = (masked_input.astype(jnp.float32) + agent_proj).astype(jnp.bfloat16)

    after_agents = lax.all_to_all(after_agents, "ta", 1, 0, tiled=True)
    steps = after_agents.shape[0]
    group = after_agents.shape[1]
    normed = layer_norm(after_agents, norm_gains[1])
    packed = project(normed, time_qkv).astype(jnp.bfloat16)
    packed = packed.reshape(steps, group, 3, head_count, head_dim)
    time_scores = (
        jnp.einsum(
            "qshe,kshe->shqk",
            packed[:, :, 0],
            packed[:, :, 1],
            preferred_element_type=jnp.float32,
        )
        * score_scale
    )
    time_max = jnp.max(time_scores, axis=-1, keepdims=True)
    time_weights = jnp.exp(time_scores - time_max)
    time_weights = time_weights / jnp.sum(time_weights, axis=-1, keepdims=True)
    time_mix = jnp.einsum(
        "shqk,kshe->qshe",
        time_weights,
        packed[:, :, 2].astype(jnp.float32),
        precision=lax.Precision.HIGHEST,
    ).astype(jnp.bfloat16)
    time_mix = time_mix.reshape(steps, group, model_width)
    after_time = (after_agents.astype(jnp.float32) + project(time_mix, time_out)).astype(
        jnp.bfloat16
    )
    normed = layer_norm(after_time, norm_gains[2])
    hidden = jnp.maximum(project(normed, widen_weight), 0.0).astype(jnp.bfloat16)
    out = (after_time.astype(jnp.float32) + project(hidden, narrow_weight)).astype(jnp.bfloat16)
    out = lax.all_to_all(out, "ta", 0, 1, tiled=True)
    return out.reshape(tokens.shape)


def solution(mesh):
    in_specs = (
        P("gx", "gy", "ta", None, None),
        P("gx", "gy", "ta", None),
        P(),
        P("gx", "gy", None),
        P(),
        P(),
        P(),
        P(),
        P(),
        P(),
        P(),
        P(),
    )
    out_specs = P("gx", "gy", "ta", None, None)
    return jax.shard_map(
        per_device, mesh=mesh, in_specs=in_specs, out_specs=out_specs, check_vma=False
    )
```

```python
import functools
import math

import jax
import jax.numpy as jnp
from jax import lax
from jax.experimental import pallas as pl
from jax.sharding import PartitionSpec as P

HEADS = 8


EPSILON = 1e-05
NEGATIVE = -1e30


def shift(piece, axis, step):
    count = lax.axis_size(axis)
    if step > 0:
        pairs = [(i, i + 1) for i in range(count - 1)]
    else:
        pairs = [(i + 1, i) for i in range(count - 1)]
    return lax.ppermute(piece, axis, pairs)


def halo(piece):
    west = shift(piece, "gx", 1)
    east = shift(piece, "gx", -1)
    south = shift(piece, "gy", 1)
    north = shift(piece, "gy", -1)
    north_east = shift(north, "gx", -1)
    south_west = shift(south, "gx", 1)
    south_east = shift(east, "gy", 1)
    north_west = shift(west, "gy", -1)
    return [south_west, west, north_west, south, piece, north, south_east, east, north_east]


def layer_norm(values, gain_row):
    values = values.astype(jnp.float32)
    center = values - jnp.mean(values, axis=-1, keepdims=True)
    spread = jnp.mean(center * center, axis=-1, keepdims=True)
    return (center * lax.rsqrt(spread + EPSILON) * gain_row).astype(jnp.bfloat16)


def project(values, weight):
    return jnp.dot(values, weight, preferred_element_type=jnp.float32)


def agent_kernel(live_ref, q_ref, k_ref, v_ref, o_ref, *, scale, head_dim):
    live = live_ref[...] != 0
    queries = q_ref[0] * jnp.asarray(scale, q_ref.dtype)
    slots = k_ref.shape[1] * k_ref.shape[2]
    keys = k_ref[0].reshape(slots, k_ref.shape[3])
    values = v_ref[0].reshape(slots, v_ref.shape[3])
    rows = queries.shape[0]
    lane = lax.broadcasted_iota(jnp.int32, (1, queries.shape[1]), 1)
    first = lane < head_dim
    zero = jnp.zeros_like(queries)
    both = jnp.concatenate(
        [jnp.where(first, queries, zero), jnp.where(first, zero, queries)], axis=0
    )
    scores = lax.dot_general(
        both, keys, (((1,), (1,)), ((), ())), preferred_element_type=jnp.float32
    )
    scores = jnp.where(live, scores, NEGATIVE)
    row_max = jnp.max(scores, axis=-1, keepdims=True)
    weights = jnp.exp(scores - row_max)
    total = jnp.sum(weights, axis=-1, keepdims=True)
    weights = (weights * (1.0 / total)).astype(jnp.bfloat16)
    part = jnp.dot(weights, values, preferred_element_type=jnp.float32)
    o_ref[0] = jnp.where(first, part[:rows], part[rows:]).astype(o_ref.dtype)


def agent_attention(live, queries, kv, head_dim, interpret=False):
    moments, slot_count, model_width = queries.shape
    lanes = 2 * head_dim
    pairs = model_width // lanes
    near = kv.shape[1]
    body = functools.partial(agent_kernel, scale=1.0 / math.sqrt(head_dim), head_dim=head_dim)
    return pl.pallas_call(
        body,
        grid=(moments, pairs),
        in_specs=[
            pl.BlockSpec(live.shape, lambda t, p: (0, 0)),
            pl.BlockSpec((1, slot_count, lanes), lambda t, p: (t, 0, p)),
            pl.BlockSpec((1, near, slot_count, lanes), lambda t, p: (t, 0, 0, p)),
            pl.BlockSpec((1, near, slot_count, lanes), lambda t, p: (t, 0, 0, p + pairs)),
        ],
        out_specs=pl.BlockSpec((1, slot_count, lanes), lambda t, p: (t, 0, p)),
        out_shape=jax.ShapeDtypeStruct(queries.shape, jnp.bfloat16),
        interpret=interpret,
    )(live, queries, kv, kv)


def per_device(
    tokens,
    validity,
    tile_counts,
    neighbours,
    mask_token,
    norm_gains,
    agent_qkv,
    agent_out,
    time_qkv,
    time_out,
    widen_weight,
    narrow_weight,
):
    model_width = tokens.shape[-1]
    head_count = HEADS
    head_dim = model_width // head_count
    moments = tokens.shape[2]
    slot_count = tokens.shape[3]
    score_scale = 1.0 / math.sqrt(head_dim)
    rows = tokens.reshape(moments, slot_count, model_width)
    live_rows = validity.reshape(moments, slot_count)
    masked_input = jnp.where(live_rows[..., None] == 1, rows, mask_token)

    normed = layer_norm(masked_input, norm_gains[0])
    near = jnp.stack(halo(normed), axis=1)
    queries = project(normed, agent_qkv[:, :model_width]).astype(jnp.bfloat16)
    kv = project(near, agent_qkv[:, model_width:]).astype(jnp.bfloat16)
    column_index = lax.axis_index("gx")
    row_index = lax.axis_index("gy")
    padded_counts = jnp.pad(tile_counts, 1)
    near_counts = lax.dynamic_slice(padded_counts, (column_index, row_index), (3, 3))
    chosen = neighbours[0, 0].reshape(3, 3) == 1
    slot_ids = jnp.arange(slot_count, dtype=jnp.int32)
    key_live = ((slot_ids[None, None, :] < near_counts[:, :, None]) & chosen[:, :, None]).reshape(
        1, 9 * slot_count
    )
    mixed = agent_attention(key_live.astype(jnp.int32), queries, kv, head_dim)
    agent_proj = project(mixed, agent_out)
    after_agents = (masked_input.astype(jnp.float32) + agent_proj).astype(jnp.bfloat16)

    after_agents = lax.all_to_all(after_agents, "ta", 1, 0, tiled=True)
    steps = after_agents.shape[0]
    group = after_agents.shape[1]
    normed = layer_norm(after_agents, norm_gains[1])
    packed = project(normed, time_qkv).astype(jnp.bfloat16)
    packed = packed.reshape(steps, group, 3, head_count, head_dim)
    time_scores = (
        jnp.einsum(
            "qshe,kshe->shqk",
            packed[:, :, 0],
            packed[:, :, 1],
            preferred_element_type=jnp.float32,
        )
        * score_scale
    )
    time_max = jnp.max(time_scores, axis=-1, keepdims=True)
    time_weights = jnp.exp(time_scores - time_max)
    time_weights = time_weights / jnp.sum(time_weights, axis=-1, keepdims=True)
    time_mix = jnp.einsum(
        "shqk,kshe->qshe",
        time_weights,
        packed[:, :, 2].astype(jnp.float32),
        precision=lax.Precision.HIGHEST,
    ).astype(jnp.bfloat16)
    time_mix = time_mix.reshape(steps, group, model_width)
    after_time = (after_agents.astype(jnp.float32) + project(time_mix, time_out)).astype(
        jnp.bfloat16
    )
    normed = layer_norm(after_time, norm_gains[2])
    hidden = jnp.maximum(project(normed, widen_weight), 0.0).astype(jnp.bfloat16)
    out = (after_time.astype(jnp.float32) + project(hidden, narrow_weight)).astype(jnp.bfloat16)
    out = lax.all_to_all(out, "ta", 0, 1, tiled=True)
    return out.reshape(tokens.shape)


def solution(mesh):
    in_specs = (
        P("gx", "gy", "ta", None, None),
        P("gx", "gy", "ta", None),
        P(),
        P("gx", "gy", None),
        P(),
        P(),
        P(),
        P(),
        P(),
        P(),
        P(),
        P(),
    )
    out_specs = P("gx", "gy", "ta", None, None)
    return jax.shard_map(
        per_device, mesh=mesh, in_specs=in_specs, out_specs=out_specs, check_vma=False
    )
```

```python
import functools
import math

import jax
import jax.numpy as jnp
from jax import lax
from jax.experimental import pallas as pl
from jax.sharding import PartitionSpec as P

HEADS = 8


EPSILON = 1e-05
NEGATIVE = -1e30


def shift(piece, axis, step):
    count = lax.axis_size(axis)
    if step > 0:
        pairs = [(i, i + 1) for i in range(count - 1)]
    else:
        pairs = [(i + 1, i) for i in range(count - 1)]
    return lax.ppermute(piece, axis, pairs)


def halo(piece):
    west = shift(piece, "gx", 1)
    east = shift(piece, "gx", -1)
    south = shift(piece, "gy", 1)
    north = shift(piece, "gy", -1)
    north_east = shift(north, "gx", -1)
    south_west = shift(south, "gx", 1)
    south_east = shift(east, "gy", 1)
    north_west = shift(west, "gy", -1)
    return [south_west, west, north_west, south, piece, north, south_east, east, north_east]


def layer_norm(values, gain_row):
    values = values.astype(jnp.float32)
    center = values - jnp.mean(values, axis=-1, keepdims=True)
    spread = jnp.mean(center * center, axis=-1, keepdims=True)
    return (center * lax.rsqrt(spread + EPSILON) * gain_row).astype(jnp.bfloat16)


def project(values, weight):
    return jnp.dot(values, weight, preferred_element_type=jnp.float32)


def agent_kernel(live_ref, q_ref, k_ref, v_ref, o_ref, *, scale, head_dim):
    live = live_ref[...] != 0
    queries = q_ref[0] * jnp.asarray(scale, q_ref.dtype)
    slots = k_ref.shape[1] * k_ref.shape[2]
    keys = k_ref[0].reshape(slots, k_ref.shape[3])
    values = v_ref[0].reshape(slots, v_ref.shape[3])
    rows = queries.shape[0]
    lane = lax.broadcasted_iota(jnp.int32, (1, queries.shape[1]), 1)
    first = lane < head_dim
    zero = jnp.zeros_like(queries)
    both = jnp.concatenate(
        [jnp.where(first, queries, zero), jnp.where(first, zero, queries)], axis=0
    )
    scores = lax.dot_general(
        both, keys, (((1,), (1,)), ((), ())), preferred_element_type=jnp.float32
    )
    scores = jnp.where(live, scores, NEGATIVE)
    row_max = jnp.max(scores, axis=-1, keepdims=True)
    weights = jnp.exp(scores - row_max)
    total = jnp.sum(weights, axis=-1, keepdims=True)
    weights = (weights * (1.0 / total)).astype(jnp.bfloat16)
    part = jnp.dot(weights, values, preferred_element_type=jnp.float32)
    o_ref[0] = jnp.where(first, part[:rows], part[rows:]).astype(o_ref.dtype)


def agent_attention(live, queries, kv, head_dim, interpret=False):
    moments, slot_count, model_width = queries.shape
    lanes = 2 * head_dim
    pairs = model_width // lanes
    near = kv.shape[1]
    body = functools.partial(agent_kernel, scale=1.0 / math.sqrt(head_dim), head_dim=head_dim)
    return pl.pallas_call(
        body,
        grid=(moments, pairs),
        in_specs=[
            pl.BlockSpec(live.shape, lambda t, p: (0, 0)),
            pl.BlockSpec((1, slot_count, lanes), lambda t, p: (t, 0, p)),
            pl.BlockSpec((1, near, slot_count, lanes), lambda t, p: (t, 0, 0, p)),
            pl.BlockSpec((1, near, slot_count, lanes), lambda t, p: (t, 0, 0, p + pairs)),
        ],
        out_specs=pl.BlockSpec((1, slot_count, lanes), lambda t, p: (t, 0, p)),
        out_shape=jax.ShapeDtypeStruct(queries.shape, jnp.bfloat16),
        interpret=interpret,
    )(live, queries, kv, kv)


def norm_kernel(x_ref, valid_ref, token_ref, gain_ref, masked_ref, normed_ref):
    masked = jnp.where(valid_ref[0] == 1, x_ref[0], token_ref[...])
    masked_ref[0] = masked
    values = masked.astype(jnp.float32)
    center = values - jnp.mean(values, axis=-1, keepdims=True)
    spread = jnp.mean(center * center, axis=-1, keepdims=True)
    normed_ref[0] = (center * lax.rsqrt(spread + EPSILON) * gain_ref[...]).astype(normed_ref.dtype)


def mask_and_norm(rows, live_rows, mask_token, gain_row, interpret=False):
    moments, slot_count, model_width = rows.shape
    row_spec = pl.BlockSpec((1, slot_count, model_width), lambda t: (t, 0, 0))
    return pl.pallas_call(
        norm_kernel,
        grid=(moments,),
        in_specs=[
            row_spec,
            pl.BlockSpec((1, slot_count, 1), lambda t: (t, 0, 0)),
            pl.BlockSpec((1, model_width), lambda t: (0, 0)),
            pl.BlockSpec((1, model_width), lambda t: (0, 0)),
        ],
        out_specs=[row_spec, row_spec],
        out_shape=[jax.ShapeDtypeStruct(rows.shape, rows.dtype)] * 2,
        interpret=interpret,
    )(
        rows,
        live_rows.reshape(moments, slot_count, 1),
        mask_token.reshape(1, model_width),
        gain_row.reshape(1, model_width),
    )


def time_kernel(p_ref, o_ref, *, group, head_dim, scale):
    packed = p_ref[...]
    count = packed.shape[0]
    width = packed.shape[1] // 3
    queries = packed[:, :width] * jnp.asarray(scale, packed.dtype)
    keys = packed[:, width : 2 * width]
    values = packed[:, 2 * width :].astype(jnp.float32)
    row = lax.broadcasted_iota(jnp.int32, (count, count), 0) % group
    col = lax.broadcasted_iota(jnp.int32, (count, count), 1) % group
    same = row == col
    lane = lax.broadcasted_iota(jnp.int32, (1, width), 1)
    pair_lane = lax.broadcasted_iota(jnp.int32, (1, 2 * head_dim), 1)
    zero = jnp.zeros_like(queries)
    pieces = []
    for pair in range(width // (2 * head_dim)):
        halves = []
        for head in (2 * pair, 2 * pair + 1):
            own = jnp.where((lane // head_dim) == head, queries, zero)
            scores = lax.dot_general(
                own, keys, (((1,), (1,)), ((), ())), preferred_element_type=jnp.float32
            )
            scores = jnp.where(same, scores, NEGATIVE)
            row_max = jnp.max(scores, axis=-1, keepdims=True)
            weights = jnp.exp(scores - row_max)
            weights = weights / jnp.sum(weights, axis=-1, keepdims=True)
            halves.append(
                jnp.dot(
                    weights,
                    values[:, pair * 2 * head_dim : (pair + 1) * 2 * head_dim],
                    precision=lax.Precision.HIGHEST,
                    preferred_element_type=jnp.float32,
                )
            )
        pieces.append(jnp.where(pair_lane < head_dim, halves[0], halves[1]))
    o_ref[...] = jnp.concatenate(pieces, axis=1).astype(o_ref.dtype)


def time_attention(packed, group, head_dim, interpret=False):
    count, width3 = packed.shape
    body = functools.partial(
        time_kernel, group=group, head_dim=head_dim, scale=1.0 / math.sqrt(head_dim)
    )
    return pl.pallas_call(
        body,
        grid=(1,),
        in_specs=[pl.BlockSpec((count, width3), lambda i: (0, 0))],
        out_specs=pl.BlockSpec((count, width3 // 3), lambda i: (0, 0)),
        out_shape=jax.ShapeDtypeStruct((count, width3 // 3), packed.dtype),
        interpret=interpret,
    )(packed)


def per_device(
    tokens,
    validity,
    tile_counts,
    neighbours,
    mask_token,
    norm_gains,
    agent_qkv,
    agent_out,
    time_qkv,
    time_out,
    widen_weight,
    narrow_weight,
):
    model_width = tokens.shape[-1]
    head_count = HEADS
    head_dim = model_width // head_count
    moments = tokens.shape[2]
    slot_count = tokens.shape[3]
    score_scale = 1.0 / math.sqrt(head_dim)
    rows = tokens.reshape(moments, slot_count, model_width)
    live_rows = validity.reshape(moments, slot_count)
    masked_input, normed = mask_and_norm(rows, live_rows, mask_token, norm_gains[0])

    near = jnp.stack(halo(normed), axis=1)
    queries = project(normed, agent_qkv[:, :model_width]).astype(jnp.bfloat16)
    kv = project(near, agent_qkv[:, model_width:]).astype(jnp.bfloat16)
    column_index = lax.axis_index("gx")
    row_index = lax.axis_index("gy")
    padded_counts = jnp.pad(tile_counts, 1)
    near_counts = lax.dynamic_slice(padded_counts, (column_index, row_index), (3, 3))
    chosen = neighbours[0, 0].reshape(3, 3) == 1
    slot_ids = jnp.arange(slot_count, dtype=jnp.int32)
    key_live = ((slot_ids[None, None, :] < near_counts[:, :, None]) & chosen[:, :, None]).reshape(
        1, 9 * slot_count
    )
    mixed = agent_attention(key_live.astype(jnp.int32), queries, kv, head_dim)
    agent_proj = project(mixed, agent_out)
    after_agents = (masked_input.astype(jnp.float32) + agent_proj).astype(jnp.bfloat16)

    after_agents = lax.all_to_all(after_agents, "ta", 1, 0, tiled=True)
    steps = after_agents.shape[0]
    group = after_agents.shape[1]
    normed = layer_norm(after_agents, norm_gains[1])
    packed = project(normed, time_qkv).astype(jnp.bfloat16)
    time_mix = time_attention(packed.reshape(steps * group, 3 * model_width), group, head_dim)
    time_mix = time_mix.reshape(steps, group, model_width)
    after_time = (after_agents.astype(jnp.float32) + project(time_mix, time_out)).astype(
        jnp.bfloat16
    )
    normed = layer_norm(after_time, norm_gains[2])
    hidden = jnp.maximum(project(normed, widen_weight), 0.0).astype(jnp.bfloat16)
    out = (after_time.astype(jnp.float32) + project(hidden, narrow_weight)).astype(jnp.bfloat16)
    out = lax.all_to_all(out, "ta", 0, 1, tiled=True)
    return out.reshape(tokens.shape)


def solution(mesh):
    in_specs = (
        P("gx", "gy", "ta", None, None),
        P("gx", "gy", "ta", None),
        P(),
        P("gx", "gy", None),
        P(),
        P(),
        P(),
        P(),
        P(),
        P(),
        P(),
        P(),
    )
    out_specs = P("gx", "gy", "ta", None, None)
    return jax.shard_map(
        per_device, mesh=mesh, in_specs=in_specs, out_specs=out_specs, check_vma=False
    )
```

```python
import functools
import math

import jax
import jax.numpy as jnp
from jax import lax
from jax.experimental import pallas as pl
from jax.sharding import PartitionSpec as P

HEADS = 8


EPSILON = 1e-05
NEGATIVE = -1e30


def shift(piece, axis, step):
    count = lax.axis_size(axis)
    if step > 0:
        pairs = [(i, i + 1) for i in range(count - 1)]
    else:
        pairs = [(i + 1, i) for i in range(count - 1)]
    return lax.ppermute(piece, axis, pairs)


def halo(piece):
    west = shift(piece, "gx", 1)
    east = shift(piece, "gx", -1)
    south = shift(piece, "gy", 1)
    north = shift(piece, "gy", -1)
    north_east = shift(north, "gx", -1)
    south_west = shift(south, "gx", 1)
    south_east = shift(east, "gy", 1)
    north_west = shift(west, "gy", -1)
    return [south_west, west, north_west, south, piece, north, south_east, east, north_east]


def layer_norm(values, gain_row):
    values = values.astype(jnp.float32)
    center = values - jnp.mean(values, axis=-1, keepdims=True)
    spread = jnp.mean(center * center, axis=-1, keepdims=True)
    return (center * lax.rsqrt(spread + EPSILON) * gain_row).astype(jnp.bfloat16)


def project(values, weight):
    return jnp.dot(values, weight, preferred_element_type=jnp.float32)


def agent_kernel(live_ref, q_ref, k_ref, v_ref, o_ref, *, scale, head_dim):
    live = live_ref[...] != 0
    queries = q_ref[0] * jnp.asarray(scale, q_ref.dtype)
    slots = k_ref.shape[1] * k_ref.shape[2]
    keys = k_ref[0].reshape(slots, k_ref.shape[3])
    values = v_ref[0].reshape(slots, v_ref.shape[3])
    rows = queries.shape[0]
    lane = lax.broadcasted_iota(jnp.int32, (1, queries.shape[1]), 1)
    first = lane < head_dim
    zero = jnp.zeros_like(queries)
    both = jnp.concatenate(
        [jnp.where(first, queries, zero), jnp.where(first, zero, queries)], axis=0
    )
    scores = lax.dot_general(
        both, keys, (((1,), (1,)), ((), ())), preferred_element_type=jnp.float32
    )
    scores = jnp.where(live, scores, NEGATIVE)
    row_max = jnp.max(scores, axis=-1, keepdims=True)
    weights = jnp.exp(scores - row_max)
    total = jnp.sum(weights, axis=-1, keepdims=True)
    weights = (weights * (1.0 / total)).astype(jnp.bfloat16)
    part = jnp.dot(weights, values, preferred_element_type=jnp.float32)
    o_ref[0] = jnp.where(first, part[:rows], part[rows:]).astype(o_ref.dtype)


def agent_attention(live, queries, kv, head_dim, interpret=False):
    moments, slot_count, model_width = queries.shape
    lanes = 2 * head_dim
    pairs = model_width // lanes
    near = kv.shape[1]
    body = functools.partial(agent_kernel, scale=1.0 / math.sqrt(head_dim), head_dim=head_dim)
    return pl.pallas_call(
        body,
        grid=(moments, pairs),
        in_specs=[
            pl.BlockSpec(live.shape, lambda t, p: (0, 0)),
            pl.BlockSpec((1, slot_count, lanes), lambda t, p: (t, 0, p)),
            pl.BlockSpec((1, near, slot_count, lanes), lambda t, p: (t, 0, 0, p)),
            pl.BlockSpec((1, near, slot_count, lanes), lambda t, p: (t, 0, 0, p + pairs)),
        ],
        out_specs=pl.BlockSpec((1, slot_count, lanes), lambda t, p: (t, 0, p)),
        out_shape=jax.ShapeDtypeStruct(queries.shape, jnp.bfloat16),
        interpret=interpret,
    )(live, queries, kv, kv)


def time_kernel(p_ref, o_ref, *, group, head_dim, scale):
    packed = p_ref[...]
    count = packed.shape[0]
    width = packed.shape[1] // 3
    lanes = 2 * head_dim
    row = lax.broadcasted_iota(jnp.int32, (count, count), 0) % group
    col = lax.broadcasted_iota(jnp.int32, (count, count), 1) % group
    same = row == col
    first = lax.broadcasted_iota(jnp.int32, (1, lanes), 1) < head_dim
    pieces = []
    for pair in range(width // lanes):
        start = pair * lanes
        queries = packed[:, start : start + lanes] * jnp.asarray(scale, packed.dtype)
        keys = packed[:, width + start : width + start + lanes]
        values = packed[:, 2 * width + start : 2 * width + start + lanes]
        zero = jnp.zeros_like(queries)
        halves = []
        for own in (jnp.where(first, queries, zero), jnp.where(first, zero, queries)):
            scores = lax.dot_general(
                own, keys, (((1,), (1,)), ((), ())), preferred_element_type=jnp.float32
            )
            scores = jnp.where(same, scores, NEGATIVE)
            row_max = jnp.max(scores, axis=-1, keepdims=True)
            weights = jnp.exp(scores - row_max)
            weights = weights / jnp.sum(weights, axis=-1, keepdims=True)
            high = weights.astype(jnp.bfloat16)
            low = (weights - high.astype(jnp.float32)).astype(jnp.bfloat16)
            halves.append(
                jnp.dot(high, values, preferred_element_type=jnp.float32)
                + jnp.dot(low, values, preferred_element_type=jnp.float32)
            )
        pieces.append(jnp.where(first, halves[0], halves[1]))
    o_ref[...] = jnp.concatenate(pieces, axis=1).astype(o_ref.dtype)


def time_attention(packed, group, head_dim, interpret=False):
    count, width3 = packed.shape
    body = functools.partial(
        time_kernel, group=group, head_dim=head_dim, scale=1.0 / math.sqrt(head_dim)
    )
    return pl.pallas_call(
        body,
        grid=(1,),
        in_specs=[pl.BlockSpec((count, width3), lambda i: (0, 0))],
        out_specs=pl.BlockSpec((count, width3 // 3), lambda i: (0, 0)),
        out_shape=jax.ShapeDtypeStruct((count, width3 // 3), packed.dtype),
        interpret=interpret,
    )(packed)


def per_device(
    tokens,
    validity,
    tile_counts,
    neighbours,
    mask_token,
    norm_gains,
    agent_qkv,
    agent_out,
    time_qkv,
    time_out,
    widen_weight,
    narrow_weight,
):
    model_width = tokens.shape[-1]
    head_count = HEADS
    head_dim = model_width // head_count
    moments = tokens.shape[2]
    slot_count = tokens.shape[3]
    score_scale = 1.0 / math.sqrt(head_dim)
    rows = tokens.reshape(moments, slot_count, model_width)
    live_rows = validity.reshape(moments, slot_count)
    masked_input = jnp.where(live_rows[..., None] == 1, rows, mask_token)
    normed = layer_norm(masked_input, norm_gains[0])

    near = jnp.stack(halo(normed), axis=1)
    queries = project(normed, agent_qkv[:, :model_width]).astype(jnp.bfloat16)
    kv = project(near, agent_qkv[:, model_width:]).astype(jnp.bfloat16)
    column_index = lax.axis_index("gx")
    row_index = lax.axis_index("gy")
    padded_counts = jnp.pad(tile_counts, 1)
    near_counts = lax.dynamic_slice(padded_counts, (column_index, row_index), (3, 3))
    chosen = neighbours[0, 0].reshape(3, 3) == 1
    slot_ids = jnp.arange(slot_count, dtype=jnp.int32)
    key_live = ((slot_ids[None, None, :] < near_counts[:, :, None]) & chosen[:, :, None]).reshape(
        1, 9 * slot_count
    )
    mixed = agent_attention(key_live.astype(jnp.int32), queries, kv, head_dim)
    agent_proj = project(mixed, agent_out)
    after_agents = (masked_input.astype(jnp.float32) + agent_proj).astype(jnp.bfloat16)

    after_agents = lax.all_to_all(after_agents, "ta", 1, 0, tiled=True)
    steps = after_agents.shape[0]
    group = after_agents.shape[1]
    normed = layer_norm(after_agents, norm_gains[1])
    packed = project(normed, time_qkv).astype(jnp.bfloat16)
    time_mix = time_attention(packed.reshape(steps * group, 3 * model_width), group, head_dim)
    time_mix = time_mix.reshape(steps, group, model_width)
    after_time = (after_agents.astype(jnp.float32) + project(time_mix, time_out)).astype(
        jnp.bfloat16
    )
    normed = layer_norm(after_time, norm_gains[2])
    hidden = jnp.maximum(project(normed, widen_weight), 0.0).astype(jnp.bfloat16)
    out = (after_time.astype(jnp.float32) + project(hidden, narrow_weight)).astype(jnp.bfloat16)
    out = lax.all_to_all(out, "ta", 0, 1, tiled=True)
    return out.reshape(tokens.shape)


def solution(mesh):
    in_specs = (
        P("gx", "gy", "ta", None, None),
        P("gx", "gy", "ta", None),
        P(),
        P("gx", "gy", None),
        P(),
        P(),
        P(),
        P(),
        P(),
        P(),
        P(),
        P(),
    )
    out_specs = P("gx", "gy", "ta", None, None)
    return jax.shard_map(
        per_device, mesh=mesh, in_specs=in_specs, out_specs=out_specs, check_vma=False
    )
```

```python
import functools
import math

import jax
import jax.numpy as jnp
from jax import lax
from jax.experimental import pallas as pl
from jax.experimental.pallas import tpu as pltpu
from jax.sharding import PartitionSpec as P

HEADS = 8


EPSILON = 1e-05
NEGATIVE = -1e30


def shift(piece, axis, step):
    count = lax.axis_size(axis)
    if step > 0:
        pairs = [(i, i + 1) for i in range(count - 1)]
    else:
        pairs = [(i + 1, i) for i in range(count - 1)]
    return lax.ppermute(piece, axis, pairs)


def halo(piece):
    west = shift(piece, "gx", 1)
    east = shift(piece, "gx", -1)
    south = shift(piece, "gy", 1)
    north = shift(piece, "gy", -1)
    north_east = shift(north, "gx", -1)
    south_west = shift(south, "gx", 1)
    south_east = shift(east, "gy", 1)
    north_west = shift(west, "gy", -1)
    return [south_west, west, north_west, south, piece, north, south_east, east, north_east]


def layer_norm(values, gain_row):
    values = values.astype(jnp.float32)
    center = values - jnp.mean(values, axis=-1, keepdims=True)
    spread = jnp.mean(center * center, axis=-1, keepdims=True)
    return (center * lax.rsqrt(spread + EPSILON) * gain_row).astype(jnp.bfloat16)


def project(values, weight):
    return jnp.dot(values, weight, preferred_element_type=jnp.float32)


def agent_kernel(
    live_ref, q_ref, near_ref, wk_ref, wv_ref, wo_ref, x_ref, o_ref, acc_ref, *, scale, head_dim
):
    pair = pl.program_id(1)
    live = live_ref[...] != 0
    rows = near_ref[0].reshape(near_ref.shape[1] * near_ref.shape[2], near_ref.shape[3])
    keys = jnp.dot(rows, wk_ref[...], preferred_element_type=jnp.float32).astype(jnp.bfloat16)
    values = jnp.dot(rows, wv_ref[...], preferred_element_type=jnp.float32).astype(jnp.bfloat16)
    queries = q_ref[0] * jnp.asarray(scale, q_ref.dtype)
    count = queries.shape[0]
    lane = lax.broadcasted_iota(jnp.int32, (1, queries.shape[1]), 1)
    first = lane < head_dim
    zero = jnp.zeros_like(queries)
    both = jnp.concatenate(
        [jnp.where(first, queries, zero), jnp.where(first, zero, queries)], axis=0
    )
    scores = lax.dot_general(
        both, keys, (((1,), (1,)), ((), ())), preferred_element_type=jnp.float32
    )
    scores = jnp.where(live, scores, NEGATIVE)
    row_max = jnp.max(scores, axis=-1, keepdims=True)
    weights = jnp.exp(scores - row_max)
    total = jnp.sum(weights, axis=-1, keepdims=True)
    weights = (weights * (1.0 / total)).astype(jnp.bfloat16)
    part = jnp.dot(weights, values, preferred_element_type=jnp.float32)
    mixed = jnp.where(first, part[:count], part[count:]).astype(jnp.bfloat16)
    contribution = jnp.dot(mixed, wo_ref[...], preferred_element_type=jnp.float32)

    @pl.when(pair == 0)
    def _():
        acc_ref[...] = contribution

    @pl.when(pair > 0)
    def _():
        acc_ref[...] += contribution

    @pl.when(pair == pl.num_programs(1) - 1)
    def _():
        o_ref[0] = (x_ref[0].astype(jnp.float32) + acc_ref[...]).astype(o_ref.dtype)


def agent_attention(live, queries, near, agent_qkv, agent_out, masked_input, head_dim):
    moments, slot_count, model_width = queries.shape
    lanes = 2 * head_dim
    pairs = model_width // lanes
    body = functools.partial(agent_kernel, scale=1.0 / math.sqrt(head_dim), head_dim=head_dim)
    return pl.pallas_call(
        body,
        grid=(moments, pairs),
        in_specs=[
            pl.BlockSpec(live.shape, lambda t, p: (0, 0)),
            pl.BlockSpec((1, slot_count, lanes), lambda t, p: (t, 0, p)),
            pl.BlockSpec((1,) + near.shape[1:], lambda t, p: (t, 0, 0, 0)),
            pl.BlockSpec((model_width, lanes), lambda t, p: (0, pairs + p)),
            pl.BlockSpec((model_width, lanes), lambda t, p: (0, 2 * pairs + p)),
            pl.BlockSpec((lanes, model_width), lambda t, p: (p, 0)),
            pl.BlockSpec((1, slot_count, model_width), lambda t, p: (t, 0, 0)),
        ],
        out_specs=pl.BlockSpec((1, slot_count, model_width), lambda t, p: (t, 0, 0)),
        out_shape=jax.ShapeDtypeStruct(queries.shape, jnp.bfloat16),
        scratch_shapes=[pltpu.VMEM((slot_count, model_width), jnp.float32)],
        compiler_params=pltpu.CompilerParams(dimension_semantics=("parallel", "arbitrary")),
    )(live, queries, near, agent_qkv, agent_qkv, agent_out, masked_input)

def time_kernel(p_ref, o_ref, *, group, head_dim, scale):
    packed = p_ref[...]
    count = packed.shape[0]
    width = packed.shape[1] // 3
    lanes = 2 * head_dim
    row = lax.broadcasted_iota(jnp.int32, (count, count), 0) % group
    col = lax.broadcasted_iota(jnp.int32, (count, count), 1) % group
    same = row == col
    first = lax.broadcasted_iota(jnp.int32, (1, lanes), 1) < head_dim
    pieces = []
    for pair in range(width // lanes):
        start = pair * lanes
        queries = packed[:, start : start + lanes] * jnp.asarray(scale, packed.dtype)
        keys = packed[:, width + start : width + start + lanes]
        values = packed[:, 2 * width + start : 2 * width + start + lanes]
        zero = jnp.zeros_like(queries)
        halves = []
        for own in (jnp.where(first, queries, zero), jnp.where(first, zero, queries)):
            scores = lax.dot_general(
                own, keys, (((1,), (1,)), ((), ())), preferred_element_type=jnp.float32
            )
            scores = jnp.where(same, scores, NEGATIVE)
            row_max = jnp.max(scores, axis=-1, keepdims=True)
            weights = jnp.exp(scores - row_max)
            weights = weights / jnp.sum(weights, axis=-1, keepdims=True)
            high = weights.astype(jnp.bfloat16)
            low = (weights - high.astype(jnp.float32)).astype(jnp.bfloat16)
            halves.append(
                jnp.dot(high, values, preferred_element_type=jnp.float32)
                + jnp.dot(low, values, preferred_element_type=jnp.float32)
            )
        pieces.append(jnp.where(first, halves[0], halves[1]))
    o_ref[...] = jnp.concatenate(pieces, axis=1).astype(o_ref.dtype)


def time_attention(packed, group, head_dim, interpret=False):
    count, width3 = packed.shape
    body = functools.partial(
        time_kernel, group=group, head_dim=head_dim, scale=1.0 / math.sqrt(head_dim)
    )
    return pl.pallas_call(
        body,
        grid=(1,),
        in_specs=[pl.BlockSpec((count, width3), lambda i: (0, 0))],
        out_specs=pl.BlockSpec((count, width3 // 3), lambda i: (0, 0)),
        out_shape=jax.ShapeDtypeStruct((count, width3 // 3), packed.dtype),
        interpret=interpret,
    )(packed)


def per_device(
    tokens,
    validity,
    tile_counts,
    neighbours,
    mask_token,
    norm_gains,
    agent_qkv,
    agent_out,
    time_qkv,
    time_out,
    widen_weight,
    narrow_weight,
):
    model_width = tokens.shape[-1]
    head_count = HEADS
    head_dim = model_width // head_count
    moments = tokens.shape[2]
    slot_count = tokens.shape[3]
    score_scale = 1.0 / math.sqrt(head_dim)
    rows = tokens.reshape(moments, slot_count, model_width)
    live_rows = validity.reshape(moments, slot_count)
    masked_input = jnp.where(live_rows[..., None] == 1, rows, mask_token)
    normed = layer_norm(masked_input, norm_gains[0])

    near = jnp.stack(halo(normed), axis=1)
    queries = project(normed, agent_qkv[:, :model_width]).astype(jnp.bfloat16)
    column_index = lax.axis_index("gx")
    row_index = lax.axis_index("gy")
    padded_counts = jnp.pad(tile_counts, 1)
    near_counts = lax.dynamic_slice(padded_counts, (column_index, row_index), (3, 3))
    chosen = neighbours[0, 0].reshape(3, 3) == 1
    slot_ids = jnp.arange(slot_count, dtype=jnp.int32)
    key_live = ((slot_ids[None, None, :] < near_counts[:, :, None]) & chosen[:, :, None]).reshape(
        1, 9 * slot_count
    )
    after_agents = agent_attention(
        key_live.astype(jnp.int32), queries, near, agent_qkv, agent_out, masked_input, head_dim
    )

    after_agents = lax.all_to_all(after_agents, "ta", 1, 0, tiled=True)
    steps = after_agents.shape[0]
    group = after_agents.shape[1]
    normed = layer_norm(after_agents, norm_gains[1])
    packed = project(normed, time_qkv).astype(jnp.bfloat16)
    time_mix = time_attention(packed.reshape(steps * group, 3 * model_width), group, head_dim)
    time_mix = time_mix.reshape(steps, group, model_width)
    after_time = (after_agents.astype(jnp.float32) + project(time_mix, time_out)).astype(
        jnp.bfloat16
    )
    normed = layer_norm(after_time, norm_gains[2])
    hidden = jnp.maximum(project(normed, widen_weight), 0.0).astype(jnp.bfloat16)
    out = (after_time.astype(jnp.float32) + project(hidden, narrow_weight)).astype(jnp.bfloat16)
    out = lax.all_to_all(out, "ta", 0, 1, tiled=True)
    return out.reshape(tokens.shape)


def solution(mesh):
    in_specs = (
        P("gx", "gy", "ta", None, None),
        P("gx", "gy", "ta", None),
        P(),
        P("gx", "gy", None),
        P(),
        P(),
        P(),
        P(),
        P(),
        P(),
        P(),
        P(),
    )
    out_specs = P("gx", "gy", "ta", None, None)
    return jax.shard_map(
        per_device, mesh=mesh, in_specs=in_specs, out_specs=out_specs, check_vma=False
    )
```

```python
import functools
import math

import jax
import jax.numpy as jnp
from jax import lax
from jax.experimental import pallas as pl
from jax.sharding import PartitionSpec as P

HEADS = 8


EPSILON = 1e-05
NEGATIVE = -1e30


def shift(piece, axis, step):
    count = lax.axis_size(axis)
    if step > 0:
        pairs = [(i, i + 1) for i in range(count - 1)]
    else:
        pairs = [(i + 1, i) for i in range(count - 1)]
    return lax.ppermute(piece, axis, pairs)


def halo(piece):
    west = shift(piece, "gx", 1)
    east = shift(piece, "gx", -1)
    south = shift(piece, "gy", 1)
    north = shift(piece, "gy", -1)
    north_east = shift(north, "gx", -1)
    south_west = shift(south, "gx", 1)
    south_east = shift(east, "gy", 1)
    north_west = shift(west, "gy", -1)
    return [south_west, west, north_west, south, piece, north, south_east, east, north_east]


def layer_norm(values, gain_row):
    values = values.astype(jnp.float32)
    center = values - jnp.mean(values, axis=-1, keepdims=True)
    spread = jnp.mean(center * center, axis=-1, keepdims=True)
    return (center * lax.rsqrt(spread + EPSILON) * gain_row).astype(jnp.bfloat16)


def project(values, weight):
    return jnp.dot(values, weight, preferred_element_type=jnp.float32)


def agent_kernel(live_ref, q_ref, k_ref, v_ref, o_ref, *, scale, head_dim):
    live = live_ref[...] != 0
    queries = q_ref[0] * jnp.asarray(scale, q_ref.dtype)
    slots = k_ref.shape[1] * k_ref.shape[2]
    keys = k_ref[0].reshape(slots, k_ref.shape[3])
    values = v_ref[0].reshape(slots, v_ref.shape[3])
    rows = queries.shape[0]
    lane = lax.broadcasted_iota(jnp.int32, (1, queries.shape[1]), 1)
    first = lane < head_dim
    zero = jnp.zeros_like(queries)
    both = jnp.concatenate(
        [jnp.where(first, queries, zero), jnp.where(first, zero, queries)], axis=0
    )
    scores = lax.dot_general(
        both, keys, (((1,), (1,)), ((), ())), preferred_element_type=jnp.float32
    )
    scores = jnp.where(live, scores, NEGATIVE)
    row_max = jnp.max(scores, axis=-1, keepdims=True)
    weights = jnp.exp(scores - row_max)
    total = jnp.sum(weights, axis=-1, keepdims=True)
    weights = (weights * (1.0 / total)).astype(jnp.bfloat16)
    part = jnp.dot(weights, values, preferred_element_type=jnp.float32)
    o_ref[0] = jnp.where(first, part[:rows], part[rows:]).astype(o_ref.dtype)


def agent_attention(live, queries, kv, head_dim, interpret=False):
    moments, slot_count, model_width = queries.shape
    lanes = 2 * head_dim
    pairs = model_width // lanes
    near = kv.shape[1]
    body = functools.partial(agent_kernel, scale=1.0 / math.sqrt(head_dim), head_dim=head_dim)
    return pl.pallas_call(
        body,
        grid=(moments, pairs),
        in_specs=[
            pl.BlockSpec(live.shape, lambda t, p: (0, 0)),
            pl.BlockSpec((1, slot_count, lanes), lambda t, p: (t, 0, p)),
            pl.BlockSpec((1, near, slot_count, lanes), lambda t, p: (t, 0, 0, p)),
            pl.BlockSpec((1, near, slot_count, lanes), lambda t, p: (t, 0, 0, p + pairs)),
        ],
        out_specs=pl.BlockSpec((1, slot_count, lanes), lambda t, p: (t, 0, p)),
        out_shape=jax.ShapeDtypeStruct(queries.shape, jnp.bfloat16),
        interpret=interpret,
    )(live, queries, kv, kv)


def norm_kernel(x_ref, gain_ref, o_ref, *, row):
    values = x_ref[...].astype(jnp.float32)
    center = values - jnp.mean(values, axis=-1, keepdims=True)
    spread = jnp.mean(center * center, axis=-1, keepdims=True)
    gain = gain_ref[row : row + 1, :]
    o_ref[...] = (center * lax.rsqrt(spread + EPSILON) * gain).astype(o_ref.dtype)


def first_norm(masked_input, norm_gains):
    return pl.pallas_call(
        functools.partial(norm_kernel, row=0),
        grid=(1,),
        in_specs=[
            pl.BlockSpec(masked_input.shape, lambda i: (0, 0, 0)),
            pl.BlockSpec(norm_gains.shape, lambda i: (0, 0)),
        ],
        out_specs=pl.BlockSpec(masked_input.shape, lambda i: (0, 0, 0)),
        out_shape=jax.ShapeDtypeStruct(masked_input.shape, jnp.bfloat16),
    )(masked_input, norm_gains)


def time_kernel(p_ref, o_ref, *, group, head_dim, scale):
    packed = p_ref[...]
    count = packed.shape[0]
    width = packed.shape[1] // 3
    lanes = 2 * head_dim
    row = lax.broadcasted_iota(jnp.int32, (count, count), 0) % group
    col = lax.broadcasted_iota(jnp.int32, (count, count), 1) % group
    same = row == col
    first = lax.broadcasted_iota(jnp.int32, (1, lanes), 1) < head_dim
    pieces = []
    for pair in range(width // lanes):
        start = pair * lanes
        queries = packed[:, start : start + lanes] * jnp.asarray(scale, packed.dtype)
        keys = packed[:, width + start : width + start + lanes]
        values = packed[:, 2 * width + start : 2 * width + start + lanes]
        zero = jnp.zeros_like(queries)
        halves = []
        for own in (jnp.where(first, queries, zero), jnp.where(first, zero, queries)):
            scores = lax.dot_general(
                own, keys, (((1,), (1,)), ((), ())), preferred_element_type=jnp.float32
            )
            scores = jnp.where(same, scores, NEGATIVE)
            row_max = jnp.max(scores, axis=-1, keepdims=True)
            weights = jnp.exp(scores - row_max)
            weights = weights / jnp.sum(weights, axis=-1, keepdims=True)
            high = weights.astype(jnp.bfloat16)
            low = (weights - high.astype(jnp.float32)).astype(jnp.bfloat16)
            halves.append(
                jnp.dot(high, values, preferred_element_type=jnp.float32)
                + jnp.dot(low, values, preferred_element_type=jnp.float32)
            )
        pieces.append(jnp.where(first, halves[0], halves[1]))
    o_ref[...] = jnp.concatenate(pieces, axis=1).astype(o_ref.dtype)


def time_attention(packed, group, head_dim, interpret=False):
    count, width3 = packed.shape
    body = functools.partial(
        time_kernel, group=group, head_dim=head_dim, scale=1.0 / math.sqrt(head_dim)
    )
    return pl.pallas_call(
        body,
        grid=(1,),
        in_specs=[pl.BlockSpec((count, width3), lambda i: (0, 0))],
        out_specs=pl.BlockSpec((count, width3 // 3), lambda i: (0, 0)),
        out_shape=jax.ShapeDtypeStruct((count, width3 // 3), packed.dtype),
        interpret=interpret,
    )(packed)


def per_device(
    tokens,
    validity,
    tile_counts,
    neighbours,
    mask_token,
    norm_gains,
    agent_qkv,
    agent_out,
    time_qkv,
    time_out,
    widen_weight,
    narrow_weight,
):
    model_width = tokens.shape[-1]
    head_count = HEADS
    head_dim = model_width // head_count
    moments = tokens.shape[2]
    slot_count = tokens.shape[3]
    score_scale = 1.0 / math.sqrt(head_dim)
    rows = tokens.reshape(moments, slot_count, model_width)
    live_rows = validity.reshape(moments, slot_count)
    masked_input = jnp.where(live_rows[..., None] == 1, rows, mask_token)
    normed = first_norm(masked_input, norm_gains)

    near = jnp.stack(halo(normed), axis=1)
    queries = project(normed, agent_qkv[:, :model_width]).astype(jnp.bfloat16)
    kv = project(near, agent_qkv[:, model_width:]).astype(jnp.bfloat16)
    column_index = lax.axis_index("gx")
    row_index = lax.axis_index("gy")
    padded_counts = jnp.pad(tile_counts, 1)
    near_counts = lax.dynamic_slice(padded_counts, (column_index, row_index), (3, 3))
    chosen = neighbours[0, 0].reshape(3, 3) == 1
    slot_ids = jnp.arange(slot_count, dtype=jnp.int32)
    key_live = ((slot_ids[None, None, :] < near_counts[:, :, None]) & chosen[:, :, None]).reshape(
        1, 9 * slot_count
    )
    mixed = agent_attention(key_live.astype(jnp.int32), queries, kv, head_dim)
    agent_proj = project(mixed, agent_out)
    after_agents = (masked_input.astype(jnp.float32) + agent_proj).astype(jnp.bfloat16)

    after_agents = lax.all_to_all(after_agents, "ta", 1, 0, tiled=True)
    steps = after_agents.shape[0]
    group = after_agents.shape[1]
    normed = layer_norm(after_agents, norm_gains[1])
    packed = project(normed, time_qkv).astype(jnp.bfloat16)
    time_mix = time_attention(packed.reshape(steps * group, 3 * model_width), group, head_dim)
    time_mix = time_mix.reshape(steps, group, model_width)
    after_time = (after_agents.astype(jnp.float32) + project(time_mix, time_out)).astype(
        jnp.bfloat16
    )
    normed = layer_norm(after_time, norm_gains[2])
    hidden = jnp.maximum(project(normed, widen_weight), 0.0).astype(jnp.bfloat16)
    out = (after_time.astype(jnp.float32) + project(hidden, narrow_weight)).astype(jnp.bfloat16)
    out = lax.all_to_all(out, "ta", 0, 1, tiled=True)
    return out.reshape(tokens.shape)


def solution(mesh):
    in_specs = (
        P("gx", "gy", "ta", None, None),
        P("gx", "gy", "ta", None),
        P(),
        P("gx", "gy", None),
        P(),
        P(),
        P(),
        P(),
        P(),
        P(),
        P(),
        P(),
    )
    out_specs = P("gx", "gy", "ta", None, None)
    return jax.shard_map(
        per_device, mesh=mesh, in_specs=in_specs, out_specs=out_specs, check_vma=False
    )
```

```python
import functools
import math

import jax
import jax.numpy as jnp
from jax import lax
from jax.experimental import pallas as pl
from jax.sharding import PartitionSpec as P

HEADS = 8


EPSILON = 1e-05
NEGATIVE = -1e30


def shift(piece, axis, step):
    count = lax.axis_size(axis)
    if step > 0:
        pairs = [(i, i + 1) for i in range(count - 1)]
    else:
        pairs = [(i + 1, i) for i in range(count - 1)]
    return lax.ppermute(piece, axis, pairs)


def halo(piece):
    west = shift(piece, "gx", 1)
    east = shift(piece, "gx", -1)
    south = shift(piece, "gy", 1)
    north = shift(piece, "gy", -1)
    north_east = shift(north, "gx", -1)
    south_west = shift(south, "gx", 1)
    south_east = shift(east, "gy", 1)
    north_west = shift(west, "gy", -1)
    near = [west, south, piece, north, east]
    corners = [south_west, north_west, south_east, north_east]
    return near, corners


HALO_ORDER = [(-1, 0), (0, -1), (0, 0), (0, 1), (1, 0), (-1, -1), (-1, 1), (1, -1), (1, 1)]


def layer_norm(values, gain_row):
    values = values.astype(jnp.float32)
    center = values - jnp.mean(values, axis=-1, keepdims=True)
    spread = jnp.mean(center * center, axis=-1, keepdims=True)
    return (center * lax.rsqrt(spread + EPSILON) * gain_row).astype(jnp.bfloat16)


def project(values, weight):
    return jnp.dot(values, weight, preferred_element_type=jnp.float32)


def agent_kernel(live_ref, q_ref, *refs, scale, head_dim):
    o_ref = refs[-1]
    groups = (len(refs) - 1) // 2
    live = live_ref[...] != 0
    queries = q_ref[0] * jnp.asarray(scale, q_ref.dtype)
    keys = []
    values = []
    for k_ref, v_ref in zip(refs[:groups], refs[groups:-1]):
        slots = k_ref.shape[1] * k_ref.shape[2]
        keys.append(k_ref[0].reshape(slots, k_ref.shape[3]))
        values.append(v_ref[0].reshape(slots, v_ref.shape[3]))
    rows = queries.shape[0]
    lane = lax.broadcasted_iota(jnp.int32, (1, queries.shape[1]), 1)
    first = lane < head_dim
    zero = jnp.zeros_like(queries)
    both = jnp.concatenate(
        [jnp.where(first, queries, zero), jnp.where(first, zero, queries)], axis=0
    )
    scores = jnp.concatenate(
        [
            lax.dot_general(
                both, key, (((1,), (1,)), ((), ())), preferred_element_type=jnp.float32
            )
            for key in keys
        ],
        axis=1,
    )
    scores = jnp.where(live, scores, NEGATIVE)
    row_max = jnp.max(scores, axis=-1, keepdims=True)
    weights = jnp.exp(scores - row_max)
    total = jnp.sum(weights, axis=-1, keepdims=True)
    weights = (weights * (1.0 / total)).astype(jnp.bfloat16)
    part = None
    start = 0
    for value in values:
        piece = jnp.dot(
            weights[:, start : start + value.shape[0]], value, preferred_element_type=jnp.float32
        )
        part = piece if part is None else part + piece
        start += value.shape[0]
    o_ref[0] = jnp.where(first, part[:rows], part[rows:]).astype(o_ref.dtype)


def agent_attention(live, queries, kv_groups, head_dim):
    moments, slot_count, model_width = queries.shape
    lanes = 2 * head_dim
    pairs = model_width // lanes
    body = functools.partial(agent_kernel, scale=1.0 / math.sqrt(head_dim), head_dim=head_dim)
    key_specs = [
        pl.BlockSpec((1, kv.shape[1], slot_count, lanes), lambda t, p: (t, 0, 0, p))
        for kv in kv_groups
    ]
    value_specs = [
        pl.BlockSpec((1, kv.shape[1], slot_count, lanes), lambda t, p: (t, 0, 0, p + pairs))
        for kv in kv_groups
    ]
    return pl.pallas_call(
        body,
        grid=(moments, pairs),
        in_specs=[
            pl.BlockSpec(live.shape, lambda t, p: (0, 0)),
            pl.BlockSpec((1, slot_count, lanes), lambda t, p: (t, 0, p)),
        ]
        + key_specs
        + value_specs,
        out_specs=pl.BlockSpec((1, slot_count, lanes), lambda t, p: (t, 0, p)),
        out_shape=jax.ShapeDtypeStruct(queries.shape, jnp.bfloat16),
    )(live, queries, *kv_groups, *kv_groups)

def norm_kernel(x_ref, gain_ref, o_ref, *, row):
    values = x_ref[...].astype(jnp.float32)
    center = values - jnp.mean(values, axis=-1, keepdims=True)
    spread = jnp.mean(center * center, axis=-1, keepdims=True)
    gain = gain_ref[row : row + 1, :]
    o_ref[...] = (center * lax.rsqrt(spread + EPSILON) * gain).astype(o_ref.dtype)


def first_norm(masked_input, norm_gains):
    return pl.pallas_call(
        functools.partial(norm_kernel, row=0),
        grid=(1,),
        in_specs=[
            pl.BlockSpec(masked_input.shape, lambda i: (0, 0, 0)),
            pl.BlockSpec(norm_gains.shape, lambda i: (0, 0)),
        ],
        out_specs=pl.BlockSpec(masked_input.shape, lambda i: (0, 0, 0)),
        out_shape=jax.ShapeDtypeStruct(masked_input.shape, jnp.bfloat16),
    )(masked_input, norm_gains)


def time_kernel(p_ref, o_ref, *, group, head_dim, scale):
    packed = p_ref[...]
    count = packed.shape[0]
    width = packed.shape[1] // 3
    lanes = 2 * head_dim
    row = lax.broadcasted_iota(jnp.int32, (count, count), 0) % group
    col = lax.broadcasted_iota(jnp.int32, (count, count), 1) % group
    same = row == col
    first = lax.broadcasted_iota(jnp.int32, (1, lanes), 1) < head_dim
    pieces = []
    for pair in range(width // lanes):
        start = pair * lanes
        queries = packed[:, start : start + lanes] * jnp.asarray(scale, packed.dtype)
        keys = packed[:, width + start : width + start + lanes]
        values = packed[:, 2 * width + start : 2 * width + start + lanes]
        zero = jnp.zeros_like(queries)
        halves = []
        for own in (jnp.where(first, queries, zero), jnp.where(first, zero, queries)):
            scores = lax.dot_general(
                own, keys, (((1,), (1,)), ((), ())), preferred_element_type=jnp.float32
            )
            scores = jnp.where(same, scores, NEGATIVE)
            row_max = jnp.max(scores, axis=-1, keepdims=True)
            weights = jnp.exp(scores - row_max)
            weights = weights / jnp.sum(weights, axis=-1, keepdims=True)
            high = weights.astype(jnp.bfloat16)
            low = (weights - high.astype(jnp.float32)).astype(jnp.bfloat16)
            halves.append(
                jnp.dot(high, values, preferred_element_type=jnp.float32)
                + jnp.dot(low, values, preferred_element_type=jnp.float32)
            )
        pieces.append(jnp.where(first, halves[0], halves[1]))
    o_ref[...] = jnp.concatenate(pieces, axis=1).astype(o_ref.dtype)


def time_attention(packed, group, head_dim, interpret=False):
    count, width3 = packed.shape
    body = functools.partial(
        time_kernel, group=group, head_dim=head_dim, scale=1.0 / math.sqrt(head_dim)
    )
    return pl.pallas_call(
        body,
        grid=(1,),
        in_specs=[pl.BlockSpec((count, width3), lambda i: (0, 0))],
        out_specs=pl.BlockSpec((count, width3 // 3), lambda i: (0, 0)),
        out_shape=jax.ShapeDtypeStruct((count, width3 // 3), packed.dtype),
        interpret=interpret,
    )(packed)


def per_device(
    tokens,
    validity,
    tile_counts,
    neighbours,
    mask_token,
    norm_gains,
    agent_qkv,
    agent_out,
    time_qkv,
    time_out,
    widen_weight,
    narrow_weight,
):
    model_width = tokens.shape[-1]
    head_count = HEADS
    head_dim = model_width // head_count
    moments = tokens.shape[2]
    slot_count = tokens.shape[3]
    score_scale = 1.0 / math.sqrt(head_dim)
    rows = tokens.reshape(moments, slot_count, model_width)
    live_rows = validity.reshape(moments, slot_count)
    masked_input = jnp.where(live_rows[..., None] == 1, rows, mask_token)
    normed = first_norm(masked_input, norm_gains)

    near, corners = halo(normed)
    queries = project(normed, agent_qkv[:, :model_width]).astype(jnp.bfloat16)
    kv_groups = [
        project(jnp.stack(group, axis=1), agent_qkv[:, model_width:]).astype(jnp.bfloat16)
        for group in (near, corners)
    ]
    column_index = lax.axis_index("gx")
    row_index = lax.axis_index("gy")
    padded_counts = jnp.pad(tile_counts, 1)
    near_counts = lax.dynamic_slice(padded_counts, (column_index, row_index), (3, 3))
    chosen = neighbours[0, 0].reshape(3, 3) == 1
    slot_ids = jnp.arange(slot_count, dtype=jnp.int32)
    key_live = (slot_ids[None, None, :] < near_counts[:, :, None]) & chosen[:, :, None]
    key_live = jnp.stack([key_live[dx + 1, dy + 1] for dx, dy in HALO_ORDER])
    key_live = key_live.reshape(1, 9 * slot_count)
    mixed = agent_attention(key_live.astype(jnp.int32), queries, kv_groups, head_dim)
    agent_proj = project(mixed, agent_out)
    after_agents = (masked_input.astype(jnp.float32) + agent_proj).astype(jnp.bfloat16)

    after_agents = lax.all_to_all(after_agents, "ta", 1, 0, tiled=True)
    steps = after_agents.shape[0]
    group = after_agents.shape[1]
    normed = layer_norm(after_agents, norm_gains[1])
    packed = project(normed, time_qkv).astype(jnp.bfloat16)
    time_mix = time_attention(packed.reshape(steps * group, 3 * model_width), group, head_dim)
    time_mix = time_mix.reshape(steps, group, model_width)
    after_time = (after_agents.astype(jnp.float32) + project(time_mix, time_out)).astype(
        jnp.bfloat16
    )
    normed = layer_norm(after_time, norm_gains[2])
    hidden = jnp.maximum(project(normed, widen_weight), 0.0).astype(jnp.bfloat16)
    out = (after_time.astype(jnp.float32) + project(hidden, narrow_weight)).astype(jnp.bfloat16)
    out = lax.all_to_all(out, "ta", 0, 1, tiled=True)
    return out.reshape(tokens.shape)


def solution(mesh):
    in_specs = (
        P("gx", "gy", "ta", None, None),
        P("gx", "gy", "ta", None),
        P(),
        P("gx", "gy", None),
        P(),
        P(),
        P(),
        P(),
        P(),
        P(),
        P(),
        P(),
    )
    out_specs = P("gx", "gy", "ta", None, None)
    return jax.shard_map(
        per_device, mesh=mesh, in_specs=in_specs, out_specs=out_specs, check_vma=False
    )
```

```python
import functools
import math

import jax
import jax.numpy as jnp
from jax import lax
from jax.experimental import pallas as pl
from jax.sharding import PartitionSpec as P

HEADS = 8


EPSILON = 1e-05
NEGATIVE = -1e30


def shift(piece, axis, step):
    count = lax.axis_size(axis)
    if step > 0:
        pairs = [(i, i + 1) for i in range(count - 1)]
    else:
        pairs = [(i + 1, i) for i in range(count - 1)]
    return lax.ppermute(piece, axis, pairs)


def halo(piece):
    west = shift(piece, "gx", 1)
    east = shift(piece, "gx", -1)
    south = shift(piece, "gy", 1)
    north = shift(piece, "gy", -1)
    north_east = shift(north, "gx", -1)
    south_west = shift(south, "gx", 1)
    south_east = shift(east, "gy", 1)
    north_west = shift(west, "gy", -1)
    near = [west, south, piece, north, east]
    corners = [south_west, north_west, south_east, north_east]
    return near, corners


HALO_ORDER = [(-1, 0), (0, -1), (0, 0), (0, 1), (1, 0), (-1, -1), (-1, 1), (1, -1), (1, 1)]


def layer_norm(values, gain_row):
    values = values.astype(jnp.float32)
    center = values - jnp.mean(values, axis=-1, keepdims=True)
    spread = jnp.mean(center * center, axis=-1, keepdims=True)
    return (center * lax.rsqrt(spread + EPSILON) * gain_row).astype(jnp.bfloat16)


def project(values, weight):
    return jnp.dot(values, weight, preferred_element_type=jnp.float32)


def agent_kernel(live_ref, q_ref, *refs, scale, head_dim):
    o_ref = refs[-1]
    groups = (len(refs) - 1) // 2
    live = live_ref[...] != 0
    queries = q_ref[0] * jnp.asarray(scale, q_ref.dtype)
    keys = []
    values = []
    for k_ref, v_ref in zip(refs[:groups], refs[groups:-1]):
        slots = k_ref.shape[1] * k_ref.shape[2]
        keys.append(k_ref[0].reshape(slots, k_ref.shape[3]))
        values.append(v_ref[0].reshape(slots, v_ref.shape[3]))
    rows = queries.shape[0]
    lane = lax.broadcasted_iota(jnp.int32, (1, queries.shape[1]), 1)
    first = lane < head_dim
    zero = jnp.zeros_like(queries)
    both = jnp.concatenate(
        [jnp.where(first, queries, zero), jnp.where(first, zero, queries)], axis=0
    )
    scores = jnp.concatenate(
        [
            lax.dot_general(
                both, key, (((1,), (1,)), ((), ())), preferred_element_type=jnp.float32
            )
            for key in keys
        ],
        axis=1,
    )
    scores = jnp.where(live, scores, NEGATIVE)
    row_max = jnp.max(scores, axis=-1, keepdims=True)
    weights = jnp.exp(scores - row_max)
    total = jnp.sum(weights, axis=-1, keepdims=True)
    weights = (weights * (1.0 / total)).astype(jnp.bfloat16)
    part = None
    start = 0
    for value in values:
        piece = jnp.dot(
            weights[:, start : start + value.shape[0]], value, preferred_element_type=jnp.float32
        )
        part = piece if part is None else part + piece
        start += value.shape[0]
    o_ref[0] = jnp.where(first, part[:rows], part[rows:]).astype(o_ref.dtype)


def agent_attention(live, queries, kv_groups, head_dim):
    moments, slot_count, model_width = queries.shape
    lanes = 2 * head_dim
    pairs = model_width // lanes
    body = functools.partial(agent_kernel, scale=1.0 / math.sqrt(head_dim), head_dim=head_dim)
    key_specs = [
        pl.BlockSpec((1, kv.shape[1], slot_count, lanes), lambda t, p: (t, 0, 0, p))
        for kv in kv_groups
    ]
    value_specs = [
        pl.BlockSpec((1, kv.shape[1], slot_count, lanes), lambda t, p: (t, 0, 0, p + pairs))
        for kv in kv_groups
    ]
    return pl.pallas_call(
        body,
        grid=(moments, pairs),
        in_specs=[
            pl.BlockSpec(live.shape, lambda t, p: (0, 0)),
            pl.BlockSpec((1, slot_count, lanes), lambda t, p: (t, 0, p)),
        ]
        + key_specs
        + value_specs,
        out_specs=pl.BlockSpec((1, slot_count, lanes), lambda t, p: (t, 0, p)),
        out_shape=jax.ShapeDtypeStruct(queries.shape, jnp.bfloat16),
    )(live, queries, *kv_groups, *kv_groups)

def norm_kernel(x_ref, gain_ref, o_ref, *, row):
    values = x_ref[...].astype(jnp.float32)
    center = values - jnp.mean(values, axis=-1, keepdims=True)
    spread = jnp.mean(center * center, axis=-1, keepdims=True)
    gain = gain_ref[row : row + 1, :]
    o_ref[...] = (center * lax.rsqrt(spread + EPSILON) * gain).astype(o_ref.dtype)


def first_norm(masked_input, norm_gains):
    return pl.pallas_call(
        functools.partial(norm_kernel, row=0),
        grid=(1,),
        in_specs=[
            pl.BlockSpec(masked_input.shape, lambda i: (0, 0, 0)),
            pl.BlockSpec(norm_gains.shape, lambda i: (0, 0)),
        ],
        out_specs=pl.BlockSpec(masked_input.shape, lambda i: (0, 0, 0)),
        out_shape=jax.ShapeDtypeStruct(masked_input.shape, jnp.bfloat16),
    )(masked_input, norm_gains)


def time_kernel(p_ref, o_ref, *, head_dim, scale):
    slots, steps, width3 = p_ref.shape
    packed = p_ref[...].reshape(slots * steps, width3)
    count = packed.shape[0]
    width = width3 // 3
    lanes = 2 * head_dim
    row = lax.broadcasted_iota(jnp.int32, (count, count), 0) // steps
    col = lax.broadcasted_iota(jnp.int32, (count, count), 1) // steps
    same = row == col
    first = lax.broadcasted_iota(jnp.int32, (1, lanes), 1) < head_dim
    pieces = []
    for pair in range(width // lanes):
        start = pair * lanes
        queries = packed[:, start : start + lanes] * jnp.asarray(scale, packed.dtype)
        keys = packed[:, width + start : width + start + lanes]
        values = packed[:, 2 * width + start : 2 * width + start + lanes]
        zero = jnp.zeros_like(queries)
        halves = []
        for own in (jnp.where(first, queries, zero), jnp.where(first, zero, queries)):
            scores = lax.dot_general(
                own, keys, (((1,), (1,)), ((), ())), preferred_element_type=jnp.float32
            )
            scores = jnp.where(same, scores, NEGATIVE)
            row_max = jnp.max(scores, axis=-1, keepdims=True)
            weights = jnp.exp(scores - row_max)
            weights = weights / jnp.sum(weights, axis=-1, keepdims=True)
            high = weights.astype(jnp.bfloat16)
            low = (weights - high.astype(jnp.float32)).astype(jnp.bfloat16)
            halves.append(
                jnp.dot(high, values, preferred_element_type=jnp.float32)
                + jnp.dot(low, values, preferred_element_type=jnp.float32)
            )
        pieces.append(jnp.where(first, halves[0], halves[1]))
    mixed = jnp.concatenate(pieces, axis=1)
    o_ref[...] = mixed.reshape(slots, steps, width).astype(o_ref.dtype)


def time_attention(packed, head_dim, block=4, interpret=False):
    slots, steps, width3 = packed.shape
    block = math.gcd(block, slots)
    body = functools.partial(time_kernel, head_dim=head_dim, scale=1.0 / math.sqrt(head_dim))
    return pl.pallas_call(
        body,
        grid=(slots // block,),
        in_specs=[pl.BlockSpec((block, steps, width3), lambda i: (i, 0, 0))],
        out_specs=pl.BlockSpec((block, steps, width3 // 3), lambda i: (i, 0, 0)),
        out_shape=jax.ShapeDtypeStruct((slots, steps, width3 // 3), packed.dtype),
        interpret=interpret,
    )(packed)

def per_device(
    tokens,
    validity,
    tile_counts,
    neighbours,
    mask_token,
    norm_gains,
    agent_qkv,
    agent_out,
    time_qkv,
    time_out,
    widen_weight,
    narrow_weight,
):
    model_width = tokens.shape[-1]
    head_count = HEADS
    head_dim = model_width // head_count
    moments = tokens.shape[2]
    slot_count = tokens.shape[3]
    score_scale = 1.0 / math.sqrt(head_dim)
    rows = tokens.reshape(moments, slot_count, model_width)
    live_rows = validity.reshape(moments, slot_count)
    masked_input = jnp.where(live_rows[..., None] == 1, rows, mask_token)
    normed = first_norm(masked_input, norm_gains)

    near, corners = halo(normed)
    queries = project(normed, agent_qkv[:, :model_width]).astype(jnp.bfloat16)
    kv_groups = [
        project(jnp.stack(group, axis=1), agent_qkv[:, model_width:]).astype(jnp.bfloat16)
        for group in (near, corners)
    ]
    column_index = lax.axis_index("gx")
    row_index = lax.axis_index("gy")
    padded_counts = jnp.pad(tile_counts, 1)
    near_counts = lax.dynamic_slice(padded_counts, (column_index, row_index), (3, 3))
    chosen = neighbours[0, 0].reshape(3, 3) == 1
    slot_ids = jnp.arange(slot_count, dtype=jnp.int32)
    key_live = (slot_ids[None, None, :] < near_counts[:, :, None]) & chosen[:, :, None]
    key_live = jnp.stack([key_live[dx + 1, dy + 1] for dx, dy in HALO_ORDER])
    key_live = key_live.reshape(1, 9 * slot_count)
    mixed = agent_attention(key_live.astype(jnp.int32), queries, kv_groups, head_dim)
    agent_proj = project(mixed, agent_out)
    after_agents = (masked_input.astype(jnp.float32) + agent_proj).astype(jnp.bfloat16)

    after_agents = lax.all_to_all(after_agents, "ta", 1, 0, tiled=True)
    steps = after_agents.shape[0]
    group = after_agents.shape[1]
    normed = layer_norm(after_agents, norm_gains[1])
    packed = jnp.einsum(
        "tsc,cf->stf", normed, time_qkv, preferred_element_type=jnp.float32
    ).astype(jnp.bfloat16)
    time_mix = time_attention(packed, head_dim)
    time_proj = jnp.einsum("stf,fc->tsc", time_mix, time_out, preferred_element_type=jnp.float32)
    after_time = (after_agents.astype(jnp.float32) + time_proj).astype(jnp.bfloat16)
    normed = layer_norm(after_time, norm_gains[2])
    hidden = jnp.maximum(project(normed, widen_weight), 0.0).astype(jnp.bfloat16)
    out = (after_time.astype(jnp.float32) + project(hidden, narrow_weight)).astype(jnp.bfloat16)
    out = lax.all_to_all(out, "ta", 0, 1, tiled=True)
    return out.reshape(tokens.shape)


def solution(mesh):
    in_specs = (
        P("gx", "gy", "ta", None, None),
        P("gx", "gy", "ta", None),
        P(),
        P("gx", "gy", None),
        P(),
        P(),
        P(),
        P(),
        P(),
        P(),
        P(),
        P(),
    )
    out_specs = P("gx", "gy", "ta", None, None)
    return jax.shard_map(
        per_device, mesh=mesh, in_specs=in_specs, out_specs=out_specs, check_vma=False
    )
```

```python
import functools
import math

import jax
import jax.numpy as jnp
from jax import lax
from jax.experimental import pallas as pl
from jax.sharding import PartitionSpec as P

HEADS = 8


EPSILON = 1e-05
NEGATIVE = -1e30


def shift(piece, axis, step):
    count = lax.axis_size(axis)
    if step > 0:
        pairs = [(i, i + 1) for i in range(count - 1)]
    else:
        pairs = [(i + 1, i) for i in range(count - 1)]
    return lax.ppermute(piece, axis, pairs)


def halo(piece):
    west = shift(piece, "gx", 1)
    east = shift(piece, "gx", -1)
    south = shift(piece, "gy", 1)
    north = shift(piece, "gy", -1)
    north_east = shift(north, "gx", -1)
    south_west = shift(south, "gx", 1)
    south_east = shift(east, "gy", 1)
    north_west = shift(west, "gy", -1)
    near = [west, south, piece, north, east]
    corners = [south_west, north_west, south_east, north_east]
    return near, corners


HALO_ORDER = [(-1, 0), (0, -1), (0, 0), (0, 1), (1, 0), (-1, -1), (-1, 1), (1, -1), (1, 1)]


def layer_norm(values, gain_row):
    values = values.astype(jnp.float32)
    center = values - jnp.mean(values, axis=-1, keepdims=True)
    spread = jnp.mean(center * center, axis=-1, keepdims=True)
    return (center * lax.rsqrt(spread + EPSILON) * gain_row).astype(jnp.bfloat16)


def project(values, weight):
    return jnp.dot(values, weight, preferred_element_type=jnp.float32)


def agent_kernel(live_ref, q_ref, *refs, scale, head_dim):
    o_ref = refs[-1]
    groups = (len(refs) - 1) // 2
    live = live_ref[...] != 0
    for moment in range(q_ref.shape[0]):
        queries = q_ref[moment] * jnp.asarray(scale, q_ref.dtype)
        keys = []
        values = []
        for k_ref, v_ref in zip(refs[:groups], refs[groups:-1]):
            slots = k_ref.shape[1] * k_ref.shape[2]
            keys.append(k_ref[moment].reshape(slots, k_ref.shape[3]))
            values.append(v_ref[moment].reshape(slots, v_ref.shape[3]))
        rows = queries.shape[0]
        lane = lax.broadcasted_iota(jnp.int32, (1, queries.shape[1]), 1)
        first = lane < head_dim
        zero = jnp.zeros_like(queries)
        both = jnp.concatenate(
            [jnp.where(first, queries, zero), jnp.where(first, zero, queries)], axis=0
        )
        scores = jnp.concatenate(
            [
                lax.dot_general(
                    both, key, (((1,), (1,)), ((), ())), preferred_element_type=jnp.float32
                )
                for key in keys
            ],
            axis=1,
        )
        scores = jnp.where(live, scores, NEGATIVE)
        row_max = jnp.max(scores, axis=-1, keepdims=True)
        weights = jnp.exp(scores - row_max)
        total = jnp.sum(weights, axis=-1, keepdims=True)
        weights = (weights * (1.0 / total)).astype(jnp.bfloat16)
        part = None
        start = 0
        for value in values:
            piece = jnp.dot(
                weights[:, start : start + value.shape[0]],
                value,
                preferred_element_type=jnp.float32,
            )
            part = piece if part is None else part + piece
            start += value.shape[0]
        o_ref[moment] = jnp.where(first, part[:rows], part[rows:]).astype(o_ref.dtype)


def agent_attention(live, queries, kv_groups, head_dim):
    moments, slot_count, model_width = queries.shape
    lanes = 2 * head_dim
    pairs = model_width // lanes
    body = functools.partial(agent_kernel, scale=1.0 / math.sqrt(head_dim), head_dim=head_dim)
    key_specs = [
        pl.BlockSpec((moments, kv.shape[1], slot_count, lanes), lambda p: (0, 0, 0, p))
        for kv in kv_groups
    ]
    value_specs = [
        pl.BlockSpec((moments, kv.shape[1], slot_count, lanes), lambda p: (0, 0, 0, p + pairs))
        for kv in kv_groups
    ]
    return pl.pallas_call(
        body,
        grid=(pairs,),
        in_specs=[
            pl.BlockSpec(live.shape, lambda p: (0, 0)),
            pl.BlockSpec((moments, slot_count, lanes), lambda p: (0, 0, p)),
        ]
        + key_specs
        + value_specs,
        out_specs=pl.BlockSpec((moments, slot_count, lanes), lambda p: (0, 0, p)),
        out_shape=jax.ShapeDtypeStruct(queries.shape, jnp.bfloat16),
    )(live, queries, *kv_groups, *kv_groups)

def norm_kernel(x_ref, gain_ref, o_ref, *, row):
    values = x_ref[...].astype(jnp.float32)
    center = values - jnp.mean(values, axis=-1, keepdims=True)
    spread = jnp.mean(center * center, axis=-1, keepdims=True)
    gain = gain_ref[row : row + 1, :]
    o_ref[...] = (center * lax.rsqrt(spread + EPSILON) * gain).astype(o_ref.dtype)


def first_norm(masked_input, norm_gains):
    return pl.pallas_call(
        functools.partial(norm_kernel, row=0),
        grid=(1,),
        in_specs=[
            pl.BlockSpec(masked_input.shape, lambda i: (0, 0, 0)),
            pl.BlockSpec(norm_gains.shape, lambda i: (0, 0)),
        ],
        out_specs=pl.BlockSpec(masked_input.shape, lambda i: (0, 0, 0)),
        out_shape=jax.ShapeDtypeStruct(masked_input.shape, jnp.bfloat16),
    )(masked_input, norm_gains)


def time_kernel(p_ref, o_ref, *, group, head_dim, scale):
    packed = p_ref[...]
    count = packed.shape[0]
    width = packed.shape[1] // 3
    lanes = 2 * head_dim
    row = lax.broadcasted_iota(jnp.int32, (count, count), 0) % group
    col = lax.broadcasted_iota(jnp.int32, (count, count), 1) % group
    same = row == col
    first = lax.broadcasted_iota(jnp.int32, (1, lanes), 1) < head_dim
    pieces = []
    for pair in range(width // lanes):
        start = pair * lanes
        queries = packed[:, start : start + lanes] * jnp.asarray(scale, packed.dtype)
        keys = packed[:, width + start : width + start + lanes]
        values = packed[:, 2 * width + start : 2 * width + start + lanes]
        zero = jnp.zeros_like(queries)
        halves = []
        for own in (jnp.where(first, queries, zero), jnp.where(first, zero, queries)):
            scores = lax.dot_general(
                own, keys, (((1,), (1,)), ((), ())), preferred_element_type=jnp.float32
            )
            scores = jnp.where(same, scores, NEGATIVE)
            row_max = jnp.max(scores, axis=-1, keepdims=True)
            weights = jnp.exp(scores - row_max)
            weights = weights / jnp.sum(weights, axis=-1, keepdims=True)
            high = weights.astype(jnp.bfloat16)
            low = (weights - high.astype(jnp.float32)).astype(jnp.bfloat16)
            halves.append(
                jnp.dot(high, values, preferred_element_type=jnp.float32)
                + jnp.dot(low, values, preferred_element_type=jnp.float32)
            )
        pieces.append(jnp.where(first, halves[0], halves[1]))
    o_ref[...] = jnp.concatenate(pieces, axis=1).astype(o_ref.dtype)


def time_attention(packed, group, head_dim, interpret=False):
    count, width3 = packed.shape
    body = functools.partial(
        time_kernel, group=group, head_dim=head_dim, scale=1.0 / math.sqrt(head_dim)
    )
    return pl.pallas_call(
        body,
        grid=(1,),
        in_specs=[pl.BlockSpec((count, width3), lambda i: (0, 0))],
        out_specs=pl.BlockSpec((count, width3 // 3), lambda i: (0, 0)),
        out_shape=jax.ShapeDtypeStruct((count, width3 // 3), packed.dtype),
        interpret=interpret,
    )(packed)


def per_device(
    tokens,
    validity,
    tile_counts,
    neighbours,
    mask_token,
    norm_gains,
    agent_qkv,
    agent_out,
    time_qkv,
    time_out,
    widen_weight,
    narrow_weight,
):
    model_width = tokens.shape[-1]
    head_count = HEADS
    head_dim = model_width // head_count
    moments = tokens.shape[2]
    slot_count = tokens.shape[3]
    score_scale = 1.0 / math.sqrt(head_dim)
    rows = tokens.reshape(moments, slot_count, model_width)
    live_rows = validity.reshape(moments, slot_count)
    masked_input = jnp.where(live_rows[..., None] == 1, rows, mask_token)
    normed = first_norm(masked_input, norm_gains)

    near, corners = halo(normed)
    queries = project(normed, agent_qkv[:, :model_width]).astype(jnp.bfloat16)
    kv_groups = [
        project(jnp.stack(group, axis=1), agent_qkv[:, model_width:]).astype(jnp.bfloat16)
        for group in (near, corners)
    ]
    column_index = lax.axis_index("gx")
    row_index = lax.axis_index("gy")
    padded_counts = jnp.pad(tile_counts, 1)
    near_counts = lax.dynamic_slice(padded_counts, (column_index, row_index), (3, 3))
    chosen = neighbours[0, 0].reshape(3, 3) == 1
    slot_ids = jnp.arange(slot_count, dtype=jnp.int32)
    key_live = (slot_ids[None, None, :] < near_counts[:, :, None]) & chosen[:, :, None]
    key_live = jnp.stack([key_live[dx + 1, dy + 1] for dx, dy in HALO_ORDER])
    key_live = key_live.reshape(1, 9 * slot_count)
    mixed = agent_attention(key_live.astype(jnp.int32), queries, kv_groups, head_dim)
    agent_proj = project(mixed, agent_out)
    after_agents = (masked_input.astype(jnp.float32) + agent_proj).astype(jnp.bfloat16)

    after_agents = lax.all_to_all(after_agents, "ta", 1, 0, tiled=True)
    steps = after_agents.shape[0]
    group = after_agents.shape[1]
    normed = layer_norm(after_agents, norm_gains[1])
    packed = project(normed, time_qkv).astype(jnp.bfloat16)
    time_mix = time_attention(packed.reshape(steps * group, 3 * model_width), group, head_dim)
    time_mix = time_mix.reshape(steps, group, model_width)
    after_time = (after_agents.astype(jnp.float32) + project(time_mix, time_out)).astype(
        jnp.bfloat16
    )
    normed = layer_norm(after_time, norm_gains[2])
    hidden = jnp.maximum(project(normed, widen_weight), 0.0).astype(jnp.bfloat16)
    out = (after_time.astype(jnp.float32) + project(hidden, narrow_weight)).astype(jnp.bfloat16)
    out = lax.all_to_all(out, "ta", 0, 1, tiled=True)
    return out.reshape(tokens.shape)


def solution(mesh):
    in_specs = (
        P("gx", "gy", "ta", None, None),
        P("gx", "gy", "ta", None),
        P(),
        P("gx", "gy", None),
        P(),
        P(),
        P(),
        P(),
        P(),
        P(),
        P(),
        P(),
    )
    out_specs = P("gx", "gy", "ta", None, None)
    return jax.shard_map(
        per_device, mesh=mesh, in_specs=in_specs, out_specs=out_specs, check_vma=False
    )
```

```python
import functools
import math

import jax
import jax.numpy as jnp
from jax import lax
from jax.experimental import pallas as pl
from jax.experimental.pallas import tpu as pltpu
from jax.sharding import PartitionSpec as P

HEADS = 8


EPSILON = 1e-05
NEGATIVE = -1e30


def shift(piece, axis, step):
    count = lax.axis_size(axis)
    if step > 0:
        pairs = [(i, i + 1) for i in range(count - 1)]
    else:
        pairs = [(i + 1, i) for i in range(count - 1)]
    return lax.ppermute(piece, axis, pairs)


def halo(piece):
    west = shift(piece, "gx", 1)
    east = shift(piece, "gx", -1)
    south = shift(piece, "gy", 1)
    north = shift(piece, "gy", -1)
    north_east = shift(north, "gx", -1)
    south_west = shift(south, "gx", 1)
    south_east = shift(east, "gy", 1)
    north_west = shift(west, "gy", -1)
    near = [west, south, piece, north, east]
    corners = [south_west, north_west, south_east, north_east]
    return near, corners


HALO_ORDER = [(-1, 0), (0, -1), (0, 0), (0, 1), (1, 0), (-1, -1), (-1, 1), (1, -1), (1, 1)]


def layer_norm(values, gain_row):
    values = values.astype(jnp.float32)
    center = values - jnp.mean(values, axis=-1, keepdims=True)
    spread = jnp.mean(center * center, axis=-1, keepdims=True)
    return (center * lax.rsqrt(spread + EPSILON) * gain_row).astype(jnp.bfloat16)


def project(values, weight):
    return jnp.dot(values, weight, preferred_element_type=jnp.float32)


def agent_kernel(live_ref, q_ref, wo_ref, x_ref, *refs, scale, head_dim):
    o_ref = refs[-2]
    acc_ref = refs[-1]
    pair = pl.program_id(0)
    groups = (len(refs) - 2) // 2
    live = live_ref[...] != 0
    for moment in range(q_ref.shape[0]):
        queries = q_ref[moment] * jnp.asarray(scale, q_ref.dtype)
        keys = []
        values = []
        for k_ref, v_ref in zip(refs[:groups], refs[groups : 2 * groups]):
            slots = k_ref.shape[1] * k_ref.shape[2]
            keys.append(k_ref[moment].reshape(slots, k_ref.shape[3]))
            values.append(v_ref[moment].reshape(slots, v_ref.shape[3]))
        rows = queries.shape[0]
        lane = lax.broadcasted_iota(jnp.int32, (1, queries.shape[1]), 1)
        first = lane < head_dim
        zero = jnp.zeros_like(queries)
        both = jnp.concatenate(
            [jnp.where(first, queries, zero), jnp.where(first, zero, queries)], axis=0
        )
        scores = jnp.concatenate(
            [
                lax.dot_general(
                    both, key, (((1,), (1,)), ((), ())), preferred_element_type=jnp.float32
                )
                for key in keys
            ],
            axis=1,
        )
        scores = jnp.where(live, scores, NEGATIVE)
        row_max = jnp.max(scores, axis=-1, keepdims=True)
        weights = jnp.exp(scores - row_max)
        total = jnp.sum(weights, axis=-1, keepdims=True)
        weights = (weights * (1.0 / total)).astype(jnp.bfloat16)
        part = None
        start = 0
        for value in values:
            piece = jnp.dot(
                weights[:, start : start + value.shape[0]],
                value,
                preferred_element_type=jnp.float32,
            )
            part = piece if part is None else part + piece
            start += value.shape[0]
        mixed = jnp.where(first, part[:rows], part[rows:]).astype(jnp.bfloat16)
        contribution = jnp.dot(mixed, wo_ref[...], preferred_element_type=jnp.float32)

        @pl.when(pair == 0)
        def _():
            acc_ref[moment] = contribution

        @pl.when(pair > 0)
        def _():
            acc_ref[moment] += contribution

    @pl.when(pair == pl.num_programs(0) - 1)
    def _():
        o_ref[...] = (x_ref[...].astype(jnp.float32) + acc_ref[...]).astype(o_ref.dtype)


def agent_attention(live, queries, kv_groups, agent_out, masked_input, head_dim):
    moments, slot_count, model_width = queries.shape
    lanes = 2 * head_dim
    pairs = model_width // lanes
    body = functools.partial(agent_kernel, scale=1.0 / math.sqrt(head_dim), head_dim=head_dim)
    key_specs = [
        pl.BlockSpec((moments, kv.shape[1], slot_count, lanes), lambda p: (0, 0, 0, p))
        for kv in kv_groups
    ]
    value_specs = [
        pl.BlockSpec((moments, kv.shape[1], slot_count, lanes), lambda p: (0, 0, 0, p + pairs))
        for kv in kv_groups
    ]
    return pl.pallas_call(
        body,
        grid=(pairs,),
        in_specs=[
            pl.BlockSpec(live.shape, lambda p: (0, 0)),
            pl.BlockSpec((moments, slot_count, lanes), lambda p: (0, 0, p)),
            pl.BlockSpec((lanes, model_width), lambda p: (p, 0)),
            pl.BlockSpec(masked_input.shape, lambda p: (0, 0, 0)),
        ]
        + key_specs
        + value_specs,
        out_specs=pl.BlockSpec(masked_input.shape, lambda p: (0, 0, 0)),
        out_shape=jax.ShapeDtypeStruct(queries.shape, jnp.bfloat16),
        scratch_shapes=[pltpu.VMEM(masked_input.shape, jnp.float32)],
        compiler_params=pltpu.CompilerParams(dimension_semantics=("arbitrary",)),
    )(live, queries, agent_out, masked_input, *kv_groups, *kv_groups)

def norm_kernel(x_ref, gain_ref, o_ref, *, row):
    values = x_ref[...].astype(jnp.float32)
    center = values - jnp.mean(values, axis=-1, keepdims=True)
    spread = jnp.mean(center * center, axis=-1, keepdims=True)
    gain = gain_ref[row : row + 1, :]
    o_ref[...] = (center * lax.rsqrt(spread + EPSILON) * gain).astype(o_ref.dtype)


def first_norm(masked_input, norm_gains):
    return pl.pallas_call(
        functools.partial(norm_kernel, row=0),
        grid=(1,),
        in_specs=[
            pl.BlockSpec(masked_input.shape, lambda i: (0, 0, 0)),
            pl.BlockSpec(norm_gains.shape, lambda i: (0, 0)),
        ],
        out_specs=pl.BlockSpec(masked_input.shape, lambda i: (0, 0, 0)),
        out_shape=jax.ShapeDtypeStruct(masked_input.shape, jnp.bfloat16),
    )(masked_input, norm_gains)


def time_kernel(p_ref, o_ref, *, group, head_dim, scale):
    packed = p_ref[...]
    count = packed.shape[0]
    width = packed.shape[1] // 3
    lanes = 2 * head_dim
    row = lax.broadcasted_iota(jnp.int32, (count, count), 0) % group
    col = lax.broadcasted_iota(jnp.int32, (count, count), 1) % group
    same = row == col
    first = lax.broadcasted_iota(jnp.int32, (1, lanes), 1) < head_dim
    pieces = []
    for pair in range(width // lanes):
        start = pair * lanes
        queries = packed[:, start : start + lanes] * jnp.asarray(scale, packed.dtype)
        keys = packed[:, width + start : width + start + lanes]
        values = packed[:, 2 * width + start : 2 * width + start + lanes]
        zero = jnp.zeros_like(queries)
        halves = []
        for own in (jnp.where(first, queries, zero), jnp.where(first, zero, queries)):
            scores = lax.dot_general(
                own, keys, (((1,), (1,)), ((), ())), preferred_element_type=jnp.float32
            )
            scores = jnp.where(same, scores, NEGATIVE)
            row_max = jnp.max(scores, axis=-1, keepdims=True)
            weights = jnp.exp(scores - row_max)
            weights = weights / jnp.sum(weights, axis=-1, keepdims=True)
            high = weights.astype(jnp.bfloat16)
            low = (weights - high.astype(jnp.float32)).astype(jnp.bfloat16)
            halves.append(
                jnp.dot(high, values, preferred_element_type=jnp.float32)
                + jnp.dot(low, values, preferred_element_type=jnp.float32)
            )
        pieces.append(jnp.where(first, halves[0], halves[1]))
    o_ref[...] = jnp.concatenate(pieces, axis=1).astype(o_ref.dtype)


def time_attention(packed, group, head_dim, interpret=False):
    count, width3 = packed.shape
    body = functools.partial(
        time_kernel, group=group, head_dim=head_dim, scale=1.0 / math.sqrt(head_dim)
    )
    return pl.pallas_call(
        body,
        grid=(1,),
        in_specs=[pl.BlockSpec((count, width3), lambda i: (0, 0))],
        out_specs=pl.BlockSpec((count, width3 // 3), lambda i: (0, 0)),
        out_shape=jax.ShapeDtypeStruct((count, width3 // 3), packed.dtype),
        interpret=interpret,
    )(packed)


def per_device(
    tokens,
    validity,
    tile_counts,
    neighbours,
    mask_token,
    norm_gains,
    agent_qkv,
    agent_out,
    time_qkv,
    time_out,
    widen_weight,
    narrow_weight,
):
    model_width = tokens.shape[-1]
    head_count = HEADS
    head_dim = model_width // head_count
    moments = tokens.shape[2]
    slot_count = tokens.shape[3]
    score_scale = 1.0 / math.sqrt(head_dim)
    rows = tokens.reshape(moments, slot_count, model_width)
    live_rows = validity.reshape(moments, slot_count)
    masked_input = jnp.where(live_rows[..., None] == 1, rows, mask_token)
    normed = first_norm(masked_input, norm_gains)

    near, corners = halo(normed)
    queries = project(normed, agent_qkv[:, :model_width]).astype(jnp.bfloat16)
    kv_groups = [
        project(jnp.stack(group, axis=1), agent_qkv[:, model_width:]).astype(jnp.bfloat16)
        for group in (near, corners)
    ]
    column_index = lax.axis_index("gx")
    row_index = lax.axis_index("gy")
    padded_counts = jnp.pad(tile_counts, 1)
    near_counts = lax.dynamic_slice(padded_counts, (column_index, row_index), (3, 3))
    chosen = neighbours[0, 0].reshape(3, 3) == 1
    slot_ids = jnp.arange(slot_count, dtype=jnp.int32)
    key_live = (slot_ids[None, None, :] < near_counts[:, :, None]) & chosen[:, :, None]
    key_live = jnp.stack([key_live[dx + 1, dy + 1] for dx, dy in HALO_ORDER])
    key_live = key_live.reshape(1, 9 * slot_count)
    after_agents = agent_attention(
        key_live.astype(jnp.int32), queries, kv_groups, agent_out, masked_input, head_dim
    )

    after_agents = lax.all_to_all(after_agents, "ta", 1, 0, tiled=True)
    steps = after_agents.shape[0]
    group = after_agents.shape[1]
    normed = layer_norm(after_agents, norm_gains[1])
    packed = project(normed, time_qkv).astype(jnp.bfloat16)
    time_mix = time_attention(packed.reshape(steps * group, 3 * model_width), group, head_dim)
    time_mix = time_mix.reshape(steps, group, model_width)
    after_time = (after_agents.astype(jnp.float32) + project(time_mix, time_out)).astype(
        jnp.bfloat16
    )
    normed = layer_norm(after_time, norm_gains[2])
    hidden = jnp.maximum(project(normed, widen_weight), 0.0).astype(jnp.bfloat16)
    out = (after_time.astype(jnp.float32) + project(hidden, narrow_weight)).astype(jnp.bfloat16)
    out = lax.all_to_all(out, "ta", 0, 1, tiled=True)
    return out.reshape(tokens.shape)


def solution(mesh):
    in_specs = (
        P("gx", "gy", "ta", None, None),
        P("gx", "gy", "ta", None),
        P(),
        P("gx", "gy", None),
        P(),
        P(),
        P(),
        P(),
        P(),
        P(),
        P(),
        P(),
    )
    out_specs = P("gx", "gy", "ta", None, None)
    return jax.shard_map(
        per_device, mesh=mesh, in_specs=in_specs, out_specs=out_specs, check_vma=False
    )
```

```python
import functools
import math

import jax
import jax.numpy as jnp
from jax import lax
from jax.experimental import pallas as pl
from jax.sharding import PartitionSpec as P

HEADS = 8


EPSILON = 1e-05
NEGATIVE = -1e30


def shift(piece, axis, step):
    count = lax.axis_size(axis)
    if step > 0:
        pairs = [(i, i + 1) for i in range(count - 1)]
    else:
        pairs = [(i + 1, i) for i in range(count - 1)]
    return lax.ppermute(piece, axis, pairs)


def halo(piece):
    west = shift(piece, "gx", 1)
    east = shift(piece, "gx", -1)
    south = shift(piece, "gy", 1)
    north = shift(piece, "gy", -1)
    north_east = shift(north, "gx", -1)
    south_west = shift(south, "gx", 1)
    south_east = shift(east, "gy", 1)
    north_west = shift(west, "gy", -1)
    near = [west, south, piece, north, east]
    corners = [south_west, north_west, south_east, north_east]
    return near, corners


HALO_ORDER = [(-1, 0), (0, -1), (0, 0), (0, 1), (1, 0), (-1, -1), (-1, 1), (1, -1), (1, 1)]


def layer_norm(values, gain_row):
    values = values.astype(jnp.float32)
    center = values - jnp.mean(values, axis=-1, keepdims=True)
    spread = jnp.mean(center * center, axis=-1, keepdims=True)
    return (center * lax.rsqrt(spread + EPSILON) * gain_row).astype(jnp.bfloat16)


def project(values, weight):
    return jnp.dot(values, weight, preferred_element_type=jnp.float32)


def agent_kernel(live_ref, q_ref, *refs, scale, head_dim):
    o_ref = refs[-1]
    groups = (len(refs) - 1) // 2
    live = live_ref[...] != 0
    for moment in range(q_ref.shape[0]):
        queries = q_ref[moment] * jnp.asarray(scale, q_ref.dtype)
        keys = []
        values = []
        for k_ref, v_ref in zip(refs[:groups], refs[groups:-1]):
            slots = k_ref.shape[1] * k_ref.shape[2]
            keys.append(k_ref[moment].reshape(slots, k_ref.shape[3]))
            values.append(v_ref[moment].reshape(slots, v_ref.shape[3]))
        rows = queries.shape[0]
        lane = lax.broadcasted_iota(jnp.int32, (1, queries.shape[1]), 1)
        first = lane < head_dim
        zero = jnp.zeros_like(queries)
        both = jnp.concatenate(
            [jnp.where(first, queries, zero), jnp.where(first, zero, queries)], axis=0
        )
        scores = jnp.concatenate(
            [
                lax.dot_general(
                    both, key, (((1,), (1,)), ((), ())), preferred_element_type=jnp.float32
                )
                for key in keys
            ],
            axis=1,
        )
        scores = jnp.where(live, scores, NEGATIVE)
        row_max = jnp.max(scores, axis=-1, keepdims=True)
        weights = jnp.exp(scores - row_max)
        total = jnp.sum(weights, axis=-1, keepdims=True)
        weights = (weights * (1.0 / total)).astype(jnp.bfloat16)
        part = None
        start = 0
        for value in values:
            piece = jnp.dot(
                weights[:, start : start + value.shape[0]],
                value,
                preferred_element_type=jnp.float32,
            )
            part = piece if part is None else part + piece
            start += value.shape[0]
        o_ref[moment] = jnp.where(first, part[:rows], part[rows:]).astype(o_ref.dtype)


def agent_attention(live, queries, kv_groups, head_dim):
    moments, slot_count, model_width = queries.shape
    lanes = 2 * head_dim
    pairs = model_width // lanes
    body = functools.partial(agent_kernel, scale=1.0 / math.sqrt(head_dim), head_dim=head_dim)
    key_specs = [
        pl.BlockSpec((moments, kv.shape[1], slot_count, lanes), lambda p: (0, 0, 0, p))
        for kv in kv_groups
    ]
    value_specs = [
        pl.BlockSpec((moments, kv.shape[1], slot_count, lanes), lambda p: (0, 0, 0, p + pairs))
        for kv in kv_groups
    ]
    return pl.pallas_call(
        body,
        grid=(pairs,),
        in_specs=[
            pl.BlockSpec(live.shape, lambda p: (0, 0)),
            pl.BlockSpec((moments, slot_count, lanes), lambda p: (0, 0, p)),
        ]
        + key_specs
        + value_specs,
        out_specs=pl.BlockSpec((moments, slot_count, lanes), lambda p: (0, 0, p)),
        out_shape=jax.ShapeDtypeStruct(queries.shape, jnp.bfloat16),
    )(live, queries, *kv_groups, *kv_groups)

def norm_kernel(x_ref, valid_ref, token_ref, gain_ref, masked_ref, normed_ref, *, row):
    slots = x_ref.shape[1]
    token = token_ref[...].reshape(1, token_ref.shape[0])
    gain = gain_ref[row : row + 1, :]
    for moment in range(x_ref.shape[0]):
        flags = jnp.broadcast_to(valid_ref[moment : moment + 1, :], (slots, slots))
        live = jnp.transpose(flags)[:, :1] == 1
        masked = jnp.where(live, x_ref[moment], token)
        masked_ref[moment] = masked
        values = masked.astype(jnp.float32)
        center = values - jnp.mean(values, axis=-1, keepdims=True)
        spread = jnp.mean(center * center, axis=-1, keepdims=True)
        normed_ref[moment] = (center * lax.rsqrt(spread + EPSILON) * gain).astype(normed_ref.dtype)


def first_norm(rows, live_rows, mask_token, norm_gains, interpret=False):
    full = lambda shape: pl.BlockSpec(shape, lambda i: (0,) * len(shape))
    return pl.pallas_call(
        functools.partial(norm_kernel, row=0),
        grid=(1,),
        in_specs=[full(rows.shape), full(live_rows.shape), full(mask_token.shape), full(norm_gains.shape)],
        out_specs=[full(rows.shape), full(rows.shape)],
        out_shape=[jax.ShapeDtypeStruct(rows.shape, jnp.bfloat16)] * 2,
        interpret=interpret,
    )(rows, live_rows, mask_token, norm_gains)

def time_kernel(p_ref, o_ref, *, group, head_dim, scale):
    packed = p_ref[...]
    count = packed.shape[0]
    width = packed.shape[1] // 3
    lanes = 2 * head_dim
    row = lax.broadcasted_iota(jnp.int32, (count, count), 0) % group
    col = lax.broadcasted_iota(jnp.int32, (count, count), 1) % group
    same = row == col
    first = lax.broadcasted_iota(jnp.int32, (1, lanes), 1) < head_dim
    pieces = []
    for pair in range(width // lanes):
        start = pair * lanes
        queries = packed[:, start : start + lanes] * jnp.asarray(scale, packed.dtype)
        keys = packed[:, width + start : width + start + lanes]
        values = packed[:, 2 * width + start : 2 * width + start + lanes]
        zero = jnp.zeros_like(queries)
        halves = []
        for own in (jnp.where(first, queries, zero), jnp.where(first, zero, queries)):
            scores = lax.dot_general(
                own, keys, (((1,), (1,)), ((), ())), preferred_element_type=jnp.float32
            )
            scores = jnp.where(same, scores, NEGATIVE)
            row_max = jnp.max(scores, axis=-1, keepdims=True)
            weights = jnp.exp(scores - row_max)
            weights = weights / jnp.sum(weights, axis=-1, keepdims=True)
            high = weights.astype(jnp.bfloat16)
            low = (weights - high.astype(jnp.float32)).astype(jnp.bfloat16)
            halves.append(
                jnp.dot(high, values, preferred_element_type=jnp.float32)
                + jnp.dot(low, values, preferred_element_type=jnp.float32)
            )
        pieces.append(jnp.where(first, halves[0], halves[1]))
    o_ref[...] = jnp.concatenate(pieces, axis=1).astype(o_ref.dtype)


def time_attention(packed, group, head_dim, interpret=False):
    count, width3 = packed.shape
    body = functools.partial(
        time_kernel, group=group, head_dim=head_dim, scale=1.0 / math.sqrt(head_dim)
    )
    return pl.pallas_call(
        body,
        grid=(1,),
        in_specs=[pl.BlockSpec((count, width3), lambda i: (0, 0))],
        out_specs=pl.BlockSpec((count, width3 // 3), lambda i: (0, 0)),
        out_shape=jax.ShapeDtypeStruct((count, width3 // 3), packed.dtype),
        interpret=interpret,
    )(packed)


def per_device(
    tokens,
    validity,
    tile_counts,
    neighbours,
    mask_token,
    norm_gains,
    agent_qkv,
    agent_out,
    time_qkv,
    time_out,
    widen_weight,
    narrow_weight,
):
    model_width = tokens.shape[-1]
    head_count = HEADS
    head_dim = model_width // head_count
    moments = tokens.shape[2]
    slot_count = tokens.shape[3]
    score_scale = 1.0 / math.sqrt(head_dim)
    rows = tokens.reshape(moments, slot_count, model_width)
    live_rows = validity.reshape(moments, slot_count)
    masked_input, normed = first_norm(rows, live_rows, mask_token, norm_gains)

    near, corners = halo(normed)
    queries = project(normed, agent_qkv[:, :model_width]).astype(jnp.bfloat16)
    kv_groups = [
        project(jnp.stack(group, axis=1), agent_qkv[:, model_width:]).astype(jnp.bfloat16)
        for group in (near, corners)
    ]
    column_index = lax.axis_index("gx")
    row_index = lax.axis_index("gy")
    padded_counts = jnp.pad(tile_counts, 1)
    near_counts = lax.dynamic_slice(padded_counts, (column_index, row_index), (3, 3))
    chosen = neighbours[0, 0].reshape(3, 3) == 1
    slot_ids = jnp.arange(slot_count, dtype=jnp.int32)
    key_live = (slot_ids[None, None, :] < near_counts[:, :, None]) & chosen[:, :, None]
    key_live = jnp.stack([key_live[dx + 1, dy + 1] for dx, dy in HALO_ORDER])
    key_live = key_live.reshape(1, 9 * slot_count)
    mixed = agent_attention(key_live.astype(jnp.int32), queries, kv_groups, head_dim)
    agent_proj = project(mixed, agent_out)
    after_agents = (masked_input.astype(jnp.float32) + agent_proj).astype(jnp.bfloat16)

    after_agents = lax.all_to_all(after_agents, "ta", 1, 0, tiled=True)
    steps = after_agents.shape[0]
    group = after_agents.shape[1]
    normed = layer_norm(after_agents, norm_gains[1])
    packed = project(normed, time_qkv).astype(jnp.bfloat16)
    time_mix = time_attention(packed.reshape(steps * group, 3 * model_width), group, head_dim)
    time_mix = time_mix.reshape(steps, group, model_width)
    after_time = (after_agents.astype(jnp.float32) + project(time_mix, time_out)).astype(
        jnp.bfloat16
    )
    normed = layer_norm(after_time, norm_gains[2])
    hidden = jnp.maximum(project(normed, widen_weight), 0.0).astype(jnp.bfloat16)
    out = (after_time.astype(jnp.float32) + project(hidden, narrow_weight)).astype(jnp.bfloat16)
    out = lax.all_to_all(out, "ta", 0, 1, tiled=True)
    return out.reshape(tokens.shape)


def solution(mesh):
    in_specs = (
        P("gx", "gy", "ta", None, None),
        P("gx", "gy", "ta", None),
        P(),
        P("gx", "gy", None),
        P(),
        P(),
        P(),
        P(),
        P(),
        P(),
        P(),
        P(),
    )
    out_specs = P("gx", "gy", "ta", None, None)
    return jax.shard_map(
        per_device, mesh=mesh, in_specs=in_specs, out_specs=out_specs, check_vma=False
    )
```

```python
import functools
import math

import jax
import jax.numpy as jnp
from jax import lax
from jax.experimental import pallas as pl
from jax.sharding import PartitionSpec as P

HEADS = 8
PAIRS_PER_STEP = 2


EPSILON = 1e-05
NEGATIVE = -1e30


def shift(piece, axis, step):
    count = lax.axis_size(axis)
    if step > 0:
        pairs = [(i, i + 1) for i in range(count - 1)]
    else:
        pairs = [(i + 1, i) for i in range(count - 1)]
    return lax.ppermute(piece, axis, pairs)


def halo(piece):
    west = shift(piece, "gx", 1)
    east = shift(piece, "gx", -1)
    south = shift(piece, "gy", 1)
    north = shift(piece, "gy", -1)
    north_east = shift(north, "gx", -1)
    south_west = shift(south, "gx", 1)
    south_east = shift(east, "gy", 1)
    north_west = shift(west, "gy", -1)
    near = [west, south, piece, north, east]
    corners = [south_west, north_west, south_east, north_east]
    return near, corners


HALO_ORDER = [(-1, 0), (0, -1), (0, 0), (0, 1), (1, 0), (-1, -1), (-1, 1), (1, -1), (1, 1)]


def layer_norm(values, gain_row):
    values = values.astype(jnp.float32)
    center = values - jnp.mean(values, axis=-1, keepdims=True)
    spread = jnp.mean(center * center, axis=-1, keepdims=True)
    return (center * lax.rsqrt(spread + EPSILON) * gain_row).astype(jnp.bfloat16)


def project(values, weight):
    return jnp.dot(values, weight, preferred_element_type=jnp.float32)


def agent_kernel(live_ref, q_ref, *refs, scale, head_dim):
    o_ref = refs[-1]
    groups = (len(refs) - 1) // 2
    live = live_ref[...] != 0
    lanes = 2 * head_dim
    for moment in range(q_ref.shape[0]):
        for window in range(q_ref.shape[2] // lanes):
            cols = slice(window * lanes, (window + 1) * lanes)
            queries = q_ref[moment, :, cols] * jnp.asarray(scale, q_ref.dtype)
            keys = []
            values = []
            for k_ref, v_ref in zip(refs[:groups], refs[groups:-1]):
                slots = k_ref.shape[1] * k_ref.shape[2]
                keys.append(k_ref[moment, :, :, cols].reshape(slots, lanes))
                values.append(v_ref[moment, :, :, cols].reshape(slots, lanes))
            rows = queries.shape[0]
            lane = lax.broadcasted_iota(jnp.int32, (1, lanes), 1)
            first = lane < head_dim
            zero = jnp.zeros_like(queries)
            both = jnp.concatenate(
                [jnp.where(first, queries, zero), jnp.where(first, zero, queries)], axis=0
            )
            scores = jnp.concatenate(
                [
                    lax.dot_general(
                        both, key, (((1,), (1,)), ((), ())), preferred_element_type=jnp.float32
                    )
                    for key in keys
                ],
                axis=1,
            )
            scores = jnp.where(live, scores, NEGATIVE)
            row_max = jnp.max(scores, axis=-1, keepdims=True)
            weights = jnp.exp(scores - row_max)
            total = jnp.sum(weights, axis=-1, keepdims=True)
            weights = (weights * (1.0 / total)).astype(jnp.bfloat16)
            part = None
            start = 0
            for value in values:
                piece = jnp.dot(
                    weights[:, start : start + value.shape[0]],
                    value,
                    preferred_element_type=jnp.float32,
                )
                part = piece if part is None else part + piece
                start += value.shape[0]
            o_ref[moment, :, cols] = jnp.where(first, part[:rows], part[rows:]).astype(
                o_ref.dtype
            )


def agent_attention(live, queries, kv_groups, head_dim):
    moments, slot_count, model_width = queries.shape
    lanes = 2 * head_dim * PAIRS_PER_STEP
    pairs = model_width // lanes
    body = functools.partial(agent_kernel, scale=1.0 / math.sqrt(head_dim), head_dim=head_dim)
    key_specs = [
        pl.BlockSpec((moments, kv.shape[1], slot_count, lanes), lambda p: (0, 0, 0, p))
        for kv in kv_groups
    ]
    value_specs = [
        pl.BlockSpec((moments, kv.shape[1], slot_count, lanes), lambda p: (0, 0, 0, p + pairs))
        for kv in kv_groups
    ]
    return pl.pallas_call(
        body,
        grid=(pairs,),
        in_specs=[
            pl.BlockSpec(live.shape, lambda p: (0, 0)),
            pl.BlockSpec((moments, slot_count, lanes), lambda p: (0, 0, p)),
        ]
        + key_specs
        + value_specs,
        out_specs=pl.BlockSpec((moments, slot_count, lanes), lambda p: (0, 0, p)),
        out_shape=jax.ShapeDtypeStruct(queries.shape, jnp.bfloat16),
    )(live, queries, *kv_groups, *kv_groups)

def norm_kernel(x_ref, valid_ref, token_ref, gain_ref, masked_ref, normed_ref, *, row):
    slots = x_ref.shape[1]
    token = token_ref[...].reshape(1, token_ref.shape[0])
    gain = gain_ref[row : row + 1, :]
    for moment in range(x_ref.shape[0]):
        flags = jnp.broadcast_to(valid_ref[moment : moment + 1, :], (slots, slots))
        live = jnp.transpose(flags)[:, :1] == 1
        masked = jnp.where(live, x_ref[moment], token)
        masked_ref[moment] = masked
        values = masked.astype(jnp.float32)
        center = values - jnp.mean(values, axis=-1, keepdims=True)
        spread = jnp.mean(center * center, axis=-1, keepdims=True)
        normed_ref[moment] = (center * lax.rsqrt(spread + EPSILON) * gain).astype(normed_ref.dtype)


def first_norm(rows, live_rows, mask_token, norm_gains, interpret=False):
    full = lambda shape: pl.BlockSpec(shape, lambda i: (0,) * len(shape))
    return pl.pallas_call(
        functools.partial(norm_kernel, row=0),
        grid=(1,),
        in_specs=[full(rows.shape), full(live_rows.shape), full(mask_token.shape), full(norm_gains.shape)],
        out_specs=[full(rows.shape), full(rows.shape)],
        out_shape=[jax.ShapeDtypeStruct(rows.shape, jnp.bfloat16)] * 2,
        interpret=interpret,
    )(rows, live_rows, mask_token, norm_gains)

def time_kernel(p_ref, o_ref, *, group, head_dim, scale):
    packed = p_ref[...]
    count = packed.shape[0]
    width = packed.shape[1] // 3
    lanes = 2 * head_dim
    row = lax.broadcasted_iota(jnp.int32, (count, count), 0) % group
    col = lax.broadcasted_iota(jnp.int32, (count, count), 1) % group
    same = row == col
    first = lax.broadcasted_iota(jnp.int32, (1, lanes), 1) < head_dim
    pieces = []
    for pair in range(width // lanes):
        start = pair * lanes
        queries = packed[:, start : start + lanes] * jnp.asarray(scale, packed.dtype)
        keys = packed[:, width + start : width + start + lanes]
        values = packed[:, 2 * width + start : 2 * width + start + lanes]
        zero = jnp.zeros_like(queries)
        halves = []
        for own in (jnp.where(first, queries, zero), jnp.where(first, zero, queries)):
            scores = lax.dot_general(
                own, keys, (((1,), (1,)), ((), ())), preferred_element_type=jnp.float32
            )
            scores = jnp.where(same, scores, NEGATIVE)
            row_max = jnp.max(scores, axis=-1, keepdims=True)
            weights = jnp.exp(scores - row_max)
            weights = weights / jnp.sum(weights, axis=-1, keepdims=True)
            high = weights.astype(jnp.bfloat16)
            low = (weights - high.astype(jnp.float32)).astype(jnp.bfloat16)
            halves.append(
                jnp.dot(high, values, preferred_element_type=jnp.float32)
                + jnp.dot(low, values, preferred_element_type=jnp.float32)
            )
        pieces.append(jnp.where(first, halves[0], halves[1]))
    o_ref[...] = jnp.concatenate(pieces, axis=1).astype(o_ref.dtype)


def time_attention(packed, group, head_dim, interpret=False):
    count, width3 = packed.shape
    body = functools.partial(
        time_kernel, group=group, head_dim=head_dim, scale=1.0 / math.sqrt(head_dim)
    )
    return pl.pallas_call(
        body,
        grid=(1,),
        in_specs=[pl.BlockSpec((count, width3), lambda i: (0, 0))],
        out_specs=pl.BlockSpec((count, width3 // 3), lambda i: (0, 0)),
        out_shape=jax.ShapeDtypeStruct((count, width3 // 3), packed.dtype),
        interpret=interpret,
    )(packed)


def per_device(
    tokens,
    validity,
    tile_counts,
    neighbours,
    mask_token,
    norm_gains,
    agent_qkv,
    agent_out,
    time_qkv,
    time_out,
    widen_weight,
    narrow_weight,
):
    model_width = tokens.shape[-1]
    head_count = HEADS
    head_dim = model_width // head_count
    moments = tokens.shape[2]
    slot_count = tokens.shape[3]
    score_scale = 1.0 / math.sqrt(head_dim)
    rows = tokens.reshape(moments, slot_count, model_width)
    live_rows = validity.reshape(moments, slot_count)
    masked_input, normed = first_norm(rows, live_rows, mask_token, norm_gains)

    near, corners = halo(normed)
    queries = project(normed, agent_qkv[:, :model_width]).astype(jnp.bfloat16)
    kv_groups = [
        project(jnp.stack(group, axis=1), agent_qkv[:, model_width:]).astype(jnp.bfloat16)
        for group in (near, corners)
    ]
    column_index = lax.axis_index("gx")
    row_index = lax.axis_index("gy")
    padded_counts = jnp.pad(tile_counts, 1)
    near_counts = lax.dynamic_slice(padded_counts, (column_index, row_index), (3, 3))
    chosen = neighbours[0, 0].reshape(3, 3) == 1
    slot_ids = jnp.arange(slot_count, dtype=jnp.int32)
    key_live = (slot_ids[None, None, :] < near_counts[:, :, None]) & chosen[:, :, None]
    key_live = jnp.stack([key_live[dx + 1, dy + 1] for dx, dy in HALO_ORDER])
    key_live = key_live.reshape(1, 9 * slot_count)
    mixed = agent_attention(key_live.astype(jnp.int32), queries, kv_groups, head_dim)
    agent_proj = project(mixed, agent_out)
    after_agents = (masked_input.astype(jnp.float32) + agent_proj).astype(jnp.bfloat16)

    after_agents = lax.all_to_all(after_agents, "ta", 1, 0, tiled=True)
    steps = after_agents.shape[0]
    group = after_agents.shape[1]
    normed = layer_norm(after_agents, norm_gains[1])
    packed = project(normed, time_qkv).astype(jnp.bfloat16)
    time_mix = time_attention(packed.reshape(steps * group, 3 * model_width), group, head_dim)
    time_mix = time_mix.reshape(steps, group, model_width)
    after_time = (after_agents.astype(jnp.float32) + project(time_mix, time_out)).astype(
        jnp.bfloat16
    )
    normed = layer_norm(after_time, norm_gains[2])
    hidden = jnp.maximum(project(normed, widen_weight), 0.0).astype(jnp.bfloat16)
    out = (after_time.astype(jnp.float32) + project(hidden, narrow_weight)).astype(jnp.bfloat16)
    out = lax.all_to_all(out, "ta", 0, 1, tiled=True)
    return out.reshape(tokens.shape)


def solution(mesh):
    in_specs = (
        P("gx", "gy", "ta", None, None),
        P("gx", "gy", "ta", None),
        P(),
        P("gx", "gy", None),
        P(),
        P(),
        P(),
        P(),
        P(),
        P(),
        P(),
        P(),
    )
    out_specs = P("gx", "gy", "ta", None, None)
    return jax.shard_map(
        per_device, mesh=mesh, in_specs=in_specs, out_specs=out_specs, check_vma=False
    )
```

```python
import functools
import math

import jax
import jax.numpy as jnp
from jax import lax
from jax.experimental import pallas as pl
from jax.sharding import PartitionSpec as P

HEADS = 8
PAIRS_PER_STEP = 2


EPSILON = 1e-05
NEGATIVE = -1e30


def shift(piece, axis, step):
    count = lax.axis_size(axis)
    if step > 0:
        pairs = [(i, i + 1) for i in range(count - 1)]
    else:
        pairs = [(i + 1, i) for i in range(count - 1)]
    return lax.ppermute(piece, axis, pairs)


def halo(piece):
    west = shift(piece, "gx", 1)
    east = shift(piece, "gx", -1)
    south = shift(piece, "gy", 1)
    north = shift(piece, "gy", -1)
    north_east = shift(north, "gx", -1)
    south_west = shift(south, "gx", 1)
    south_east = shift(east, "gy", 1)
    north_west = shift(west, "gy", -1)
    near = [west, south, piece, north, east]
    corners = [south_west, north_west, south_east, north_east]
    return near, corners


HALO_ORDER = [(-1, 0), (0, -1), (0, 0), (0, 1), (1, 0), (-1, -1), (-1, 1), (1, -1), (1, 1)]


def layer_norm(values, gain_row):
    values = values.astype(jnp.float32)
    center = values - jnp.mean(values, axis=-1, keepdims=True)
    spread = jnp.mean(center * center, axis=-1, keepdims=True)
    return (center * lax.rsqrt(spread + EPSILON) * gain_row).astype(jnp.bfloat16)


def project(values, weight):
    return jnp.dot(values, weight, preferred_element_type=jnp.float32)


def agent_kernel(live_ref, q_ref, *refs, scale, head_dim):
    o_ref = refs[-1]
    groups = (len(refs) - 1) // 2
    live = live_ref[...] != 0
    lanes = 2 * head_dim
    for moment in range(q_ref.shape[0]):
        for window in range(q_ref.shape[2] // lanes):
            cols = slice(window * lanes, (window + 1) * lanes)
            queries = q_ref[moment, :, cols] * jnp.asarray(scale, q_ref.dtype)
            keys = []
            values = []
            for k_ref, v_ref in zip(refs[:groups], refs[groups:-1]):
                slots = k_ref.shape[1] * k_ref.shape[2]
                keys.append(k_ref[moment, :, :, cols].reshape(slots, lanes))
                values.append(v_ref[moment, :, :, cols].reshape(slots, lanes))
            rows = queries.shape[0]
            lane = lax.broadcasted_iota(jnp.int32, (1, lanes), 1)
            first = lane < head_dim
            zero = jnp.zeros_like(queries)
            both = jnp.concatenate(
                [jnp.where(first, queries, zero), jnp.where(first, zero, queries)], axis=0
            )
            scores = jnp.concatenate(
                [
                    lax.dot_general(
                        both, key, (((1,), (1,)), ((), ())), preferred_element_type=jnp.float32
                    )
                    for key in keys
                ],
                axis=1,
            )
            scores = jnp.where(live, scores, NEGATIVE)
            row_max = jnp.max(scores, axis=-1, keepdims=True)
            weights = jnp.exp(scores - row_max)
            total = jnp.sum(weights, axis=-1, keepdims=True)
            weights = (weights * (1.0 / total)).astype(jnp.bfloat16)
            part = None
            start = 0
            for value in values:
                piece = jnp.dot(
                    weights[:, start : start + value.shape[0]],
                    value,
                    preferred_element_type=jnp.float32,
                )
                part = piece if part is None else part + piece
                start += value.shape[0]
            o_ref[moment, :, cols] = jnp.where(first, part[:rows], part[rows:]).astype(
                o_ref.dtype
            )


def agent_attention(live, queries, kv_groups, head_dim):
    moments, slot_count, model_width = queries.shape
    lanes = 2 * head_dim * PAIRS_PER_STEP
    pairs = model_width // lanes
    body = functools.partial(agent_kernel, scale=1.0 / math.sqrt(head_dim), head_dim=head_dim)
    key_specs = [
        pl.BlockSpec((moments, kv.shape[1], slot_count, lanes), lambda p: (0, 0, 0, p))
        for kv in kv_groups
    ]
    value_specs = [
        pl.BlockSpec((moments, kv.shape[1], slot_count, lanes), lambda p: (0, 0, 0, p + pairs))
        for kv in kv_groups
    ]
    return pl.pallas_call(
        body,
        grid=(pairs,),
        in_specs=[
            pl.BlockSpec(live.shape, lambda p: (0, 0)),
            pl.BlockSpec((moments, slot_count, lanes), lambda p: (0, 0, p)),
        ]
        + key_specs
        + value_specs,
        out_specs=pl.BlockSpec((moments, slot_count, lanes), lambda p: (0, 0, p)),
        out_shape=jax.ShapeDtypeStruct(queries.shape, jnp.bfloat16),
    )(live, queries, *kv_groups, *kv_groups)

def norm_kernel(x_ref, valid_ref, token_ref, gain_ref, masked_ref, normed_ref, *, row):
    slots = x_ref.shape[1]
    token = token_ref[...].reshape(1, token_ref.shape[0])
    gain = gain_ref[row : row + 1, :]
    for moment in range(x_ref.shape[0]):
        flags = jnp.broadcast_to(valid_ref[moment : moment + 1, :], (slots, slots))
        live = jnp.transpose(flags)[:, :1] == 1
        masked = jnp.where(live, x_ref[moment], token)
        masked_ref[moment] = masked
        values = masked.astype(jnp.float32)
        center = values - jnp.mean(values, axis=-1, keepdims=True)
        spread = jnp.mean(center * center, axis=-1, keepdims=True)
        normed_ref[moment] = (center * lax.rsqrt(spread + EPSILON) * gain).astype(normed_ref.dtype)


def first_norm(rows, live_rows, mask_token, norm_gains, interpret=False):
    full = lambda shape: pl.BlockSpec(shape, lambda i: (0,) * len(shape))
    return pl.pallas_call(
        functools.partial(norm_kernel, row=0),
        grid=(1,),
        in_specs=[full(rows.shape), full(live_rows.shape), full(mask_token.shape), full(norm_gains.shape)],
        out_specs=[full(rows.shape), full(rows.shape)],
        out_shape=[jax.ShapeDtypeStruct(rows.shape, jnp.bfloat16)] * 2,
        interpret=interpret,
    )(rows, live_rows, mask_token, norm_gains)

def time_kernel(p_ref, o_ref, *, group, head_dim, scale):
    packed = p_ref[...]
    count = packed.shape[0]
    width = packed.shape[1] // 3
    lanes = 2 * head_dim
    row = lax.broadcasted_iota(jnp.int32, (count, count), 0)
    col = lax.broadcasted_iota(jnp.int32, (count, count), 1)
    if group & (group - 1) == 0:
        same = jnp.bitwise_and(row ^ col, group - 1) == 0
    else:
        same = row % group == col % group
    first = lax.broadcasted_iota(jnp.int32, (1, lanes), 1) < head_dim
    pieces = []
    for pair in range(width // lanes):
        start = pair * lanes
        queries = packed[:, start : start + lanes] * jnp.asarray(scale, packed.dtype)
        keys = packed[:, width + start : width + start + lanes]
        values = packed[:, 2 * width + start : 2 * width + start + lanes]
        zero = jnp.zeros_like(queries)
        halves = []
        for own in (jnp.where(first, queries, zero), jnp.where(first, zero, queries)):
            scores = lax.dot_general(
                own, keys, (((1,), (1,)), ((), ())), preferred_element_type=jnp.float32
            )
            scores = jnp.where(same, scores, NEGATIVE)
            row_max = jnp.max(scores, axis=-1, keepdims=True)
            weights = jnp.exp(scores - row_max)
            weights = weights / jnp.sum(weights, axis=-1, keepdims=True)
            high = weights.astype(jnp.bfloat16)
            low = (weights - high.astype(jnp.float32)).astype(jnp.bfloat16)
            halves.append(
                jnp.dot(high, values, preferred_element_type=jnp.float32)
                + jnp.dot(low, values, preferred_element_type=jnp.float32)
            )
        pieces.append(jnp.where(first, halves[0], halves[1]))
    o_ref[...] = jnp.concatenate(pieces, axis=1).astype(o_ref.dtype)


def time_attention(packed, group, head_dim, interpret=False):
    count, width3 = packed.shape
    body = functools.partial(
        time_kernel, group=group, head_dim=head_dim, scale=1.0 / math.sqrt(head_dim)
    )
    return pl.pallas_call(
        body,
        grid=(1,),
        in_specs=[pl.BlockSpec((count, width3), lambda i: (0, 0))],
        out_specs=pl.BlockSpec((count, width3 // 3), lambda i: (0, 0)),
        out_shape=jax.ShapeDtypeStruct((count, width3 // 3), packed.dtype),
        interpret=interpret,
    )(packed)


def per_device(
    tokens,
    validity,
    tile_counts,
    neighbours,
    mask_token,
    norm_gains,
    agent_qkv,
    agent_out,
    time_qkv,
    time_out,
    widen_weight,
    narrow_weight,
):
    model_width = tokens.shape[-1]
    head_count = HEADS
    head_dim = model_width // head_count
    moments = tokens.shape[2]
    slot_count = tokens.shape[3]
    score_scale = 1.0 / math.sqrt(head_dim)
    rows = tokens.reshape(moments, slot_count, model_width)
    live_rows = validity.reshape(moments, slot_count)
    masked_input, normed = first_norm(rows, live_rows, mask_token, norm_gains)

    near, corners = halo(normed)
    queries = project(normed, agent_qkv[:, :model_width]).astype(jnp.bfloat16)
    kv_groups = [
        project(jnp.stack(group, axis=1), agent_qkv[:, model_width:]).astype(jnp.bfloat16)
        for group in (near, corners)
    ]
    column_index = lax.axis_index("gx")
    row_index = lax.axis_index("gy")
    padded_counts = jnp.pad(tile_counts, 1)
    near_counts = lax.dynamic_slice(padded_counts, (column_index, row_index), (3, 3))
    chosen = neighbours[0, 0].reshape(3, 3) == 1
    slot_ids = jnp.arange(slot_count, dtype=jnp.int32)
    key_live = (slot_ids[None, None, :] < near_counts[:, :, None]) & chosen[:, :, None]
    key_live = jnp.stack([key_live[dx + 1, dy + 1] for dx, dy in HALO_ORDER])
    key_live = key_live.reshape(1, 9 * slot_count)
    mixed = agent_attention(key_live.astype(jnp.int32), queries, kv_groups, head_dim)
    agent_proj = project(mixed, agent_out)
    after_agents = (masked_input.astype(jnp.float32) + agent_proj).astype(jnp.bfloat16)

    after_agents = lax.all_to_all(after_agents, "ta", 1, 0, tiled=True)
    steps = after_agents.shape[0]
    group = after_agents.shape[1]
    normed = layer_norm(after_agents, norm_gains[1])
    packed = project(normed, time_qkv).astype(jnp.bfloat16)
    time_mix = time_attention(packed.reshape(steps * group, 3 * model_width), group, head_dim)
    time_mix = time_mix.reshape(steps, group, model_width)
    after_time = (after_agents.astype(jnp.float32) + project(time_mix, time_out)).astype(
        jnp.bfloat16
    )
    normed = layer_norm(after_time, norm_gains[2])
    hidden = jnp.maximum(project(normed, widen_weight), 0.0).astype(jnp.bfloat16)
    out = (after_time.astype(jnp.float32) + project(hidden, narrow_weight)).astype(jnp.bfloat16)
    out = lax.all_to_all(out, "ta", 0, 1, tiled=True)
    return out.reshape(tokens.shape)


def solution(mesh):
    in_specs = (
        P("gx", "gy", "ta", None, None),
        P("gx", "gy", "ta", None),
        P(),
        P("gx", "gy", None),
        P(),
        P(),
        P(),
        P(),
        P(),
        P(),
        P(),
        P(),
    )
    out_specs = P("gx", "gy", "ta", None, None)
    return jax.shard_map(
        per_device, mesh=mesh, in_specs=in_specs, out_specs=out_specs, check_vma=False
    )
```

```python
import functools
import math

import jax
import jax.numpy as jnp
from jax import lax
from jax.experimental import pallas as pl
from jax.sharding import PartitionSpec as P

HEADS = 8
PAIRS_PER_STEP = 2


EPSILON = 1e-05
NEGATIVE = -1e30


def shift(piece, axis, step):
    count = lax.axis_size(axis)
    if step > 0:
        pairs = [(i, i + 1) for i in range(count - 1)]
    else:
        pairs = [(i + 1, i) for i in range(count - 1)]
    return lax.ppermute(piece, axis, pairs)


def halo(piece):
    west = shift(piece, "gx", 1)
    east = shift(piece, "gx", -1)
    south = shift(piece, "gy", 1)
    north = shift(piece, "gy", -1)
    north_east = shift(north, "gx", -1)
    south_west = shift(south, "gx", 1)
    south_east = shift(east, "gy", 1)
    north_west = shift(west, "gy", -1)
    near = [west, south, piece, north, east]
    corners = [south_west, north_west, south_east, north_east]
    return near, corners


HALO_ORDER = [(-1, 0), (0, -1), (0, 0), (0, 1), (1, 0), (-1, -1), (-1, 1), (1, -1), (1, 1)]


def layer_norm(values, gain_row):
    values = values.astype(jnp.float32)
    center = values - jnp.mean(values, axis=-1, keepdims=True)
    spread = jnp.mean(center * center, axis=-1, keepdims=True)
    return (center * lax.rsqrt(spread + EPSILON) * gain_row).astype(jnp.bfloat16)


def project(values, weight):
    return jnp.dot(values, weight, preferred_element_type=jnp.float32)


def agent_kernel(live_ref, q_ref, *refs, scale, head_dim):
    o_ref = refs[-1]
    groups = (len(refs) - 1) // 2
    live = live_ref[...] != 0
    lanes = 2 * head_dim
    for moment in range(q_ref.shape[0]):
        for window in range(q_ref.shape[2] // lanes):
            cols = slice(window * lanes, (window + 1) * lanes)
            queries = q_ref[moment, :, cols] * jnp.asarray(scale, q_ref.dtype)
            keys = []
            values = []
            for k_ref, v_ref in zip(refs[:groups], refs[groups:-1]):
                slots = k_ref.shape[1] * k_ref.shape[2]
                keys.append(k_ref[moment, :, :, cols].reshape(slots, lanes))
                values.append(v_ref[moment, :, :, cols].reshape(slots, lanes))
            rows = queries.shape[0]
            lane = lax.broadcasted_iota(jnp.int32, (1, lanes), 1)
            first = lane < head_dim
            zero = jnp.zeros_like(queries)
            both = jnp.concatenate(
                [jnp.where(first, queries, zero), jnp.where(first, zero, queries)], axis=0
            )
            scores = jnp.concatenate(
                [
                    lax.dot_general(
                        both, key, (((1,), (1,)), ((), ())), preferred_element_type=jnp.float32
                    )
                    for key in keys
                ],
                axis=1,
            )
            scores = jnp.where(live, scores, NEGATIVE)
            row_max = jnp.max(scores, axis=-1, keepdims=True)
            weights = jnp.exp(scores - row_max)
            total = jnp.sum(weights, axis=-1, keepdims=True)
            weights = (weights * (1.0 / total)).astype(jnp.bfloat16)
            part = None
            start = 0
            for value in values:
                piece = jnp.dot(
                    weights[:, start : start + value.shape[0]],
                    value,
                    preferred_element_type=jnp.float32,
                )
                part = piece if part is None else part + piece
                start += value.shape[0]
            o_ref[moment, :, cols] = jnp.where(first, part[:rows], part[rows:]).astype(
                o_ref.dtype
            )


def agent_attention(live, queries, kv_groups, head_dim):
    moments, slot_count, model_width = queries.shape
    lanes = 2 * head_dim * PAIRS_PER_STEP
    pairs = model_width // lanes
    body = functools.partial(agent_kernel, scale=1.0 / math.sqrt(head_dim), head_dim=head_dim)
    key_specs = [
        pl.BlockSpec((moments, kv.shape[1], slot_count, lanes), lambda p: (0, 0, 0, p))
        for kv in kv_groups
    ]
    value_specs = [
        pl.BlockSpec((moments, kv.shape[1], slot_count, lanes), lambda p: (0, 0, 0, p + pairs))
        for kv in kv_groups
    ]
    return pl.pallas_call(
        body,
        grid=(pairs,),
        in_specs=[
            pl.BlockSpec(live.shape, lambda p: (0, 0)),
            pl.BlockSpec((moments, slot_count, lanes), lambda p: (0, 0, p)),
        ]
        + key_specs
        + value_specs,
        out_specs=pl.BlockSpec((moments, slot_count, lanes), lambda p: (0, 0, p)),
        out_shape=jax.ShapeDtypeStruct(queries.shape, jnp.bfloat16),
    )(live, queries, *kv_groups, *kv_groups)

def norm_kernel(x_ref, valid_ref, token_ref, gain_ref, masked_ref, normed_ref, *, row):
    slots = x_ref.shape[1]
    token = token_ref[...].reshape(1, token_ref.shape[0])
    gain = gain_ref[row : row + 1, :]
    for moment in range(x_ref.shape[0]):
        flags = jnp.broadcast_to(valid_ref[moment : moment + 1, :], (slots, slots))
        live = jnp.transpose(flags)[:, :1] == 1
        masked = jnp.where(live, x_ref[moment], token)
        masked_ref[moment] = masked
        values = masked.astype(jnp.float32)
        center = values - jnp.mean(values, axis=-1, keepdims=True)
        spread = jnp.mean(center * center, axis=-1, keepdims=True)
        normed_ref[moment] = (center * lax.rsqrt(spread + EPSILON) * gain).astype(normed_ref.dtype)


def first_norm(rows, live_rows, mask_token, norm_gains, interpret=False):
    full = lambda shape: pl.BlockSpec(shape, lambda i: (0,) * len(shape))
    return pl.pallas_call(
        functools.partial(norm_kernel, row=0),
        grid=(1,),
        in_specs=[full(rows.shape), full(live_rows.shape), full(mask_token.shape), full(norm_gains.shape)],
        out_specs=[full(rows.shape), full(rows.shape)],
        out_shape=[jax.ShapeDtypeStruct(rows.shape, jnp.bfloat16)] * 2,
        interpret=interpret,
    )(rows, live_rows, mask_token, norm_gains)

def time_kernel(p_ref, o_ref, *, head_dim, scale):
    slots, steps, width3 = p_ref.shape
    packed = p_ref[...].reshape(slots * steps, width3)
    count = packed.shape[0]
    width = width3 // 3
    lanes = 2 * head_dim
    row = lax.broadcasted_iota(jnp.int32, (count, count), 0) // steps
    col = lax.broadcasted_iota(jnp.int32, (count, count), 1) // steps
    same = row == col
    first = lax.broadcasted_iota(jnp.int32, (1, lanes), 1) < head_dim
    pieces = []
    for pair in range(width // lanes):
        start = pair * lanes
        queries = packed[:, start : start + lanes] * jnp.asarray(scale, packed.dtype)
        keys = packed[:, width + start : width + start + lanes]
        values = packed[:, 2 * width + start : 2 * width + start + lanes]
        zero = jnp.zeros_like(queries)
        halves = []
        for own in (jnp.where(first, queries, zero), jnp.where(first, zero, queries)):
            scores = lax.dot_general(
                own, keys, (((1,), (1,)), ((), ())), preferred_element_type=jnp.float32
            )
            scores = jnp.where(same, scores, NEGATIVE)
            row_max = jnp.max(scores, axis=-1, keepdims=True)
            weights = jnp.exp(scores - row_max)
            weights = weights / jnp.sum(weights, axis=-1, keepdims=True)
            high = weights.astype(jnp.bfloat16)
            low = (weights - high.astype(jnp.float32)).astype(jnp.bfloat16)
            halves.append(
                jnp.dot(high, values, preferred_element_type=jnp.float32)
                + jnp.dot(low, values, preferred_element_type=jnp.float32)
            )
        pieces.append(jnp.where(first, halves[0], halves[1]))
    mixed = jnp.concatenate(pieces, axis=1)
    o_ref[...] = mixed.reshape(slots, steps, width).astype(o_ref.dtype)


def time_attention(packed, head_dim, block=4, interpret=False):
    slots, steps, width3 = packed.shape
    block = math.gcd(block, slots)
    body = functools.partial(time_kernel, head_dim=head_dim, scale=1.0 / math.sqrt(head_dim))
    return pl.pallas_call(
        body,
        grid=(slots // block,),
        in_specs=[pl.BlockSpec((block, steps, width3), lambda i: (i, 0, 0))],
        out_specs=pl.BlockSpec((block, steps, width3 // 3), lambda i: (i, 0, 0)),
        out_shape=jax.ShapeDtypeStruct((slots, steps, width3 // 3), packed.dtype),
        interpret=interpret,
    )(packed)

def per_device(
    tokens,
    validity,
    tile_counts,
    neighbours,
    mask_token,
    norm_gains,
    agent_qkv,
    agent_out,
    time_qkv,
    time_out,
    widen_weight,
    narrow_weight,
):
    model_width = tokens.shape[-1]
    head_count = HEADS
    head_dim = model_width // head_count
    moments = tokens.shape[2]
    slot_count = tokens.shape[3]
    score_scale = 1.0 / math.sqrt(head_dim)
    rows = tokens.reshape(moments, slot_count, model_width)
    live_rows = validity.reshape(moments, slot_count)
    masked_input, normed = first_norm(rows, live_rows, mask_token, norm_gains)

    near, corners = halo(normed)
    queries = project(normed, agent_qkv[:, :model_width]).astype(jnp.bfloat16)
    kv_groups = [
        project(jnp.stack(group, axis=1), agent_qkv[:, model_width:]).astype(jnp.bfloat16)
        for group in (near, corners)
    ]
    column_index = lax.axis_index("gx")
    row_index = lax.axis_index("gy")
    padded_counts = jnp.pad(tile_counts, 1)
    near_counts = lax.dynamic_slice(padded_counts, (column_index, row_index), (3, 3))
    chosen = neighbours[0, 0].reshape(3, 3) == 1
    slot_ids = jnp.arange(slot_count, dtype=jnp.int32)
    key_live = (slot_ids[None, None, :] < near_counts[:, :, None]) & chosen[:, :, None]
    key_live = jnp.stack([key_live[dx + 1, dy + 1] for dx, dy in HALO_ORDER])
    key_live = key_live.reshape(1, 9 * slot_count)
    mixed = agent_attention(key_live.astype(jnp.int32), queries, kv_groups, head_dim)
    agent_proj = project(mixed, agent_out)
    after_agents = (masked_input.astype(jnp.float32) + agent_proj).astype(jnp.bfloat16)

    after_agents = lax.all_to_all(after_agents, "ta", 1, 0, tiled=True)
    steps = after_agents.shape[0]
    group = after_agents.shape[1]
    normed = layer_norm(after_agents, norm_gains[1])
    packed = project(normed.transpose(1, 0, 2), time_qkv).astype(jnp.bfloat16)
    time_mix = time_attention(packed, head_dim)
    time_proj = project(time_mix, time_out).transpose(1, 0, 2)
    after_time = (after_agents.astype(jnp.float32) + time_proj).astype(jnp.bfloat16)
    normed = layer_norm(after_time, norm_gains[2])
    hidden = jnp.maximum(project(normed, widen_weight), 0.0).astype(jnp.bfloat16)
    out = (after_time.astype(jnp.float32) + project(hidden, narrow_weight)).astype(jnp.bfloat16)
    out = lax.all_to_all(out, "ta", 0, 1, tiled=True)
    return out.reshape(tokens.shape)


def solution(mesh):
    in_specs = (
        P("gx", "gy", "ta", None, None),
        P("gx", "gy", "ta", None),
        P(),
        P("gx", "gy", None),
        P(),
        P(),
        P(),
        P(),
        P(),
        P(),
        P(),
        P(),
    )
    out_specs = P("gx", "gy", "ta", None, None)
    return jax.shard_map(
        per_device, mesh=mesh, in_specs=in_specs, out_specs=out_specs, check_vma=False
    )
```

```python
import functools
import math

import jax
import jax.numpy as jnp
from jax import lax
from jax.experimental import pallas as pl
from jax.sharding import PartitionSpec as P

HEADS = 8
PAIRS_PER_STEP = 2


EPSILON = 1e-05
NEGATIVE = -1e30


def shift(piece, axis, step):
    count = lax.axis_size(axis)
    if step > 0:
        pairs = [(i, i + 1) for i in range(count - 1)]
    else:
        pairs = [(i + 1, i) for i in range(count - 1)]
    return lax.ppermute(piece, axis, pairs)


def halo(piece):
    west = shift(piece, "gx", 1)
    east = shift(piece, "gx", -1)
    south = shift(piece, "gy", 1)
    north = shift(piece, "gy", -1)
    north_east = shift(north, "gx", -1)
    south_west = shift(south, "gx", 1)
    south_east = shift(east, "gy", 1)
    north_west = shift(west, "gy", -1)
    near = [west, south, piece, north, east]
    corners = [south_west, north_west, south_east, north_east]
    return near, corners


HALO_ORDER = [(-1, 0), (0, -1), (0, 0), (0, 1), (1, 0), (-1, -1), (-1, 1), (1, -1), (1, 1)]


def layer_norm(values, gain_row):
    values = values.astype(jnp.float32)
    center = values - jnp.mean(values, axis=-1, keepdims=True)
    spread = jnp.mean(center * center, axis=-1, keepdims=True)
    return (center * lax.rsqrt(spread + EPSILON) * gain_row).astype(jnp.bfloat16)


def project(values, weight):
    return jnp.dot(values, weight, preferred_element_type=jnp.float32)


def agent_kernel(live_ref, q_ref, *refs, scale, head_dim):
    o_ref = refs[-1]
    groups = (len(refs) - 1) // 2
    live = live_ref[...] != 0
    lanes = 2 * head_dim
    for moment in range(q_ref.shape[0]):
        for window in range(q_ref.shape[2] // lanes):
            cols = slice(window * lanes, (window + 1) * lanes)
            queries = q_ref[moment, :, cols] * jnp.asarray(scale, q_ref.dtype)
            keys = []
            values = []
            for k_ref, v_ref in zip(refs[:groups], refs[groups:-1]):
                slots = k_ref.shape[1] * k_ref.shape[2]
                keys.append(k_ref[moment, :, :, cols].reshape(slots, lanes))
                values.append(v_ref[moment, :, :, cols].reshape(slots, lanes))
            rows = queries.shape[0]
            lane = lax.broadcasted_iota(jnp.int32, (1, lanes), 1)
            first = lane < head_dim
            zero = jnp.zeros_like(queries)
            both = jnp.concatenate(
                [jnp.where(first, queries, zero), jnp.where(first, zero, queries)], axis=0
            )
            scores = jnp.concatenate(
                [
                    lax.dot_general(
                        both, key, (((1,), (1,)), ((), ())), preferred_element_type=jnp.float32
                    )
                    for key in keys
                ],
                axis=1,
            )
            scores = jnp.where(live, scores, NEGATIVE)
            row_max = jnp.max(scores, axis=-1, keepdims=True)
            weights = jnp.exp(scores - row_max)
            total = jnp.sum(weights, axis=-1, keepdims=True)
            weights = (weights * (1.0 / total)).astype(jnp.bfloat16)
            part = None
            start = 0
            for value in values:
                piece = jnp.dot(
                    weights[:, start : start + value.shape[0]],
                    value,
                    preferred_element_type=jnp.float32,
                )
                part = piece if part is None else part + piece
                start += value.shape[0]
            o_ref[moment, :, cols] = jnp.where(first, part[:rows], part[rows:]).astype(
                o_ref.dtype
            )


def agent_attention(live, queries, kv_groups, head_dim):
    moments, slot_count, model_width = queries.shape
    lanes = 2 * head_dim * PAIRS_PER_STEP
    pairs = model_width // lanes
    body = functools.partial(agent_kernel, scale=1.0 / math.sqrt(head_dim), head_dim=head_dim)
    key_specs = [
        pl.BlockSpec((moments, kv.shape[1], slot_count, lanes), lambda p: (0, 0, 0, p))
        for kv in kv_groups
    ]
    value_specs = [
        pl.BlockSpec((moments, kv.shape[1], slot_count, lanes), lambda p: (0, 0, 0, p + pairs))
        for kv in kv_groups
    ]
    return pl.pallas_call(
        body,
        grid=(pairs,),
        in_specs=[
            pl.BlockSpec(live.shape, lambda p: (0, 0)),
            pl.BlockSpec((moments, slot_count, lanes), lambda p: (0, 0, p)),
        ]
        + key_specs
        + value_specs,
        out_specs=pl.BlockSpec((moments, slot_count, lanes), lambda p: (0, 0, p)),
        out_shape=jax.ShapeDtypeStruct(queries.shape, jnp.bfloat16),
    )(live, queries, *kv_groups, *kv_groups)

def norm_kernel(x_ref, valid_ref, token_ref, gain_ref, masked_ref, normed_ref, *, row):
    slots = x_ref.shape[1]
    token = token_ref[...].reshape(1, token_ref.shape[0])
    gain = gain_ref[row : row + 1, :]
    for moment in range(x_ref.shape[0]):
        flags = jnp.broadcast_to(valid_ref[moment : moment + 1, :], (slots, slots))
        live = jnp.transpose(flags)[:, :1] == 1
        masked = jnp.where(live, x_ref[moment], token)
        masked_ref[moment] = masked
        values = masked.astype(jnp.float32)
        center = values - jnp.mean(values, axis=-1, keepdims=True)
        spread = jnp.mean(center * center, axis=-1, keepdims=True)
        normed_ref[moment] = (center * lax.rsqrt(spread + EPSILON) * gain).astype(normed_ref.dtype)


def first_norm(rows, live_rows, mask_token, norm_gains, interpret=False):
    full = lambda shape: pl.BlockSpec(shape, lambda i: (0,) * len(shape))
    return pl.pallas_call(
        functools.partial(norm_kernel, row=0),
        grid=(1,),
        in_specs=[full(rows.shape), full(live_rows.shape), full(mask_token.shape), full(norm_gains.shape)],
        out_specs=[full(rows.shape), full(rows.shape)],
        out_shape=[jax.ShapeDtypeStruct(rows.shape, jnp.bfloat16)] * 2,
        interpret=interpret,
    )(rows, live_rows, mask_token, norm_gains)

def time_kernel(p_ref, o_ref, *, group, head_dim, scale):
    packed = p_ref[...]
    count = packed.shape[0]
    width = packed.shape[1] // 3
    lanes = 2 * head_dim
    row = lax.broadcasted_iota(jnp.int32, (count, count), 0) % group
    col = lax.broadcasted_iota(jnp.int32, (count, count), 1) % group
    same = row == col
    first = lax.broadcasted_iota(jnp.int32, (1, lanes), 1) < head_dim
    pieces = []
    for pair in range(width // lanes):
        start = pair * lanes
        queries = packed[:, start : start + lanes] * jnp.asarray(scale, packed.dtype)
        keys = packed[:, width + start : width + start + lanes]
        values = packed[:, 2 * width + start : 2 * width + start + lanes]
        zero = jnp.zeros_like(queries)
        halves = []
        for own in (jnp.where(first, queries, zero), jnp.where(first, zero, queries)):
            scores = lax.dot_general(
                own, keys, (((1,), (1,)), ((), ())), preferred_element_type=jnp.float32
            )
            scores = jnp.where(same, scores, NEGATIVE)
            row_max = jnp.max(scores, axis=-1, keepdims=True)
            weights = jnp.exp(scores - row_max)
            weights = weights / jnp.sum(weights, axis=-1, keepdims=True)
            high = weights.astype(jnp.bfloat16)
            low = (weights - high.astype(jnp.float32)).astype(jnp.bfloat16)
            halves.append(
                jnp.dot(high, values, preferred_element_type=jnp.float32)
                + jnp.dot(low, values, preferred_element_type=jnp.float32)
            )
        pieces.append(jnp.where(first, halves[0], halves[1]))
    o_ref[...] = jnp.concatenate(pieces, axis=1).astype(o_ref.dtype)


def time_attention(packed, group, head_dim, interpret=False):
    count, width3 = packed.shape
    body = functools.partial(
        time_kernel, group=group, head_dim=head_dim, scale=1.0 / math.sqrt(head_dim)
    )
    return pl.pallas_call(
        body,
        grid=(1,),
        in_specs=[pl.BlockSpec((count, width3), lambda i: (0, 0))],
        out_specs=pl.BlockSpec((count, width3 // 3), lambda i: (0, 0)),
        out_shape=jax.ShapeDtypeStruct((count, width3 // 3), packed.dtype),
        interpret=interpret,
    )(packed)


def per_device(
    tokens,
    validity,
    tile_counts,
    neighbours,
    mask_token,
    norm_gains,
    agent_qkv,
    agent_out,
    time_qkv,
    time_out,
    widen_weight,
    narrow_weight,
):
    model_width = tokens.shape[-1]
    head_count = HEADS
    head_dim = model_width // head_count
    moments = tokens.shape[2]
    slot_count = tokens.shape[3]
    score_scale = 1.0 / math.sqrt(head_dim)
    rows = tokens.reshape(moments, slot_count, model_width)
    live_rows = validity.reshape(moments, slot_count)
    masked_input, normed = first_norm(rows, live_rows, mask_token, norm_gains)

    near, corners = halo(normed)
    queries = project(normed, agent_qkv[:, :model_width]).astype(jnp.bfloat16)
    kv_groups = [
        project(jnp.stack(group, axis=1), agent_qkv[:, model_width:]).astype(jnp.bfloat16)
        for group in (near, corners)
    ]
    column_index = lax.axis_index("gx")
    row_index = lax.axis_index("gy")
    padded_counts = jnp.pad(tile_counts, 1)
    near_counts = lax.dynamic_slice(padded_counts, (column_index, row_index), (3, 3))
    chosen = neighbours[0, 0].reshape(3, 3) == 1
    slot_ids = jnp.arange(slot_count, dtype=jnp.int32)
    key_live = (slot_ids[None, None, :] < near_counts[:, :, None]) & chosen[:, :, None]
    key_live = jnp.stack([key_live[dx + 1, dy + 1] for dx, dy in HALO_ORDER])
    key_live = key_live.reshape(1, 9 * slot_count)
    mixed = agent_attention(key_live.astype(jnp.int32), queries, kv_groups, head_dim)
    agent_proj = project(mixed, agent_out)
    after_agents = (masked_input.astype(jnp.float32) + agent_proj).astype(jnp.bfloat16)

    after_agents = lax.all_to_all(after_agents.transpose(1, 0, 2), "ta", 0, 1, tiled=True)
    after_agents = after_agents.transpose(1, 0, 2)
    steps = after_agents.shape[0]
    group = after_agents.shape[1]
    normed = layer_norm(after_agents, norm_gains[1])
    packed = project(normed, time_qkv).astype(jnp.bfloat16)
    time_mix = time_attention(packed.reshape(steps * group, 3 * model_width), group, head_dim)
    time_mix = time_mix.reshape(steps, group, model_width)
    after_time = (after_agents.astype(jnp.float32) + project(time_mix, time_out)).astype(
        jnp.bfloat16
    )
    normed = layer_norm(after_time, norm_gains[2])
    hidden = jnp.maximum(project(normed, widen_weight), 0.0).astype(jnp.bfloat16)
    out = (after_time.astype(jnp.float32) + project(hidden, narrow_weight)).astype(jnp.bfloat16)
    out = lax.all_to_all(out, "ta", 0, 1, tiled=True)
    return out.reshape(tokens.shape)


def solution(mesh):
    in_specs = (
        P("gx", "gy", "ta", None, None),
        P("gx", "gy", "ta", None),
        P(),
        P("gx", "gy", None),
        P(),
        P(),
        P(),
        P(),
        P(),
        P(),
        P(),
        P(),
    )
    out_specs = P("gx", "gy", "ta", None, None)
    return jax.shard_map(
        per_device, mesh=mesh, in_specs=in_specs, out_specs=out_specs, check_vma=False
    )
```

```python
import functools
import math

import jax
import jax.numpy as jnp
from jax import lax
from jax.experimental import pallas as pl
from jax.sharding import PartitionSpec as P

HEADS = 8
PAIRS_PER_STEP = 4


EPSILON = 1e-05
NEGATIVE = -1e30


def shift(piece, axis, step):
    count = lax.axis_size(axis)
    if step > 0:
        pairs = [(i, i + 1) for i in range(count - 1)]
    else:
        pairs = [(i + 1, i) for i in range(count - 1)]
    return lax.ppermute(piece, axis, pairs)


def halo(piece):
    west = shift(piece, "gx", 1)
    east = shift(piece, "gx", -1)
    south = shift(piece, "gy", 1)
    north = shift(piece, "gy", -1)
    north_east = shift(north, "gx", -1)
    south_west = shift(south, "gx", 1)
    south_east = shift(east, "gy", 1)
    north_west = shift(west, "gy", -1)
    near = [west, south, piece, north, east]
    corners = [south_west, north_west, south_east, north_east]
    return near, corners


HALO_ORDER = [(-1, 0), (0, -1), (0, 0), (0, 1), (1, 0), (-1, -1), (-1, 1), (1, -1), (1, 1)]


def layer_norm(values, gain_row):
    values = values.astype(jnp.float32)
    center = values - jnp.mean(values, axis=-1, keepdims=True)
    spread = jnp.mean(center * center, axis=-1, keepdims=True)
    return (center * lax.rsqrt(spread + EPSILON) * gain_row).astype(jnp.bfloat16)


def project(values, weight):
    return jnp.dot(values, weight, preferred_element_type=jnp.float32)


def agent_kernel(live_ref, q_ref, *refs, scale, head_dim):
    o_ref = refs[-1]
    groups = (len(refs) - 1) // 2
    live = live_ref[...] != 0
    lanes = 2 * head_dim
    for moment in range(q_ref.shape[0]):
        for window in range(q_ref.shape[2] // lanes):
            cols = slice(window * lanes, (window + 1) * lanes)
            queries = q_ref[moment, :, cols] * jnp.asarray(scale, q_ref.dtype)
            keys = []
            values = []
            for k_ref, v_ref in zip(refs[:groups], refs[groups:-1]):
                slots = k_ref.shape[1] * k_ref.shape[2]
                keys.append(k_ref[moment, :, :, cols].reshape(slots, lanes))
                values.append(v_ref[moment, :, :, cols].reshape(slots, lanes))
            rows = queries.shape[0]
            lane = lax.broadcasted_iota(jnp.int32, (1, lanes), 1)
            first = lane < head_dim
            zero = jnp.zeros_like(queries)
            both = jnp.concatenate(
                [jnp.where(first, queries, zero), jnp.where(first, zero, queries)], axis=0
            )
            scores = jnp.concatenate(
                [
                    lax.dot_general(
                        both, key, (((1,), (1,)), ((), ())), preferred_element_type=jnp.float32
                    )
                    for key in keys
                ],
                axis=1,
            )
            scores = jnp.where(live, scores, NEGATIVE)
            row_max = jnp.max(scores, axis=-1, keepdims=True)
            weights = jnp.exp(scores - row_max)
            total = jnp.sum(weights, axis=-1, keepdims=True)
            weights = (weights * (1.0 / total)).astype(jnp.bfloat16)
            part = None
            start = 0
            for value in values:
                piece = jnp.dot(
                    weights[:, start : start + value.shape[0]],
                    value,
                    preferred_element_type=jnp.float32,
                )
                part = piece if part is None else part + piece
                start += value.shape[0]
            o_ref[moment, :, cols] = jnp.where(first, part[:rows], part[rows:]).astype(
                o_ref.dtype
            )


def agent_attention(live, queries, kv_groups, head_dim):
    moments, slot_count, model_width = queries.shape
    lanes = 2 * head_dim * PAIRS_PER_STEP
    pairs = model_width // lanes
    body = functools.partial(agent_kernel, scale=1.0 / math.sqrt(head_dim), head_dim=head_dim)
    key_specs = [
        pl.BlockSpec((moments, kv.shape[1], slot_count, lanes), lambda p: (0, 0, 0, p))
        for kv in kv_groups
    ]
    value_specs = [
        pl.BlockSpec((moments, kv.shape[1], slot_count, lanes), lambda p: (0, 0, 0, p + pairs))
        for kv in kv_groups
    ]
    return pl.pallas_call(
        body,
        grid=(pairs,),
        in_specs=[
            pl.BlockSpec(live.shape, lambda p: (0, 0)),
            pl.BlockSpec((moments, slot_count, lanes), lambda p: (0, 0, p)),
        ]
        + key_specs
        + value_specs,
        out_specs=pl.BlockSpec((moments, slot_count, lanes), lambda p: (0, 0, p)),
        out_shape=jax.ShapeDtypeStruct(queries.shape, jnp.bfloat16),
    )(live, queries, *kv_groups, *kv_groups)

def norm_kernel(x_ref, valid_ref, token_ref, gain_ref, masked_ref, normed_ref, *, row):
    slots = x_ref.shape[1]
    token = token_ref[...].reshape(1, token_ref.shape[0])
    gain = gain_ref[row : row + 1, :]
    for moment in range(x_ref.shape[0]):
        flags = jnp.broadcast_to(valid_ref[moment : moment + 1, :], (slots, slots))
        live = jnp.transpose(flags)[:, :1] == 1
        masked = jnp.where(live, x_ref[moment], token)
        masked_ref[moment] = masked
        values = masked.astype(jnp.float32)
        center = values - jnp.mean(values, axis=-1, keepdims=True)
        spread = jnp.mean(center * center, axis=-1, keepdims=True)
        normed_ref[moment] = (center * lax.rsqrt(spread + EPSILON) * gain).astype(normed_ref.dtype)


def first_norm(rows, live_rows, mask_token, norm_gains, interpret=False):
    full = lambda shape: pl.BlockSpec(shape, lambda i: (0,) * len(shape))
    return pl.pallas_call(
        functools.partial(norm_kernel, row=0),
        grid=(1,),
        in_specs=[full(rows.shape), full(live_rows.shape), full(mask_token.shape), full(norm_gains.shape)],
        out_specs=[full(rows.shape), full(rows.shape)],
        out_shape=[jax.ShapeDtypeStruct(rows.shape, jnp.bfloat16)] * 2,
        interpret=interpret,
    )(rows, live_rows, mask_token, norm_gains)

def time_kernel(p_ref, o_ref, *, group, head_dim, scale):
    packed = p_ref[...]
    count = packed.shape[0]
    width = packed.shape[1] // 3
    lanes = 2 * head_dim
    row = lax.broadcasted_iota(jnp.int32, (count, count), 0) % group
    col = lax.broadcasted_iota(jnp.int32, (count, count), 1) % group
    same = row == col
    first = lax.broadcasted_iota(jnp.int32, (1, lanes), 1) < head_dim
    pieces = []
    for pair in range(width // lanes):
        start = pair * lanes
        queries = packed[:, start : start + lanes] * jnp.asarray(scale, packed.dtype)
        keys = packed[:, width + start : width + start + lanes]
        values = packed[:, 2 * width + start : 2 * width + start + lanes]
        zero = jnp.zeros_like(queries)
        halves = []
        for own in (jnp.where(first, queries, zero), jnp.where(first, zero, queries)):
            scores = lax.dot_general(
                own, keys, (((1,), (1,)), ((), ())), preferred_element_type=jnp.float32
            )
            scores = jnp.where(same, scores, NEGATIVE)
            row_max = jnp.max(scores, axis=-1, keepdims=True)
            weights = jnp.exp(scores - row_max)
            weights = weights / jnp.sum(weights, axis=-1, keepdims=True)
            high = weights.astype(jnp.bfloat16)
            low = (weights - high.astype(jnp.float32)).astype(jnp.bfloat16)
            halves.append(
                jnp.dot(high, values, preferred_element_type=jnp.float32)
                + jnp.dot(low, values, preferred_element_type=jnp.float32)
            )
        pieces.append(jnp.where(first, halves[0], halves[1]))
    o_ref[...] = jnp.concatenate(pieces, axis=1).astype(o_ref.dtype)


def time_attention(packed, group, head_dim, interpret=False):
    count, width3 = packed.shape
    body = functools.partial(
        time_kernel, group=group, head_dim=head_dim, scale=1.0 / math.sqrt(head_dim)
    )
    return pl.pallas_call(
        body,
        grid=(1,),
        in_specs=[pl.BlockSpec((count, width3), lambda i: (0, 0))],
        out_specs=pl.BlockSpec((count, width3 // 3), lambda i: (0, 0)),
        out_shape=jax.ShapeDtypeStruct((count, width3 // 3), packed.dtype),
        interpret=interpret,
    )(packed)


def per_device(
    tokens,
    validity,
    tile_counts,
    neighbours,
    mask_token,
    norm_gains,
    agent_qkv,
    agent_out,
    time_qkv,
    time_out,
    widen_weight,
    narrow_weight,
):
    model_width = tokens.shape[-1]
    head_count = HEADS
    head_dim = model_width // head_count
    moments = tokens.shape[2]
    slot_count = tokens.shape[3]
    score_scale = 1.0 / math.sqrt(head_dim)
    rows = tokens.reshape(moments, slot_count, model_width)
    live_rows = validity.reshape(moments, slot_count)
    masked_input, normed = first_norm(rows, live_rows, mask_token, norm_gains)

    near, corners = halo(normed)
    queries = project(normed, agent_qkv[:, :model_width]).astype(jnp.bfloat16)
    kv_groups = [
        project(jnp.stack(group, axis=1), agent_qkv[:, model_width:]).astype(jnp.bfloat16)
        for group in (near, corners)
    ]
    column_index = lax.axis_index("gx")
    row_index = lax.axis_index("gy")
    padded_counts = jnp.pad(tile_counts, 1)
    near_counts = lax.dynamic_slice(padded_counts, (column_index, row_index), (3, 3))
    chosen = neighbours[0, 0].reshape(3, 3) == 1
    slot_ids = jnp.arange(slot_count, dtype=jnp.int32)
    key_live = (slot_ids[None, None, :] < near_counts[:, :, None]) & chosen[:, :, None]
    key_live = jnp.stack([key_live[dx + 1, dy + 1] for dx, dy in HALO_ORDER])
    key_live = key_live.reshape(1, 9 * slot_count)
    mixed = agent_attention(key_live.astype(jnp.int32), queries, kv_groups, head_dim)
    agent_proj = project(mixed, agent_out)
    after_agents = (masked_input.astype(jnp.float32) + agent_proj).astype(jnp.bfloat16)

    after_agents = lax.all_to_all(after_agents, "ta", 1, 0, tiled=True)
    steps = after_agents.shape[0]
    group = after_agents.shape[1]
    normed = layer_norm(after_agents, norm_gains[1])
    packed = project(normed, time_qkv).astype(jnp.bfloat16)
    time_mix = time_attention(packed.reshape(steps * group, 3 * model_width), group, head_dim)
    time_mix = time_mix.reshape(steps, group, model_width)
    after_time = (after_agents.astype(jnp.float32) + project(time_mix, time_out)).astype(
        jnp.bfloat16
    )
    normed = layer_norm(after_time, norm_gains[2])
    hidden = jnp.maximum(project(normed, widen_weight), 0.0).astype(jnp.bfloat16)
    out = (after_time.astype(jnp.float32) + project(hidden, narrow_weight)).astype(jnp.bfloat16)
    out = lax.all_to_all(out, "ta", 0, 1, tiled=True)
    return out.reshape(tokens.shape)


def solution(mesh):
    in_specs = (
        P("gx", "gy", "ta", None, None),
        P("gx", "gy", "ta", None),
        P(),
        P("gx", "gy", None),
        P(),
        P(),
        P(),
        P(),
        P(),
        P(),
        P(),
        P(),
    )
    out_specs = P("gx", "gy", "ta", None, None)
    return jax.shard_map(
        per_device, mesh=mesh, in_specs=in_specs, out_specs=out_specs, check_vma=False
    )
```
